128 devices in a mesh: phase: 16 (over z_hi, y, core), axial: 2 (over z_lo), radial: 4 (over x).
Axes of the slice: x: 4, y: 4, z: 4 (z_hi: 2, z_lo: 2; z = z_hi * 2 + z_lo), core: 2. Of those that a mesh axis runs over, the one named last changes fastest.
Arguments:
- psi_start: float32 [16, 10, 8, 64, 128], P('phase', None, 'axial', 'radial'), may hold values from -6 to 6
- source: float32 [16, 10, 8, 64, 128], P('phase', None, 'axial', 'radial'), may hold values from -6 to 6
- face_coef: bfloat16 [6, 8, 64, 128], P(None, 'axial', 'radial'), may hold values from 0.099609375 to 1
- diag_coef: float32 [8, 64, 128], P('axial', 'radial'), may hold values from 6 to 10
- flux_jac: float32 [6, 2, 5, 5], replicated, may hold values from -2 to 2
- omega: float32 [1], replicated, may hold values from 0.5 to 2
- metric: float32 [3, 10], replicated, may hold values from -2 to 2
- mode_shape: bfloat16 [12, 3, 8, 64, 128], P(None, None, 'axial', 'radial'), may hold values from -6 to 6
- phase_weight: float32 [16], P('phase'), may hold values from 0.05 to 0.5
- pairing: int32 [2, 4, 64], P('axial', 'radial'), may hold values from 0 to 63, each once within a row
- owner_order: int32 [2, 4, 8192], P('axial', 'radial'), may hold values from 0 to 8191, each once within a row
Outputs:
- psi_out: float32 [16, 10, 8, 64, 128], P('phase', None, 'axial', 'radial')
- sens: float32 [12, 2, 4, 8192], P(None, 'axial', 'radial', 'phase')
The draws below stay inside these ranges and needn't reach their ends.
Inputs may be any that keep to these rules, and one draw needn't show every extreme that they name: `pairing`: each tile's row is a permutation of its pitch-end nodes. `owner_order`: each tile's row is a permutation of its cells.
All inputs are finite; a program needn't handle non-finite values.
Results may differ from the reference program's by a relative error of at most 0.0003.
Values sent between devices are 32-bit elements; how exact they have to be, the bound alone decides.
No kernel may reach another device: no remote copies, remote signals or barrier semaphores. Data moves between devices by JAX's collectives and lax.ppermute only.
A program may use at most 64 MiB of HBM per device.

```python
import math
import jax
import jax.numpy as jnp
from jax import lax

FIELDS = 5
MODES = 12
BLADES = 16
ITERS = 4
NT = 128
PHASES = 16
NA = 8
NR = 64
FACE = 64
CELLS = 8192
N_AXIAL = 2
N_RADIAL = 4


def block_scale(key, dims, cuts, least, top_value):
    gain, own = 1.0, jax.random.fold_in(key, 6)
    for axis_at, blocks in cuts:
        draws = jnp.exp(jax.random.uniform(jax.random.fold_in(own, axis_at), (blocks,), jnp.float32, least / len(cuts), top_value / len(cuts)))
        gain = gain * jnp.repeat(draws, dims[axis_at] // blocks).reshape([-1 if axis == axis_at else 1 for axis in range(len(dims))])
    return gain


def bell_draw(rng, shape, spread, bound, shards=(), held_as=jnp.bfloat16):
    gain = block_scale(rng, shape, shards, -0.22, 0.18) if shards else 1.0
    result = jax.random.normal(rng, shape, jnp.float32) * spread * gain
    return jnp.minimum(jnp.maximum(result, -bound), bound).astype(held_as)


def setup_inputs(seed: int = 0) -> dict:
    splits = jax.random.split(jax.random.key(seed), 12)
    return {
        "psi_start": bell_draw(splits[0], (PHASES, 2 * FIELDS, NA, NR, NT), 1.0, 6.0, ((0, 16), (2, 2), (3, 4)), jnp.float32),
        "source": bell_draw(splits[1], (PHASES, 2 * FIELDS, NA, NR, NT), 1.0, 6.0, ((0, 16), (2, 2), (3, 4)), jnp.float32),
        "face_coef": jnp.clip(jnp.exp(math.log(1.0) - 2.306499 * jax.random.uniform(splits[2], (6, NA, NR, NT), jnp.float32) ** block_scale(splits[2], (6, NA, NR, NT), ((1, 2), (2, 4)), -0.2, 0.2)), 0.099609375, 1.0).astype(jnp.bfloat16),
        "diag_coef": jnp.clip(6.0 + 4.0 * jax.random.uniform(splits[3], (NA, NR, NT), jnp.float32) ** block_scale(splits[3], (NA, NR, NT), ((0, 2), (1, 4)), -0.2, 0.2), 6.0, 10.0),
        "flux_jac": bell_draw(splits[4], (6, 2, FIELDS, FIELDS), (2 * FIELDS) ** -0.5, 2.0, (), jnp.float32),
        "omega": jnp.clip(jax.random.uniform(splits[5], (1,), jnp.float32, 0.5, 2.0), 0.5, 2.0),
        "metric": bell_draw(splits[6], (3, 2 * FIELDS), (2 * FIELDS) ** -0.5, 2.0, (), jnp.float32),
        "mode_shape": bell_draw(splits[7], (MODES, 3, NA, NR, NT), 1.0, 6.0, ((2, 2), (3, 4))),
        "phase_weight": jnp.clip(jnp.exp(math.log(0.5) - 2.3025851 * jax.random.uniform(splits[8], (PHASES,), jnp.float32) ** block_scale(splits[8], (PHASES,), ((0, 16),), -0.2, 0.2)), 0.05, 0.5),
        "pairing": jax.vmap(lambda own: jax.random.permutation(own, FACE))(jax.random.split(splits[9], N_AXIAL * N_RADIAL)).reshape((N_AXIAL, N_RADIAL, FACE)).astype(jnp.int32),
        "owner_order": jax.vmap(lambda own: jax.random.permutation(own, CELLS))(jax.random.split(splits[10], N_AXIAL * N_RADIAL)).reshape((N_AXIAL, N_RADIAL, CELLS)).astype(jnp.int32),
    }


RELAX = 0.8


def build_matrices(flux_jac):
    real_part = jnp.swapaxes(flux_jac[:, 0], 1, 2)
    imag_part = jnp.swapaxes(flux_jac[:, 1], 1, 2)
    top_rows = jnp.concatenate([real_part, imag_part], axis=2)
    low_rows = jnp.concatenate([-imag_part, real_part], axis=2)
    return jnp.concatenate([top_rows, low_rows], axis=1)


def rotate(values, angle):
    shape = (-1,) + (1,) * (values.ndim - 1)
    cosine = jnp.cos(angle).reshape(shape)
    sine = jnp.sin(angle).reshape(shape)
    half = values.shape[1] // 2
    real_part = values[:, :half]
    imag_part = values[:, half:]
    return jnp.concatenate([cosine * real_part - sine * imag_part, sine * real_part + cosine * imag_part], axis=1)


def pair_face(face, pairing):
    phases, comps, total_a, total_r = face.shape
    n_ax, n_ra, face_n = pairing.shape
    tile_a = total_a // n_ax
    tile_r = total_r // n_ra
    tiles = face.reshape(phases, comps, n_ax, tile_a, n_ra, tile_r).transpose(0, 1, 2, 4, 3, 5)
    tiles = tiles.reshape(phases, comps, n_ax, n_ra, tile_a * tile_r)
    index = jnp.broadcast_to(pairing.astype(jnp.int32)[None, None], tiles.shape)
    picked = jnp.take_along_axis(tiles, index, axis=4)
    picked = picked.reshape(phases, comps, n_ax, n_ra, tile_a, tile_r).transpose(0, 1, 2, 4, 3, 5)
    return picked.reshape(phases, comps, total_a, total_r)


def reference(psi_start, source, face_coef, diag_coef, flux_jac, omega, metric, mode_shape, phase_weight, pairing, owner_order):
    matrices = build_matrices(flux_jac)
    coef = face_coef.astype(jnp.float32)
    phases = psi_start.shape[0]
    angle = jnp.arange(phases).astype(jnp.float32) * (2.0 * math.pi / BLADES)
    half = psi_start.shape[1] // 2
    psi = psi_start
    for section in range(ITERS):
        parts = []
        for direction in range(6):
            applied = jnp.einsum("xc,pcart->pxart", matrices[direction], psi, precision=lax.Precision.HIGHEST)
            parts.append(applied * coef[direction][None, None])
        zero_a = jnp.zeros_like(parts[0][:, :, :1])
        zero_r = jnp.zeros_like(parts[0][:, :, :, :1])
        incoming = jnp.concatenate([zero_a, parts[0][:, :, :-1]], axis=2)
        incoming = incoming + jnp.concatenate([parts[1][:, :, 1:], zero_a], axis=2)
        incoming = incoming + jnp.concatenate([zero_r, parts[2][:, :, :, :-1]], axis=3)
        incoming = incoming + jnp.concatenate([parts[3][:, :, :, 1:], zero_r], axis=3)
        plus_wrap = rotate(pair_face(parts[4][..., -1], pairing), angle)
        minus_wrap = rotate(pair_face(parts[5][..., 0], pairing), -angle)
        incoming = incoming + jnp.concatenate([plus_wrap[..., None], parts[4][..., :-1]], axis=4)
        incoming = incoming + jnp.concatenate([parts[5][..., 1:], minus_wrap[..., None]], axis=4)
        swapped = jnp.concatenate([psi[:, half:], -psi[:, :half]], axis=1)
        residual = source - (diag_coef * psi + omega[0] * swapped) + incoming
        psi = psi + RELAX * residual / diag_coef
    heights = jnp.einsum("dc,pcart->pdart", metric, psi, precision=lax.Precision.HIGHEST)
    weighted = jnp.sum(phase_weight[:, None, None, None, None] * heights, axis=0)
    modes = mode_shape.astype(jnp.float32)
    total = modes[:, 0] * weighted[0] + modes[:, 1] * weighted[1] + modes[:, 2] * weighted[2]
    n_ax, n_ra, cells = owner_order.shape
    count_k, total_a, total_r, pitch = total.shape
    tile_a = total_a // n_ax
    tile_r = total_r // n_ra
    tiles = total.reshape(count_k, n_ax, tile_a, n_ra, tile_r, pitch).transpose(0, 1, 3, 2, 4, 5)
    tiles = tiles.reshape(count_k, n_ax, n_ra, cells)
    index = jnp.broadcast_to(owner_order.astype(jnp.int32)[None], tiles.shape)
    sens = jnp.take_along_axis(tiles, index, axis=3)
    return psi, sens
```

```python
import math

import jax
import jax.numpy as jnp
from jax import lax
from jax.sharding import PartitionSpec as P

BLADES = 16
ITERS = 4


RELAX = 0.8


def padded(value, sides, width):
    for axis, dim in sides:
        count, length = (lax.axis_size(axis), value.shape[dim])
        up = [(i, (i + 1) % count) for i in range(count - 1)]
        down = [(j, i) for i, j in up]
        last = lax.slice_in_dim(value, length - width, length, axis=dim)
        leading = lax.slice_in_dim(value, 0, width, axis=dim)
        before = lax.ppermute(last, axis, up)
        after = lax.ppermute(leading, axis, down)
        value = jnp.concatenate([before, value, after], axis=dim)
    return value


def exchange_pair(value, axis, dim):
    me = lax.axis_index(axis)
    leading = lax.slice_in_dim(value, 0, 1, axis=dim)
    last = lax.slice_in_dim(value, value.shape[dim] - 1, value.shape[dim], axis=dim)
    got = lax.ppermute(jnp.where(me == 0, last, leading), axis, [(0, 1), (1, 0)])
    zero = jnp.zeros_like(got)
    before = jnp.where(me == 1, got, zero)
    after = jnp.where(me == 0, got, zero)
    return jnp.concatenate([before, value, after], axis=dim)


def split_up(value, dim, count):
    dims = value.shape
    blocks = value.reshape(*dims[:dim], count, dims[dim] // count, *dims[dim + 1 :])
    return jnp.moveaxis(blocks, dim, 0)


def sum_at_owner(value, axis, dim):
    count = lax.axis_size(axis)
    blocks = lax.all_to_all(split_up(value, dim, count), axis, 0, 0, tiled=True)
    return jnp.sum(blocks, axis=0)


def build_matrices(flux_jac):
    real_part = jnp.swapaxes(flux_jac[:, 0], 1, 2)
    imag_part = jnp.swapaxes(flux_jac[:, 1], 1, 2)
    top_rows = jnp.concatenate([real_part, imag_part], axis=2)
    low_rows = jnp.concatenate([-imag_part, real_part], axis=2)
    return jnp.concatenate([top_rows, low_rows], axis=1)


def rotate(values, angle):
    shape = (-1,) + (1,) * (values.ndim - 1)
    cosine = jnp.cos(angle).reshape(shape)
    sine = jnp.sin(angle).reshape(shape)
    half = values.shape[1] // 2
    real_part = values[:, :half]
    imag_part = values[:, half:]
    return jnp.concatenate(
        [cosine * real_part - sine * imag_part, sine * real_part + cosine * imag_part], axis=1
    )


def pair_face(face, partner):
    phases, comps, tile_a, tile_r = face.shape
    flat = face.reshape(phases, comps, tile_a * tile_r)
    return jnp.take(flat, partner, axis=2).reshape(phases, comps, tile_a, tile_r)


def body(
    psi_start,
    source,
    face_coef,
    diag_coef,
    flux_jac,
    omega,
    metric,
    mode_shape,
    phase_weight,
    pairing,
    owner_order,
):
    matrices = build_matrices(flux_jac)
    comps = matrices.shape[1]
    stacked = matrices.reshape(6 * comps, comps)
    coef = face_coef.astype(jnp.float32)
    local_phases, _, tile_a, tile_r, pitch = psi_start.shape
    first = lax.axis_index("phase") * local_phases
    angle = (first + jnp.arange(local_phases, dtype=jnp.int32)).astype(jnp.float32) * (
        2.0 * math.pi / BLADES
    )
    half = comps // 2
    partner = pairing[0, 0]
    psi = psi_start
    for section in range(ITERS):
        flat = psi.reshape(local_phases, comps, tile_a * tile_r * pitch)
        applied = jnp.einsum("yc,pcn->pyn", stacked, flat, precision=lax.Precision.HIGHEST)
        applied = applied.reshape(local_phases, 6, comps, tile_a, tile_r, pitch)
        parts = [applied[:, d] * coef[d][None, None] for d in range(6)]
        axial_edge = jnp.concatenate([parts[1][:, :, :1], parts[0][:, :, -1:]], axis=2)
        radial_edge = jnp.concatenate([parts[3][:, :, :, :1], parts[2][:, :, :, -1:]], axis=3)
        axial_got = exchange_pair(axial_edge, "axial", 2) if lax.axis_size("axial") == 2 else padded(axial_edge, (("axial", 2),), 1)
        radial_got = padded(radial_edge, (("radial", 3),), 1)
        plus_wrap = rotate(pair_face(parts[4][..., -1], partner), angle)
        minus_wrap = rotate(pair_face(parts[5][..., 0], partner), -angle)
        from_lower_a = jnp.concatenate([axial_got[:, :, 0:1], parts[0][:, :, :-1]], axis=2)
        from_upper_a = jnp.concatenate([parts[1][:, :, 1:], axial_got[:, :, 3:4]], axis=2)
        from_lower_r = jnp.concatenate([radial_got[:, :, :, 0:1], parts[2][:, :, :, :-1]], axis=3)
        from_upper_r = jnp.concatenate([parts[3][:, :, :, 1:], radial_got[:, :, :, 3:4]], axis=3)
        from_lower_t = jnp.concatenate([plus_wrap[..., None], parts[4][..., :-1]], axis=4)
        from_upper_t = jnp.concatenate([parts[5][..., 1:], minus_wrap[..., None]], axis=4)
        swapped = jnp.concatenate([psi[:, half:], -psi[:, :half]], axis=1)
        residual = (
            source
            - (diag_coef * psi + omega[0] * swapped)
            + (
                from_lower_a
                + from_upper_a
                + from_lower_r
                + from_upper_r
                + from_lower_t
                + from_upper_t
            )
        )
        psi = psi + RELAX * residual / diag_coef
    cells = tile_a * tile_r * pitch
    heights = jnp.einsum(
        "dc,pcn->pdn",
        metric,
        psi.reshape(local_phases, comps, cells),
        precision=lax.Precision.HIGHEST,
    )
    weighted = jnp.sum(phase_weight[:, None, None] * heights, axis=0)
    order = owner_order[0, 0]
    owners = lax.axis_size("phase")
    owned = cells // owners
    dims = weighted.shape[0]
    lanes = 128
    rows = cells // lanes
    lane_of = order % lanes
    row_of = order // lanes
    pick_lane = (lane_of[None, :] == jnp.arange(lanes, dtype=order.dtype)[:, None]).astype(jnp.float32)
    by_lane = jnp.einsum(
        "xl,lj->xj",
        weighted.reshape(dims * rows, lanes),
        pick_lane,
        precision=lax.Precision.HIGHEST,
    ).reshape(dims, rows, cells)
    pick_row = row_of[None, None, :] == jnp.arange(rows, dtype=order.dtype)[None, :, None]
    in_order = jnp.sum(jnp.where(pick_row, by_lane, 0.0), axis=1)
    gathered = sum_at_owner(in_order, "phase", 1)
    mine = lax.dynamic_slice_in_dim(order, lax.axis_index("phase") * owned, owned)
    count_k = mode_shape.shape[0]
    modes = jnp.take(mode_shape.reshape(count_k, 3, cells), mine, axis=2).astype(jnp.float32)
    sens = modes[:, 0] * gathered[0] + modes[:, 1] * gathered[1] + modes[:, 2] * gathered[2]
    return (psi, sens.reshape(count_k, 1, 1, owned))


def solution(mesh):
    return jax.shard_map(
        body,
        mesh=mesh,
        in_specs=(
            P("phase", None, "axial", "radial", None),
            P("phase", None, "axial", "radial", None),
            P(None, "axial", "radial", None),
            P("axial", "radial", None),
            P(),
            P(),
            P(),
            P(None, None, "axial", "radial", None),
            P("phase"),
            P("axial", "radial", None),
            P("axial", "radial", None),
        ),
        out_specs=(P("phase", None, "axial", "radial", None), P(None, "axial", "radial", "phase")),
        check_vma=False,
    )
```

```python
import functools
import math

import jax
import jax.numpy as jnp
from jax import lax
from jax.experimental import pallas as pl
from jax.experimental.pallas import tpu as pltpu
from jax.sharding import PartitionSpec as P

BLADES = 16
ITERS = 4


RELAX = 0.8
LANES = 128
SMEM = pltpu.MemorySpace.SMEM


def split_up(value, dim, count):
    dims = value.shape
    blocks = value.reshape(*dims[:dim], count, dims[dim] // count, *dims[dim + 1 :])
    return jnp.moveaxis(blocks, dim, 0)


def sum_at_owner(value, axis, dim):
    count = lax.axis_size(axis)
    blocks = lax.all_to_all(split_up(value, dim, count), axis, 0, 0, tiled=True)
    return jnp.sum(blocks, axis=0)


def build_matrices(flux_jac):
    real_part = jnp.swapaxes(flux_jac[:, 0], 1, 2)
    imag_part = jnp.swapaxes(flux_jac[:, 1], 1, 2)
    top_rows = jnp.concatenate([real_part, imag_part], axis=2)
    low_rows = jnp.concatenate([-imag_part, real_part], axis=2)
    return jnp.concatenate([top_rows, low_rows], axis=1)


def exact_pick(pick, values):
    first = values.astype(jnp.bfloat16)
    rest = values - first.astype(jnp.float32)
    second = rest.astype(jnp.bfloat16)
    third = (rest - second.astype(jnp.float32)).astype(jnp.bfloat16)
    out = jnp.dot(pick, first, preferred_element_type=jnp.float32)
    out = out + jnp.dot(pick, second, preferred_element_type=jnp.float32)
    return out + jnp.dot(pick, third, preferred_element_type=jnp.float32)


def applied(mat_ref, d, x, comps, load):
    total = mat_ref[(d * comps + x) * comps] * load(0)
    for c in range(1, comps):
        total = total + mat_ref[(d * comps + x) * comps + c] * load(c)
    return total


def write_edges(mat_ref, wt_ref, psi_ref, face_ref, axs_ref, q2_ref, q3_ref, comps, tile_r):
    rows = psi_ref.shape[1]
    layers = rows // tile_r
    top = pl.ds(rows - tile_r, tile_r)
    bottom = pl.ds(0, tile_r)
    r_top = pl.ds(tile_r - 1, layers, stride=tile_r)
    r_bottom = pl.ds(0, layers, stride=tile_r)
    keep_top = wt_ref[1]
    keep_bottom = wt_ref[0]
    for x in range(comps):
        up = face_ref[0, top, :] * applied(mat_ref, 0, x, comps, lambda c: psi_ref[c, top, :])
        down = face_ref[1, bottom, :] * applied(mat_ref, 1, x, comps, lambda c: psi_ref[c, bottom, :])
        axs_ref[x] = up * keep_top + down * keep_bottom
        q2_ref[x] = face_ref[2, r_top, :] * applied(mat_ref, 2, x, comps, lambda c: psi_ref[c, r_top, :])
        q3_ref[x] = face_ref[3, r_bottom, :] * applied(mat_ref, 3, x, comps, lambda c: psi_ref[c, r_bottom, :])


def edges_kernel(mat_ref, wt_ref, psi_ref, face_ref, axs_ref, q2_ref, q3_ref, *, tile_r):
    write_edges(mat_ref, wt_ref, psi_ref, face_ref, axs_ref, q2_ref, q3_ref, psi_ref.shape[0], tile_r)


def section_kernel(
    mat_ref, wt_ref, psi_ref, src_ref, face_ref, diag_ref, pick_ref, axr_ref, ralo_ref, rahi_ref,
    out_ref, axs_ref, q2_ref, q3_ref, inc_ref, *, tile_r, edges,
):
    comps, rows, lanes = psi_ref.shape
    half = comps // 2
    layers = rows // tile_r
    lane = lax.broadcasted_iota(jnp.int32, (rows, lanes), 1)
    row = lax.broadcasted_iota(jnp.int32, (rows, lanes), 0) % tile_r
    omega = wt_ref[2]
    cosine = wt_ref[3]
    sine = wt_ref[4]
    from_below = wt_ref[5]
    from_above = wt_ref[6]
    pack4 = jnp.zeros((rows, lanes), jnp.float32)
    pack5 = jnp.zeros((rows, lanes), jnp.float32)
    load = lambda c: psi_ref[c]
    for x in range(comps):
        q0 = face_ref[0] * applied(mat_ref, 0, x, comps, load)
        q1 = face_ref[1] * applied(mat_ref, 1, x, comps, load)
        q2 = face_ref[2] * applied(mat_ref, 2, x, comps, load)
        q3 = face_ref[3] * applied(mat_ref, 3, x, comps, load)
        q4 = face_ref[4] * applied(mat_ref, 4, x, comps, load)
        q5 = face_ref[5] * applied(mat_ref, 5, x, comps, load)
        got = axr_ref[x]
        lower_a = jnp.concatenate([got * from_below, q0[: rows - tile_r]], axis=0)
        upper_a = jnp.concatenate([q1[tile_r:], got * from_above], axis=0)
        low_r = ralo_ref[x]
        high_r = rahi_ref[x]
        low_rows = jnp.concatenate(
            [jnp.broadcast_to(low_r[j : j + 1, :], (tile_r, lanes)) for j in range(layers)], axis=0
        )
        high_rows = jnp.concatenate(
            [jnp.broadcast_to(high_r[j : j + 1, :], (tile_r, lanes)) for j in range(layers)], axis=0
        )
        lower_r = jnp.where(row == 0, low_rows, pltpu.roll(q2, 1, 0))
        upper_r = jnp.where(row == tile_r - 1, high_rows, pltpu.roll(q3, rows - 1, 0))
        lower_t = jnp.where(lane == 0, 0.0, pltpu.roll(q4, 1, 1))
        upper_t = jnp.where(lane == lanes - 1, 0.0, pltpu.roll(q5, lanes - 1, 1))
        inc_ref[x] = lower_a + upper_a + lower_r + upper_r + lower_t + upper_t
        pack4 = pack4 + jnp.where(lane == x, pltpu.roll(q4, (x + 1) % lanes, 1), 0.0)
        pack5 = pack5 + jnp.where(lane == x, pltpu.roll(q5, x, 1), 0.0) if x else jnp.where(lane == 0, q5, 0.0)
    pick = pick_ref[...]
    got4 = exact_pick(pick, pack4)
    got5 = exact_pick(pick, pack5)
    up4 = pltpu.roll(got4, lanes - half, 1)
    down4 = pltpu.roll(got4, half, 1)
    up5 = pltpu.roll(got5, lanes - half, 1)
    down5 = pltpu.roll(got5, half, 1)
    real_half = lane < half
    wrap4 = jnp.where(real_half, cosine * got4 - sine * up4, sine * down4 + cosine * got4)
    wrap5 = jnp.where(real_half, cosine * got5 - (-sine) * up5, (-sine) * down5 + cosine * got5)
    diag = diag_ref[...]
    for x in range(comps):
        at_start = pltpu.roll(wrap4, (lanes - x) % lanes, 1)
        at_end = pltpu.roll(wrap5, lanes - 1 - x, 1)
        incoming = inc_ref[x] + jnp.where(lane == 0, at_start, 0.0) + jnp.where(lane == lanes - 1, at_end, 0.0)
        psi = psi_ref[x]
        swapped = psi_ref[x + half] if x < half else -psi_ref[x - half]
        residual = src_ref[x] - (diag * psi + omega * swapped) + incoming
        out_ref[x] = psi + RELAX * residual / diag
    if edges:
        write_edges(mat_ref, wt_ref, out_ref, face_ref, axs_ref, q2_ref, q3_ref, comps, tile_r)


def vmem_spec():
    return pl.BlockSpec(memory_space=pltpu.MemorySpace.VMEM)


def smem_spec():
    return pl.BlockSpec(memory_space=SMEM)


def edge_shapes(comps, rows, tile_r):
    layers = rows // tile_r
    return (
        jax.ShapeDtypeStruct((comps, tile_r, LANES), jnp.float32),
        jax.ShapeDtypeStruct((comps, layers, LANES), jnp.float32),
        jax.ShapeDtypeStruct((comps, layers, LANES), jnp.float32),
    )


def run_edges(mat, weights, psi, face, tile_r):
    comps, rows, _ = psi.shape
    return pl.pallas_call(
        functools.partial(edges_kernel, tile_r=tile_r),
        out_shape=edge_shapes(comps, rows, tile_r),
        in_specs=[smem_spec(), smem_spec(), vmem_spec(), vmem_spec()],
        out_specs=tuple(vmem_spec() for _ in range(3)),
    )(mat, weights, psi, face)


def run_section(mat, weights, psi, src, face, diag, pick, axr, ralo, rahi, tile_r, edges):
    comps, rows, lanes = psi.shape
    return pl.pallas_call(
        functools.partial(section_kernel, tile_r=tile_r, edges=edges),
        out_shape=(jax.ShapeDtypeStruct(psi.shape, jnp.float32),) + edge_shapes(comps, rows, tile_r),
        in_specs=[smem_spec(), smem_spec()] + [vmem_spec() for _ in range(8)],
        out_specs=tuple(vmem_spec() for _ in range(4)),
        scratch_shapes=[pltpu.VMEM((comps, rows, lanes), jnp.float32)],
    )(mat, weights, psi, src, face, diag, pick, axr, ralo, rahi)


def neighbours(axis):
    count = lax.axis_size(axis)
    up = [(i, (i + 1) % count) for i in range(count - 1)]
    return up, [(j, i) for i, j in up]


def body(
    psi_start,
    source,
    face_coef,
    diag_coef,
    flux_jac,
    omega,
    metric,
    mode_shape,
    phase_weight,
    pairing,
    owner_order,
):
    matrices = build_matrices(flux_jac)
    comps = matrices.shape[1]
    mat = matrices.reshape(-1)
    local_phases, _, tile_a, tile_r, pitch = psi_start.shape
    rows = tile_a * tile_r
    cells = rows * pitch
    angle = lax.axis_index("phase").astype(jnp.float32) * (2.0 * math.pi / BLADES)
    me_axial = lax.axis_index("axial")
    lower_side = (me_axial == 0).astype(jnp.float32)
    upper_side = 1.0 - lower_side
    weights = jnp.stack(
        [
            upper_side,
            lower_side,
            omega[0],
            jnp.cos(angle),
            jnp.sin(angle),
            upper_side,
            lower_side,
        ]
    ).astype(jnp.float32)
    partner = pairing[0, 0]
    faces = face_coef.astype(jnp.float32).reshape(6, rows, pitch)
    diag = diag_coef.reshape(rows, pitch)
    pick = (partner[:, None] == jnp.arange(rows, dtype=partner.dtype)[None, :]).astype(jnp.bfloat16)
    up_r, down_r = neighbours("radial")
    psi = psi_start.reshape(comps, rows, pitch)
    src = source.reshape(comps, rows, pitch)
    axs, q2, q3 = run_edges(mat, weights, psi, faces, tile_r)
    for section in range(ITERS):
        axr = lax.ppermute(axs, "axial", [(0, 1), (1, 0)])
        ralo = lax.ppermute(q2, "radial", up_r)
        rahi = lax.ppermute(q3, "radial", down_r)
        psi, axs, q2, q3 = run_section(
            mat, weights, psi, src, faces, diag, pick, axr, ralo, rahi, tile_r, section < ITERS - 1
        )
    psi_out = psi.reshape(psi_start.shape)
    heights = jnp.einsum(
        "dc,cn->dn",
        metric,
        psi.reshape(comps, cells),
        precision=lax.Precision.HIGHEST,
    )
    weighted = phase_weight[0] * heights
    order = owner_order[0, 0]
    owners = lax.axis_size("phase")
    owned = cells // owners
    dims = weighted.shape[0]
    lanes = LANES
    blocks = cells // lanes
    lane_of = order % lanes
    row_of = order // lanes
    pick_lane = (lane_of[None, :] == jnp.arange(lanes, dtype=order.dtype)[:, None]).astype(jnp.float32)
    by_lane = jnp.einsum(
        "xl,lj->xj",
        weighted.reshape(dims * blocks, lanes),
        pick_lane,
        precision=lax.Precision.HIGHEST,
    ).reshape(dims, blocks, cells)
    pick_row = row_of[None, None, :] == jnp.arange(blocks, dtype=order.dtype)[None, :, None]
    in_order = jnp.sum(jnp.where(pick_row, by_lane, 0.0), axis=1)
    gathered = sum_at_owner(in_order, "phase", 1)
    mine = lax.dynamic_slice_in_dim(order, lax.axis_index("phase") * owned, owned)
    count_k = mode_shape.shape[0]
    mine_lane = (mine[None, :] % lanes == jnp.arange(lanes, dtype=mine.dtype)[:, None]).astype(jnp.bfloat16)
    mode_lane = jnp.einsum(
        "xl,lj->xj",
        mode_shape.reshape(count_k * 3 * blocks, lanes),
        mine_lane,
        preferred_element_type=jnp.float32,
    ).reshape(count_k, 3, blocks, owned)
    mine_row = (mine // lanes)[None, None, None, :] == jnp.arange(blocks, dtype=mine.dtype)[None, None, :, None]
    modes = jnp.sum(jnp.where(mine_row, mode_lane, 0.0), axis=2)
    sens = modes[:, 0] * gathered[0] + modes[:, 1] * gathered[1] + modes[:, 2] * gathered[2]
    return (psi_out, sens.reshape(count_k, 1, 1, owned))


def solution(mesh):
    return jax.shard_map(
        body,
        mesh=mesh,
        in_specs=(
            P("phase", None, "axial", "radial", None),
            P("phase", None, "axial", "radial", None),
            P(None, "axial", "radial", None),
            P("axial", "radial", None),
            P(),
            P(),
            P(),
            P(None, None, "axial", "radial", None),
            P("phase"),
            P("axial", "radial", None),
            P("axial", "radial", None),
        ),
        out_specs=(P("phase", None, "axial", "radial", None), P(None, "axial", "radial", "phase")),
        check_vma=False,
    )
```

```python
import functools
import math

import jax
import jax.numpy as jnp
from jax import lax
from jax.experimental import pallas as pl
from jax.experimental.pallas import tpu as pltpu
from jax.sharding import PartitionSpec as P

BLADES = 16
ITERS = 4


RELAX = 0.8
LANES = 128
SMEM = pltpu.MemorySpace.SMEM


def split_up(value, dim, count):
    dims = value.shape
    blocks = value.reshape(*dims[:dim], count, dims[dim] // count, *dims[dim + 1 :])
    return jnp.moveaxis(blocks, dim, 0)


def sum_at_owner(value, axis, dim):
    count = lax.axis_size(axis)
    blocks = lax.all_to_all(split_up(value, dim, count), axis, 0, 0, tiled=True)
    return jnp.sum(blocks, axis=0)


def build_matrices(flux_jac):
    real_part = jnp.swapaxes(flux_jac[:, 0], 1, 2)
    imag_part = jnp.swapaxes(flux_jac[:, 1], 1, 2)
    top_rows = jnp.concatenate([real_part, imag_part], axis=2)
    low_rows = jnp.concatenate([-imag_part, real_part], axis=2)
    return jnp.concatenate([top_rows, low_rows], axis=1)


def exact_pick(pick, values):
    first = values.astype(jnp.bfloat16)
    rest = values - first.astype(jnp.float32)
    second = rest.astype(jnp.bfloat16)
    third = (rest - second.astype(jnp.float32)).astype(jnp.bfloat16)
    out = jnp.dot(pick, first, preferred_element_type=jnp.float32)
    out = out + jnp.dot(pick, second, preferred_element_type=jnp.float32)
    return out + jnp.dot(pick, third, preferred_element_type=jnp.float32)


def applied(mat_ref, d, x, comps, load):
    total = mat_ref[(d * comps + x) * comps] * load(0)
    for c in range(1, comps):
        total = total + mat_ref[(d * comps + x) * comps + c] * load(c)
    return total


def write_edges(mat_ref, wt_ref, psi_ref, face_ref, axs_ref, q2_ref, q3_ref, comps, tile_r):
    rows = psi_ref.shape[1]
    layers = rows // tile_r
    top = pl.ds(rows - tile_r, tile_r)
    bottom = pl.ds(0, tile_r)
    r_top = pl.ds(tile_r - 1, layers, stride=tile_r)
    r_bottom = pl.ds(0, layers, stride=tile_r)
    keep_top = wt_ref[1]
    keep_bottom = wt_ref[0]
    for x in range(comps):
        up = face_ref[0, top, :] * applied(mat_ref, 0, x, comps, lambda c: psi_ref[c, top, :])
        down = face_ref[1, bottom, :] * applied(mat_ref, 1, x, comps, lambda c: psi_ref[c, bottom, :])
        axs_ref[x] = up * keep_top + down * keep_bottom
        q2_ref[x] = face_ref[2, r_top, :] * applied(mat_ref, 2, x, comps, lambda c: psi_ref[c, r_top, :])
        q3_ref[x] = face_ref[3, r_bottom, :] * applied(mat_ref, 3, x, comps, lambda c: psi_ref[c, r_bottom, :])


def edges_kernel(mat_ref, wt_ref, psi_ref, face_ref, axs_ref, q2_ref, q3_ref, *, tile_r):
    write_edges(mat_ref, wt_ref, psi_ref, face_ref, axs_ref, q2_ref, q3_ref, psi_ref.shape[0], tile_r)


def section_kernel(
    mat_ref, wt_ref, psi_ref, src_ref, face_ref, diag_ref, pick_ref, axr_ref, ralo_ref, rahi_ref,
    out_ref, axs_ref, q2_ref, q3_ref, inc_ref, *, tile_r, edges,
):
    comps, rows, lanes = psi_ref.shape
    half = comps // 2
    layers = rows // tile_r
    lane = lax.broadcasted_iota(jnp.int32, (rows, lanes), 1)
    row = lax.broadcasted_iota(jnp.int32, (rows, lanes), 0) % tile_r
    omega = wt_ref[2]
    cosine = wt_ref[3]
    sine = wt_ref[4]
    from_below = wt_ref[5]
    from_above = wt_ref[6]
    pack4 = jnp.zeros((rows, lanes), jnp.float32)
    pack5 = jnp.zeros((rows, lanes), jnp.float32)
    load = lambda c: psi_ref[c]
    for x in range(comps):
        q0 = face_ref[0] * applied(mat_ref, 0, x, comps, load)
        q1 = face_ref[1] * applied(mat_ref, 1, x, comps, load)
        q2 = face_ref[2] * applied(mat_ref, 2, x, comps, load)
        q3 = face_ref[3] * applied(mat_ref, 3, x, comps, load)
        q4 = face_ref[4] * applied(mat_ref, 4, x, comps, load)
        q5 = face_ref[5] * applied(mat_ref, 5, x, comps, load)
        got = axr_ref[x]
        lower_a = jnp.concatenate([got * from_below, q0[: rows - tile_r]], axis=0)
        upper_a = jnp.concatenate([q1[tile_r:], got * from_above], axis=0)
        low_r = ralo_ref[x]
        high_r = rahi_ref[x]
        low_rows = jnp.concatenate(
            [jnp.broadcast_to(low_r[j : j + 1, :], (tile_r, lanes)) for j in range(layers)], axis=0
        )
        high_rows = jnp.concatenate(
            [jnp.broadcast_to(high_r[j : j + 1, :], (tile_r, lanes)) for j in range(layers)], axis=0
        )
        lower_r = jnp.where(row == 0, low_rows, pltpu.roll(q2, 1, 0))
        upper_r = jnp.where(row == tile_r - 1, high_rows, pltpu.roll(q3, rows - 1, 0))
        lower_t = jnp.where(lane == 0, 0.0, pltpu.roll(q4, 1, 1))
        upper_t = jnp.where(lane == lanes - 1, 0.0, pltpu.roll(q5, lanes - 1, 1))
        inc_ref[x] = lower_a + upper_a + lower_r + upper_r + lower_t + upper_t
        pack4 = pack4 + jnp.where(lane == x, pltpu.roll(q4, (x + 1) % lanes, 1), 0.0)
        pack5 = pack5 + jnp.where(lane == x, pltpu.roll(q5, x, 1), 0.0) if x else jnp.where(lane == 0, q5, 0.0)
    pick = (pick_ref[...] == lax.broadcasted_iota(jnp.int32, (rows, rows), 1)).astype(jnp.bfloat16)
    got4 = exact_pick(pick, pack4)
    got5 = exact_pick(pick, pack5)
    up4 = pltpu.roll(got4, lanes - half, 1)
    down4 = pltpu.roll(got4, half, 1)
    up5 = pltpu.roll(got5, lanes - half, 1)
    down5 = pltpu.roll(got5, half, 1)
    real_half = lane < half
    wrap4 = jnp.where(real_half, cosine * got4 - sine * up4, sine * down4 + cosine * got4)
    wrap5 = jnp.where(real_half, cosine * got5 - (-sine) * up5, (-sine) * down5 + cosine * got5)
    diag = diag_ref[...]
    for x in range(comps):
        at_start = pltpu.roll(wrap4, (lanes - x) % lanes, 1)
        at_end = pltpu.roll(wrap5, lanes - 1 - x, 1)
        incoming = inc_ref[x] + jnp.where(lane == 0, at_start, 0.0) + jnp.where(lane == lanes - 1, at_end, 0.0)
        psi = psi_ref[x]
        swapped = psi_ref[x + half] if x < half else -psi_ref[x - half]
        residual = src_ref[x] - (diag * psi + omega * swapped) + incoming
        out_ref[x] = psi + RELAX * residual / diag
    if edges:
        write_edges(mat_ref, wt_ref, out_ref, face_ref, axs_ref, q2_ref, q3_ref, comps, tile_r)


def modes_kernel(where_ref, mode_ref, out_ref, *, blocks):
    owned = where_ref.shape[1]
    lanes = mode_ref.shape[1]
    lane_of = where_ref[0:1, :]
    row_of = where_ref[1:2, :]
    pick = (lax.broadcasted_iota(jnp.int32, (lanes, owned), 0) == lane_of).astype(jnp.bfloat16)
    hit = lax.broadcasted_iota(jnp.int32, (blocks, owned), 0) == row_of
    for g in range(out_ref.shape[0]):
        part = jnp.dot(mode_ref[pl.ds(g * blocks, blocks), :], pick, preferred_element_type=jnp.float32)
        out_ref[pl.ds(g, 1), :] = jnp.sum(jnp.where(hit, part, 0.0), axis=0, keepdims=True)


def vmem_spec():
    return pl.BlockSpec(memory_space=pltpu.MemorySpace.VMEM)


def smem_spec():
    return pl.BlockSpec(memory_space=SMEM)


def edge_shapes(comps, rows, tile_r):
    layers = rows // tile_r
    return (
        jax.ShapeDtypeStruct((comps, tile_r, LANES), jnp.float32),
        jax.ShapeDtypeStruct((comps, layers, LANES), jnp.float32),
        jax.ShapeDtypeStruct((comps, layers, LANES), jnp.float32),
    )


def run_edges(mat, weights, psi, face, tile_r):
    comps, rows, _ = psi.shape
    return pl.pallas_call(
        functools.partial(edges_kernel, tile_r=tile_r),
        out_shape=edge_shapes(comps, rows, tile_r),
        in_specs=[smem_spec(), smem_spec(), vmem_spec(), vmem_spec()],
        out_specs=tuple(vmem_spec() for _ in range(3)),
    )(mat, weights, psi, face)


def run_section(mat, weights, psi, src, face, diag, pick, axr, ralo, rahi, tile_r, edges):
    comps, rows, lanes = psi.shape
    return pl.pallas_call(
        functools.partial(section_kernel, tile_r=tile_r, edges=edges),
        out_shape=(jax.ShapeDtypeStruct(psi.shape, jnp.float32),) + edge_shapes(comps, rows, tile_r),
        in_specs=[smem_spec(), smem_spec()] + [vmem_spec() for _ in range(8)],
        out_specs=tuple(vmem_spec() for _ in range(4)),
        scratch_shapes=[pltpu.VMEM((comps, rows, lanes), jnp.float32)],
    )(mat, weights, psi, src, face, diag, pick, axr, ralo, rahi)


def neighbours(axis):
    count = lax.axis_size(axis)
    up = [(i, (i + 1) % count) for i in range(count - 1)]
    return up, [(j, i) for i, j in up]


def body(
    psi_start,
    source,
    face_coef,
    diag_coef,
    flux_jac,
    omega,
    metric,
    mode_shape,
    phase_weight,
    pairing,
    owner_order,
):
    matrices = build_matrices(flux_jac)
    comps = matrices.shape[1]
    mat = matrices.reshape(-1)
    local_phases, _, tile_a, tile_r, pitch = psi_start.shape
    rows = tile_a * tile_r
    cells = rows * pitch
    angle = lax.axis_index("phase").astype(jnp.float32) * (2.0 * math.pi / BLADES)
    me_axial = lax.axis_index("axial")
    lower_side = (me_axial == 0).astype(jnp.float32)
    upper_side = 1.0 - lower_side
    weights = jnp.stack(
        [
            upper_side,
            lower_side,
            omega[0],
            jnp.cos(angle),
            jnp.sin(angle),
            upper_side,
            lower_side,
        ]
    ).astype(jnp.float32)
    partner = pairing[0, 0]
    faces = face_coef.astype(jnp.float32).reshape(6, rows, pitch)
    diag = diag_coef.reshape(rows, pitch)
    pick = partner.astype(jnp.int32).reshape(rows, 1)
    up_r, down_r = neighbours("radial")
    psi = psi_start.reshape(comps, rows, pitch)
    src = source.reshape(comps, rows, pitch)
    axs, q2, q3 = run_edges(mat, weights, psi, faces, tile_r)
    for section in range(ITERS):
        axr = lax.ppermute(axs, "axial", [(0, 1), (1, 0)])
        ralo = lax.ppermute(q2, "radial", up_r)
        rahi = lax.ppermute(q3, "radial", down_r)
        psi, axs, q2, q3 = run_section(
            mat, weights, psi, src, faces, diag, pick, axr, ralo, rahi, tile_r, section < ITERS - 1
        )
    psi_out = psi.reshape(psi_start.shape)
    heights = jnp.einsum(
        "dc,cn->dn",
        metric,
        psi.reshape(comps, cells),
        precision=lax.Precision.HIGHEST,
    )
    weighted = phase_weight[0] * heights
    order = owner_order[0, 0]
    owners = lax.axis_size("phase")
    owned = cells // owners
    dims = weighted.shape[0]
    lanes = LANES
    blocks = cells // lanes
    lane_of = order % lanes
    row_of = order // lanes
    pick_lane = (lane_of[None, :] == jnp.arange(lanes, dtype=order.dtype)[:, None]).astype(jnp.float32)
    by_lane = jnp.einsum(
        "xl,lj->xj",
        weighted.reshape(dims * blocks, lanes),
        pick_lane,
        precision=lax.Precision.HIGHEST,
    ).reshape(dims, blocks, cells)
    pick_row = row_of[None, None, :] == jnp.arange(blocks, dtype=order.dtype)[None, :, None]
    in_order = jnp.sum(jnp.where(pick_row, by_lane, 0.0), axis=1)
    gathered = sum_at_owner(in_order, "phase", 1)
    mine = lax.dynamic_slice_in_dim(order, lax.axis_index("phase") * owned, owned)
    count_k = mode_shape.shape[0]
    where = jnp.stack([mine % lanes, mine // lanes]).astype(jnp.int32)
    modes = pl.pallas_call(
        functools.partial(modes_kernel, blocks=blocks),
        out_shape=jax.ShapeDtypeStruct((count_k * 3, owned), jnp.float32),
        in_specs=[vmem_spec(), vmem_spec()],
        out_specs=vmem_spec(),
    )(where, mode_shape.reshape(count_k * 3 * blocks, lanes)).reshape(count_k, 3, owned)
    sens = modes[:, 0] * gathered[0] + modes[:, 1] * gathered[1] + modes[:, 2] * gathered[2]
    return (psi_out, sens.reshape(count_k, 1, 1, owned))


def solution(mesh):
    return jax.shard_map(
        body,
        mesh=mesh,
        in_specs=(
            P("phase", None, "axial", "radial", None),
            P("phase", None, "axial", "radial", None),
            P(None, "axial", "radial", None),
            P("axial", "radial", None),
            P(),
            P(),
            P(),
            P(None, None, "axial", "radial", None),
            P("phase"),
            P("axial", "radial", None),
            P("axial", "radial", None),
        ),
        out_specs=(P("phase", None, "axial", "radial", None), P(None, "axial", "radial", "phase")),
        check_vma=False,
    )
```

```python
import functools
import math

import jax
import jax.numpy as jnp
from jax import lax
from jax.experimental import pallas as pl
from jax.experimental.pallas import tpu as pltpu
from jax.sharding import PartitionSpec as P

BLADES = 16
ITERS = 4


RELAX = 0.8
LANES = 128
SMEM = pltpu.MemorySpace.SMEM


def split_up(value, dim, count):
    dims = value.shape
    blocks = value.reshape(*dims[:dim], count, dims[dim] // count, *dims[dim + 1 :])
    return jnp.moveaxis(blocks, dim, 0)


def sum_at_owner(value, axis, dim):
    count = lax.axis_size(axis)
    blocks = lax.all_to_all(split_up(value, dim, count), axis, 0, 0, tiled=True)
    return jnp.sum(blocks, axis=0)


def sum_at_owner_paired(value, axis, dim):
    count = lax.axis_size(axis)
    blocks = split_up(value, dim, count)
    core = lax.axis_index(axis) % 2
    even, odd = blocks[0::2], blocks[1::2]
    send = jnp.where(core == 0, odd, even)
    keep = jnp.where(core == 0, even, odd)
    got = lax.ppermute(send, axis, [(p, p ^ 1) for p in range(count)])
    groups = [list(range(parity, count, 2)) for parity in range(2)]
    mixed = lax.all_to_all(keep + got, axis, 0, 0, tiled=True, axis_index_groups=groups)
    return jnp.sum(mixed, axis=0)


def build_matrices(flux_jac):
    real_part = jnp.swapaxes(flux_jac[:, 0], 1, 2)
    imag_part = jnp.swapaxes(flux_jac[:, 1], 1, 2)
    top_rows = jnp.concatenate([real_part, imag_part], axis=2)
    low_rows = jnp.concatenate([-imag_part, real_part], axis=2)
    return jnp.concatenate([top_rows, low_rows], axis=1)


def exact_pick(pick, values):
    first = values.astype(jnp.bfloat16)
    rest = values - first.astype(jnp.float32)
    second = rest.astype(jnp.bfloat16)
    third = (rest - second.astype(jnp.float32)).astype(jnp.bfloat16)
    out = jnp.dot(pick, first, preferred_element_type=jnp.float32)
    out = out + jnp.dot(pick, second, preferred_element_type=jnp.float32)
    return out + jnp.dot(pick, third, preferred_element_type=jnp.float32)


def applied(mat_ref, d, x, comps, load):
    total = mat_ref[(d * comps + x) * comps] * load(0)
    for c in range(1, comps):
        total = total + mat_ref[(d * comps + x) * comps + c] * load(c)
    return total


def write_edges(mat_ref, wt_ref, psi_ref, face_ref, axs_ref, q2_ref, q3_ref, comps, tile_r):
    rows = psi_ref.shape[1]
    layers = rows // tile_r
    top = pl.ds(rows - tile_r, tile_r)
    bottom = pl.ds(0, tile_r)
    r_top = pl.ds(tile_r - 1, layers, stride=tile_r)
    r_bottom = pl.ds(0, layers, stride=tile_r)
    keep_top = wt_ref[1]
    keep_bottom = wt_ref[0]
    for x in range(comps):
        up = face_ref[0, top, :] * applied(mat_ref, 0, x, comps, lambda c: psi_ref[c, top, :])
        down = face_ref[1, bottom, :] * applied(mat_ref, 1, x, comps, lambda c: psi_ref[c, bottom, :])
        axs_ref[x] = up * keep_top + down * keep_bottom
        q2_ref[x] = face_ref[2, r_top, :] * applied(mat_ref, 2, x, comps, lambda c: psi_ref[c, r_top, :])
        q3_ref[x] = face_ref[3, r_bottom, :] * applied(mat_ref, 3, x, comps, lambda c: psi_ref[c, r_bottom, :])


def edges_kernel(mat_ref, wt_ref, psi_ref, face_ref, axs_ref, q2_ref, q3_ref, *, tile_r):
    write_edges(mat_ref, wt_ref, psi_ref, face_ref, axs_ref, q2_ref, q3_ref, psi_ref.shape[0], tile_r)


def section_kernel(
    mat_ref, wt_ref, psi_ref, src_ref, face_ref, diag_ref, pick_ref, axr_ref, ralo_ref, rahi_ref,
    out_ref, axs_ref, q2_ref, q3_ref, inc_ref, *, tile_r, edges,
):
    comps, rows, lanes = psi_ref.shape
    half = comps // 2
    layers = rows // tile_r
    lane = lax.broadcasted_iota(jnp.int32, (rows, lanes), 1)
    row = lax.broadcasted_iota(jnp.int32, (rows, lanes), 0) % tile_r
    omega = wt_ref[2]
    cosine = wt_ref[3]
    sine = wt_ref[4]
    from_below = wt_ref[5]
    from_above = wt_ref[6]
    pack4 = jnp.zeros((rows, lanes), jnp.float32)
    pack5 = jnp.zeros((rows, lanes), jnp.float32)
    load = lambda c: psi_ref[c]
    for x in range(comps):
        q0 = face_ref[0] * applied(mat_ref, 0, x, comps, load)
        q1 = face_ref[1] * applied(mat_ref, 1, x, comps, load)
        q2 = face_ref[2] * applied(mat_ref, 2, x, comps, load)
        q3 = face_ref[3] * applied(mat_ref, 3, x, comps, load)
        q4 = face_ref[4] * applied(mat_ref, 4, x, comps, load)
        q5 = face_ref[5] * applied(mat_ref, 5, x, comps, load)
        got = axr_ref[x]
        lower_a = jnp.concatenate([got * from_below, q0[: rows - tile_r]], axis=0)
        upper_a = jnp.concatenate([q1[tile_r:], got * from_above], axis=0)
        low_r = ralo_ref[x]
        high_r = rahi_ref[x]
        low_rows = jnp.concatenate(
            [jnp.broadcast_to(low_r[j : j + 1, :], (tile_r, lanes)) for j in range(layers)], axis=0
        )
        high_rows = jnp.concatenate(
            [jnp.broadcast_to(high_r[j : j + 1, :], (tile_r, lanes)) for j in range(layers)], axis=0
        )
        lower_r = jnp.where(row == 0, low_rows, pltpu.roll(q2, 1, 0))
        upper_r = jnp.where(row == tile_r - 1, high_rows, pltpu.roll(q3, rows - 1, 0))
        lower_t = jnp.where(lane == 0, 0.0, pltpu.roll(q4, 1, 1))
        upper_t = jnp.where(lane == lanes - 1, 0.0, pltpu.roll(q5, lanes - 1, 1))
        inc_ref[x] = lower_a + upper_a + lower_r + upper_r + lower_t + upper_t
        pack4 = pack4 + jnp.where(lane == x, pltpu.roll(q4, (x + 1) % lanes, 1), 0.0)
        pack5 = pack5 + jnp.where(lane == x, pltpu.roll(q5, x, 1), 0.0) if x else jnp.where(lane == 0, q5, 0.0)
    pick = (pick_ref[...] == lax.broadcasted_iota(jnp.int32, (rows, rows), 1)).astype(jnp.bfloat16)
    got4 = exact_pick(pick, pack4)
    got5 = exact_pick(pick, pack5)
    up4 = pltpu.roll(got4, lanes - half, 1)
    down4 = pltpu.roll(got4, half, 1)
    up5 = pltpu.roll(got5, lanes - half, 1)
    down5 = pltpu.roll(got5, half, 1)
    real_half = lane < half
    wrap4 = jnp.where(real_half, cosine * got4 - sine * up4, sine * down4 + cosine * got4)
    wrap5 = jnp.where(real_half, cosine * got5 - (-sine) * up5, (-sine) * down5 + cosine * got5)
    diag = diag_ref[...]
    for x in range(comps):
        at_start = pltpu.roll(wrap4, (lanes - x) % lanes, 1)
        at_end = pltpu.roll(wrap5, lanes - 1 - x, 1)
        incoming = inc_ref[x] + jnp.where(lane == 0, at_start, 0.0) + jnp.where(lane == lanes - 1, at_end, 0.0)
        psi = psi_ref[x]
        swapped = psi_ref[x + half] if x < half else -psi_ref[x - half]
        residual = src_ref[x] - (diag * psi + omega * swapped) + incoming
        out_ref[x] = psi + RELAX * residual / diag
    if edges:
        write_edges(mat_ref, wt_ref, out_ref, face_ref, axs_ref, q2_ref, q3_ref, comps, tile_r)


def modes_kernel(where_ref, mode_ref, out_ref, *, blocks):
    owned = where_ref.shape[1]
    lanes = mode_ref.shape[1]
    lane_of = where_ref[0:1, :]
    row_of = where_ref[1:2, :]
    pick = (lax.broadcasted_iota(jnp.int32, (lanes, owned), 0) == lane_of).astype(jnp.bfloat16)
    hit = lax.broadcasted_iota(jnp.int32, (blocks, owned), 0) == row_of
    for g in range(out_ref.shape[0]):
        part = jnp.dot(mode_ref[pl.ds(g * blocks, blocks), :], pick, preferred_element_type=jnp.float32)
        out_ref[pl.ds(g, 1), :] = jnp.sum(jnp.where(hit, part, 0.0), axis=0, keepdims=True)


def vmem_spec():
    return pl.BlockSpec(memory_space=pltpu.MemorySpace.VMEM)


def smem_spec():
    return pl.BlockSpec(memory_space=SMEM)


def edge_shapes(comps, rows, tile_r):
    layers = rows // tile_r
    return (
        jax.ShapeDtypeStruct((comps, tile_r, LANES), jnp.float32),
        jax.ShapeDtypeStruct((comps, layers, LANES), jnp.float32),
        jax.ShapeDtypeStruct((comps, layers, LANES), jnp.float32),
    )


def run_edges(mat, weights, psi, face, tile_r):
    comps, rows, _ = psi.shape
    return pl.pallas_call(
        functools.partial(edges_kernel, tile_r=tile_r),
        out_shape=edge_shapes(comps, rows, tile_r),
        in_specs=[smem_spec(), smem_spec(), vmem_spec(), vmem_spec()],
        out_specs=tuple(vmem_spec() for _ in range(3)),
    )(mat, weights, psi, face)


def run_section(mat, weights, psi, src, face, diag, pick, axr, ralo, rahi, tile_r, edges):
    comps, rows, lanes = psi.shape
    return pl.pallas_call(
        functools.partial(section_kernel, tile_r=tile_r, edges=edges),
        out_shape=(jax.ShapeDtypeStruct(psi.shape, jnp.float32),) + edge_shapes(comps, rows, tile_r),
        in_specs=[smem_spec(), smem_spec()] + [vmem_spec() for _ in range(8)],
        out_specs=tuple(vmem_spec() for _ in range(4)),
        scratch_shapes=[pltpu.VMEM((comps, rows, lanes), jnp.float32)],
    )(mat, weights, psi, src, face, diag, pick, axr, ralo, rahi)


def neighbours(axis):
    count = lax.axis_size(axis)
    up = [(i, (i + 1) % count) for i in range(count - 1)]
    return up, [(j, i) for i, j in up]


def body(
    psi_start,
    source,
    face_coef,
    diag_coef,
    flux_jac,
    omega,
    metric,
    mode_shape,
    phase_weight,
    pairing,
    owner_order,
):
    matrices = build_matrices(flux_jac)
    comps = matrices.shape[1]
    mat = matrices.reshape(-1)
    local_phases, _, tile_a, tile_r, pitch = psi_start.shape
    rows = tile_a * tile_r
    cells = rows * pitch
    angle = lax.axis_index("phase").astype(jnp.float32) * (2.0 * math.pi / BLADES)
    me_axial = lax.axis_index("axial")
    lower_side = (me_axial == 0).astype(jnp.float32)
    upper_side = 1.0 - lower_side
    weights = jnp.stack(
        [
            upper_side,
            lower_side,
            omega[0],
            jnp.cos(angle),
            jnp.sin(angle),
            upper_side,
            lower_side,
        ]
    ).astype(jnp.float32)
    partner = pairing[0, 0]
    faces = face_coef.astype(jnp.float32).reshape(6, rows, pitch)
    diag = diag_coef.reshape(rows, pitch)
    pick = partner.astype(jnp.int32).reshape(rows, 1)
    up_r, down_r = neighbours("radial")
    psi = psi_start.reshape(comps, rows, pitch)
    src = source.reshape(comps, rows, pitch)
    axs, q2, q3 = run_edges(mat, weights, psi, faces, tile_r)
    for section in range(ITERS):
        axr = lax.ppermute(axs, "axial", [(0, 1), (1, 0)])
        ralo = lax.ppermute(q2, "radial", up_r)
        rahi = lax.ppermute(q3, "radial", down_r)
        psi, axs, q2, q3 = run_section(
            mat, weights, psi, src, faces, diag, pick, axr, ralo, rahi, tile_r, section < ITERS - 1
        )
    psi_out = psi.reshape(psi_start.shape)
    heights = jnp.einsum(
        "dc,cn->dn",
        metric,
        psi.reshape(comps, cells),
        precision=lax.Precision.HIGHEST,
    )
    weighted = phase_weight[0] * heights
    order = owner_order[0, 0]
    owners = lax.axis_size("phase")
    owned = cells // owners
    dims = weighted.shape[0]
    lanes = LANES
    blocks = cells // lanes
    lane_of = order % lanes
    row_of = order // lanes
    pick_lane = (lane_of[None, :] == jnp.arange(lanes, dtype=order.dtype)[:, None]).astype(jnp.float32)
    by_lane = jnp.einsum(
        "xl,lj->xj",
        weighted.reshape(dims * blocks, lanes),
        pick_lane,
        precision=lax.Precision.HIGHEST,
    ).reshape(dims, blocks, cells)
    pick_row = row_of[None, None, :] == jnp.arange(blocks, dtype=order.dtype)[None, :, None]
    in_order = jnp.sum(jnp.where(pick_row, by_lane, 0.0), axis=1)
    gathered = sum_at_owner_paired(in_order, "phase", 1) if owners % 2 == 0 else sum_at_owner(in_order, "phase", 1)
    mine = lax.dynamic_slice_in_dim(order, lax.axis_index("phase") * owned, owned)
    count_k = mode_shape.shape[0]
    where = jnp.stack([mine % lanes, mine // lanes]).astype(jnp.int32)
    modes = pl.pallas_call(
        functools.partial(modes_kernel, blocks=blocks),
        out_shape=jax.ShapeDtypeStruct((count_k * 3, owned), jnp.float32),
        in_specs=[vmem_spec(), vmem_spec()],
        out_specs=vmem_spec(),
    )(where, mode_shape.reshape(count_k * 3 * blocks, lanes)).reshape(count_k, 3, owned)
    sens = modes[:, 0] * gathered[0] + modes[:, 1] * gathered[1] + modes[:, 2] * gathered[2]
    return (psi_out, sens.reshape(count_k, 1, 1, owned))


def solution(mesh):
    return jax.shard_map(
        body,
        mesh=mesh,
        in_specs=(
            P("phase", None, "axial", "radial", None),
            P("phase", None, "axial", "radial", None),
            P(None, "axial", "radial", None),
            P("axial", "radial", None),
            P(),
            P(),
            P(),
            P(None, None, "axial", "radial", None),
            P("phase"),
            P("axial", "radial", None),
            P("axial", "radial", None),
        ),
        out_specs=(P("phase", None, "axial", "radial", None), P(None, "axial", "radial", "phase")),
        check_vma=False,
    )
```

```python
import functools
import math

import jax
import jax.numpy as jnp
from jax import lax
from jax.experimental import pallas as pl
from jax.experimental.pallas import tpu as pltpu
from jax.sharding import PartitionSpec as P

BLADES = 16
ITERS = 4


RELAX = 0.8
LANES = 128
SMEM = pltpu.MemorySpace.SMEM


def split_up(value, dim, count):
    dims = value.shape
    blocks = value.reshape(*dims[:dim], count, dims[dim] // count, *dims[dim + 1 :])
    return jnp.moveaxis(blocks, dim, 0)


def sum_at_owner(value, axis, dim):
    count = lax.axis_size(axis)
    blocks = lax.all_to_all(split_up(value, dim, count), axis, 0, 0, tiled=True)
    return jnp.sum(blocks, axis=0)


def sum_at_owner_paired(value, axis, dim):
    count = lax.axis_size(axis)
    blocks = split_up(value, dim, count)
    core = lax.axis_index(axis) % 2
    even, odd = blocks[0::2], blocks[1::2]
    send = jnp.where(core == 0, odd, even)
    keep = jnp.where(core == 0, even, odd)
    got = lax.ppermute(send, axis, [(p, p ^ 1) for p in range(count)])
    groups = [list(range(parity, count, 2)) for parity in range(2)]
    mixed = lax.all_to_all(keep + got, axis, 0, 0, tiled=True, axis_index_groups=groups)
    return jnp.sum(mixed, axis=0)


def build_matrices(flux_jac):
    real_part = jnp.swapaxes(flux_jac[:, 0], 1, 2)
    imag_part = jnp.swapaxes(flux_jac[:, 1], 1, 2)
    top_rows = jnp.concatenate([real_part, imag_part], axis=2)
    low_rows = jnp.concatenate([-imag_part, real_part], axis=2)
    return jnp.concatenate([top_rows, low_rows], axis=1)


def exact_pick(pick, values):
    first = values.astype(jnp.bfloat16)
    rest = values - first.astype(jnp.float32)
    second = rest.astype(jnp.bfloat16)
    third = (rest - second.astype(jnp.float32)).astype(jnp.bfloat16)
    out = jnp.dot(pick, first, preferred_element_type=jnp.float32)
    out = out + jnp.dot(pick, second, preferred_element_type=jnp.float32)
    return out + jnp.dot(pick, third, preferred_element_type=jnp.float32)


def applied(mat_ref, d, x, comps, load):
    total = mat_ref[(d * comps + x) * comps] * load(0)
    for c in range(1, comps):
        total = total + mat_ref[(d * comps + x) * comps + c] * load(c)
    return total


def write_edges(mat_ref, wt_ref, psi_ref, face_ref, axs_ref, q2_ref, q3_ref, comps, tile_r):
    rows = psi_ref.shape[1]
    layers = rows // tile_r
    top = pl.ds(rows - tile_r, tile_r)
    bottom = pl.ds(0, tile_r)
    r_top = pl.ds(tile_r - 1, layers, stride=tile_r)
    r_bottom = pl.ds(0, layers, stride=tile_r)
    keep_top = wt_ref[1]
    keep_bottom = wt_ref[0]
    for x in range(comps):
        up = face_ref[0, top, :] * applied(mat_ref, 0, x, comps, lambda c: psi_ref[c, top, :])
        down = face_ref[1, bottom, :] * applied(mat_ref, 1, x, comps, lambda c: psi_ref[c, bottom, :])
        axs_ref[x] = up * keep_top + down * keep_bottom
        q2_ref[x] = face_ref[2, r_top, :] * applied(mat_ref, 2, x, comps, lambda c: psi_ref[c, r_top, :])
        q3_ref[x] = face_ref[3, r_bottom, :] * applied(mat_ref, 3, x, comps, lambda c: psi_ref[c, r_bottom, :])


def edges_kernel(mat_ref, wt_ref, psi_ref, face_ref, axs_ref, q2_ref, q3_ref, *, tile_r):
    write_edges(mat_ref, wt_ref, psi_ref, face_ref, axs_ref, q2_ref, q3_ref, psi_ref.shape[0], tile_r)


def interior_kernel(
    mat_ref, wt_ref, psi_ref, src_ref, face_ref, diag_ref, pick_ref, res_ref, inc_ref, *, tile_r,
):
    comps, rows, lanes = psi_ref.shape
    half = comps // 2
    lane = lax.broadcasted_iota(jnp.int32, (rows, lanes), 1)
    row = lax.broadcasted_iota(jnp.int32, (rows, lanes), 0) % tile_r
    omega = wt_ref[2]
    cosine = wt_ref[3]
    sine = wt_ref[4]
    pack4 = jnp.zeros((rows, lanes), jnp.float32)
    pack5 = jnp.zeros((rows, lanes), jnp.float32)
    edge = jnp.zeros((tile_r, lanes), jnp.float32)
    load = lambda c: psi_ref[c]
    for x in range(comps):
        q0 = face_ref[0] * applied(mat_ref, 0, x, comps, load)
        q1 = face_ref[1] * applied(mat_ref, 1, x, comps, load)
        q2 = face_ref[2] * applied(mat_ref, 2, x, comps, load)
        q3 = face_ref[3] * applied(mat_ref, 3, x, comps, load)
        q4 = face_ref[4] * applied(mat_ref, 4, x, comps, load)
        q5 = face_ref[5] * applied(mat_ref, 5, x, comps, load)
        lower_a = jnp.concatenate([edge, q0[: rows - tile_r]], axis=0)
        upper_a = jnp.concatenate([q1[tile_r:], edge], axis=0)
        lower_r = jnp.where(row == 0, 0.0, pltpu.roll(q2, 1, 0))
        upper_r = jnp.where(row == tile_r - 1, 0.0, pltpu.roll(q3, rows - 1, 0))
        lower_t = jnp.where(lane == 0, 0.0, pltpu.roll(q4, 1, 1))
        upper_t = jnp.where(lane == lanes - 1, 0.0, pltpu.roll(q5, lanes - 1, 1))
        inc_ref[x] = lower_a + upper_a + lower_r + upper_r + lower_t + upper_t
        pack4 = pack4 + jnp.where(lane == x, pltpu.roll(q4, (x + 1) % lanes, 1), 0.0)
        pack5 = pack5 + jnp.where(lane == x, pltpu.roll(q5, x, 1), 0.0) if x else jnp.where(lane == 0, q5, 0.0)
    pick = (pick_ref[...] == lax.broadcasted_iota(jnp.int32, (rows, rows), 1)).astype(jnp.bfloat16)
    got4 = exact_pick(pick, pack4)
    got5 = exact_pick(pick, pack5)
    up4 = pltpu.roll(got4, lanes - half, 1)
    down4 = pltpu.roll(got4, half, 1)
    up5 = pltpu.roll(got5, lanes - half, 1)
    down5 = pltpu.roll(got5, half, 1)
    real_half = lane < half
    wrap4 = jnp.where(real_half, cosine * got4 - sine * up4, sine * down4 + cosine * got4)
    wrap5 = jnp.where(real_half, cosine * got5 - (-sine) * up5, (-sine) * down5 + cosine * got5)
    diag = diag_ref[...]
    for x in range(comps):
        at_start = pltpu.roll(wrap4, (lanes - x) % lanes, 1)
        at_end = pltpu.roll(wrap5, lanes - 1 - x, 1)
        incoming = inc_ref[x] + jnp.where(lane == 0, at_start, 0.0) + jnp.where(lane == lanes - 1, at_end, 0.0)
        psi = psi_ref[x]
        swapped = psi_ref[x + half] if x < half else -psi_ref[x - half]
        res_ref[x] = src_ref[x] - (diag * psi + omega * swapped) + incoming


def fixup_kernel(
    mat_ref, wt_ref, psi_ref, res_ref, face_ref, diag_ref, axr_ref, ralo_ref, rahi_ref,
    out_ref, axs_ref, q2_ref, q3_ref, *, tile_r, edges,
):
    comps, rows, lanes = psi_ref.shape
    layers = rows // tile_r
    row = lax.broadcasted_iota(jnp.int32, (rows, lanes), 0) % tile_r
    from_below = wt_ref[5]
    from_above = wt_ref[6]
    middle = jnp.zeros((rows - 2 * tile_r, lanes), jnp.float32)
    diag = diag_ref[...]
    for x in range(comps):
        got = axr_ref[x]
        low_r = ralo_ref[x]
        high_r = rahi_ref[x]
        low_rows = jnp.concatenate(
            [jnp.broadcast_to(low_r[j : j + 1, :], (tile_r, lanes)) for j in range(layers)], axis=0
        )
        high_rows = jnp.concatenate(
            [jnp.broadcast_to(high_r[j : j + 1, :], (tile_r, lanes)) for j in range(layers)], axis=0
        )
        halo = jnp.concatenate([got * from_below, middle, got * from_above], axis=0)
        halo = halo + jnp.where(row == 0, low_rows, 0.0) + jnp.where(row == tile_r - 1, high_rows, 0.0)
        out_ref[x] = psi_ref[x] + RELAX * (res_ref[x] + halo) / diag
    if edges:
        write_edges(mat_ref, wt_ref, out_ref, face_ref, axs_ref, q2_ref, q3_ref, comps, tile_r)


def modes_kernel(where_ref, mode_ref, out_ref, *, blocks):
    owned = where_ref.shape[1]
    lanes = mode_ref.shape[1]
    lane_of = where_ref[0:1, :]
    row_of = where_ref[1:2, :]
    pick = (lax.broadcasted_iota(jnp.int32, (lanes, owned), 0) == lane_of).astype(jnp.bfloat16)
    hit = lax.broadcasted_iota(jnp.int32, (blocks, owned), 0) == row_of
    for g in range(out_ref.shape[0]):
        part = jnp.dot(mode_ref[pl.ds(g * blocks, blocks), :], pick, preferred_element_type=jnp.float32)
        out_ref[pl.ds(g, 1), :] = jnp.sum(jnp.where(hit, part, 0.0), axis=0, keepdims=True)


def vmem_spec():
    return pl.BlockSpec(memory_space=pltpu.MemorySpace.VMEM)


def smem_spec():
    return pl.BlockSpec(memory_space=SMEM)


def edge_shapes(comps, rows, tile_r):
    layers = rows // tile_r
    return (
        jax.ShapeDtypeStruct((comps, tile_r, LANES), jnp.float32),
        jax.ShapeDtypeStruct((comps, layers, LANES), jnp.float32),
        jax.ShapeDtypeStruct((comps, layers, LANES), jnp.float32),
    )


def run_edges(mat, weights, psi, face, tile_r):
    comps, rows, _ = psi.shape
    return pl.pallas_call(
        functools.partial(edges_kernel, tile_r=tile_r),
        out_shape=edge_shapes(comps, rows, tile_r),
        in_specs=[smem_spec(), smem_spec(), vmem_spec(), vmem_spec()],
        out_specs=tuple(vmem_spec() for _ in range(3)),
    )(mat, weights, psi, face)


def run_interior(mat, weights, psi, src, face, diag, pick, tile_r):
    comps, rows, lanes = psi.shape
    return pl.pallas_call(
        functools.partial(interior_kernel, tile_r=tile_r),
        out_shape=jax.ShapeDtypeStruct(psi.shape, jnp.float32),
        in_specs=[smem_spec(), smem_spec()] + [vmem_spec() for _ in range(5)],
        out_specs=vmem_spec(),
        scratch_shapes=[pltpu.VMEM((comps, rows, lanes), jnp.float32)],
    )(mat, weights, psi, src, face, diag, pick)


def run_fixup(mat, weights, psi, res, face, diag, axr, ralo, rahi, tile_r, edges):
    comps, rows, lanes = psi.shape
    return pl.pallas_call(
        functools.partial(fixup_kernel, tile_r=tile_r, edges=edges),
        out_shape=(jax.ShapeDtypeStruct(psi.shape, jnp.float32),) + edge_shapes(comps, rows, tile_r),
        in_specs=[smem_spec(), smem_spec()] + [vmem_spec() for _ in range(7)],
        out_specs=tuple(vmem_spec() for _ in range(4)),
    )(mat, weights, psi, res, face, diag, axr, ralo, rahi)


def neighbours(axis):
    count = lax.axis_size(axis)
    up = [(i, (i + 1) % count) for i in range(count - 1)]
    return up, [(j, i) for i, j in up]


def body(
    psi_start,
    source,
    face_coef,
    diag_coef,
    flux_jac,
    omega,
    metric,
    mode_shape,
    phase_weight,
    pairing,
    owner_order,
):
    matrices = build_matrices(flux_jac)
    comps = matrices.shape[1]
    mat = matrices.reshape(-1)
    local_phases, _, tile_a, tile_r, pitch = psi_start.shape
    rows = tile_a * tile_r
    cells = rows * pitch
    angle = lax.axis_index("phase").astype(jnp.float32) * (2.0 * math.pi / BLADES)
    me_axial = lax.axis_index("axial")
    lower_side = (me_axial == 0).astype(jnp.float32)
    upper_side = 1.0 - lower_side
    weights = jnp.stack(
        [
            upper_side,
            lower_side,
            omega[0],
            jnp.cos(angle),
            jnp.sin(angle),
            upper_side,
            lower_side,
        ]
    ).astype(jnp.float32)
    partner = pairing[0, 0]
    faces = face_coef.astype(jnp.float32).reshape(6, rows, pitch)
    diag = diag_coef.reshape(rows, pitch)
    pick = partner.astype(jnp.int32).reshape(rows, 1)
    up_r, down_r = neighbours("radial")
    psi = psi_start.reshape(comps, rows, pitch)
    src = source.reshape(comps, rows, pitch)
    axs, q2, q3 = run_edges(mat, weights, psi, faces, tile_r)
    for section in range(ITERS):
        axr = lax.ppermute(axs, "axial", [(0, 1), (1, 0)])
        ralo = lax.ppermute(q2, "radial", up_r)
        rahi = lax.ppermute(q3, "radial", down_r)
        res = run_interior(mat, weights, psi, src, faces, diag, pick, tile_r)
        psi, axs, q2, q3 = run_fixup(
            mat, weights, psi, res, faces, diag, axr, ralo, rahi, tile_r, section < ITERS - 1
        )
    psi_out = psi.reshape(psi_start.shape)
    heights = jnp.einsum(
        "dc,cn->dn",
        metric,
        psi.reshape(comps, cells),
        precision=lax.Precision.HIGHEST,
    )
    weighted = phase_weight[0] * heights
    order = owner_order[0, 0]
    owners = lax.axis_size("phase")
    owned = cells // owners
    dims = weighted.shape[0]
    lanes = LANES
    blocks = cells // lanes
    lane_of = order % lanes
    row_of = order // lanes
    pick_lane = (lane_of[None, :] == jnp.arange(lanes, dtype=order.dtype)[:, None]).astype(jnp.float32)
    by_lane = jnp.einsum(
        "xl,lj->xj",
        weighted.reshape(dims * blocks, lanes),
        pick_lane,
        precision=lax.Precision.HIGHEST,
    ).reshape(dims, blocks, cells)
    pick_row = row_of[None, None, :] == jnp.arange(blocks, dtype=order.dtype)[None, :, None]
    in_order = jnp.sum(jnp.where(pick_row, by_lane, 0.0), axis=1)
    gathered = sum_at_owner_paired(in_order, "phase", 1) if owners % 2 == 0 else sum_at_owner(in_order, "phase", 1)
    mine = lax.dynamic_slice_in_dim(order, lax.axis_index("phase") * owned, owned)
    count_k = mode_shape.shape[0]
    where = jnp.stack([mine % lanes, mine // lanes]).astype(jnp.int32)
    modes = pl.pallas_call(
        functools.partial(modes_kernel, blocks=blocks),
        out_shape=jax.ShapeDtypeStruct((count_k * 3, owned), jnp.float32),
        in_specs=[vmem_spec(), vmem_spec()],
        out_specs=vmem_spec(),
    )(where, mode_shape.reshape(count_k * 3 * blocks, lanes)).reshape(count_k, 3, owned)
    sens = modes[:, 0] * gathered[0] + modes[:, 1] * gathered[1] + modes[:, 2] * gathered[2]
    return (psi_out, sens.reshape(count_k, 1, 1, owned))


def solution(mesh):
    return jax.shard_map(
        body,
        mesh=mesh,
        in_specs=(
            P("phase", None, "axial", "radial", None),
            P("phase", None, "axial", "radial", None),
            P(None, "axial", "radial", None),
            P("axial", "radial", None),
            P(),
            P(),
            P(),
            P(None, None, "axial", "radial", None),
            P("phase"),
            P("axial", "radial", None),
            P("axial", "radial", None),
        ),
        out_specs=(P("phase", None, "axial", "radial", None), P(None, "axial", "radial", "phase")),
        check_vma=False,
    )
```

```python
import functools
import math

import jax
import jax.numpy as jnp
from jax import lax
from jax.experimental import pallas as pl
from jax.experimental.pallas import tpu as pltpu
from jax.sharding import PartitionSpec as P

BLADES = 16
ITERS = 4


RELAX = 0.8
LANES = 128
SMEM = pltpu.MemorySpace.SMEM
METRIC = 8


def split_up(value, dim, count):
    dims = value.shape
    blocks = value.reshape(*dims[:dim], count, dims[dim] // count, *dims[dim + 1 :])
    return jnp.moveaxis(blocks, dim, 0)


def sum_at_owner(value, axis, dim):
    count = lax.axis_size(axis)
    blocks = lax.all_to_all(split_up(value, dim, count), axis, 0, 0, tiled=True)
    return jnp.sum(blocks, axis=0)


def sum_at_owner_paired(value, axis, dim):
    count = lax.axis_size(axis)
    blocks = split_up(value, dim, count)
    core = lax.axis_index(axis) % 2
    even, odd = blocks[0::2], blocks[1::2]
    send = jnp.where(core == 0, odd, even)
    keep = jnp.where(core == 0, even, odd)
    got = lax.ppermute(send, axis, [(p, p ^ 1) for p in range(count)])
    groups = [list(range(parity, count, 2)) for parity in range(2)]
    mixed = lax.all_to_all(keep + got, axis, 0, 0, tiled=True, axis_index_groups=groups)
    return jnp.sum(mixed, axis=0)


def build_matrices(flux_jac):
    real_part = jnp.swapaxes(flux_jac[:, 0], 1, 2)
    imag_part = jnp.swapaxes(flux_jac[:, 1], 1, 2)
    top_rows = jnp.concatenate([real_part, imag_part], axis=2)
    low_rows = jnp.concatenate([-imag_part, real_part], axis=2)
    return jnp.concatenate([top_rows, low_rows], axis=1)


def exact_pick(pick, values):
    first = values.astype(jnp.bfloat16)
    rest = values - first.astype(jnp.float32)
    second = rest.astype(jnp.bfloat16)
    third = (rest - second.astype(jnp.float32)).astype(jnp.bfloat16)
    out = jnp.dot(pick, first, preferred_element_type=jnp.float32)
    out = out + jnp.dot(pick, second, preferred_element_type=jnp.float32)
    return out + jnp.dot(pick, third, preferred_element_type=jnp.float32)


def applied(mat_ref, d, x, comps, load):
    total = mat_ref[(d * comps + x) * comps] * load(0)
    for c in range(1, comps):
        total = total + mat_ref[(d * comps + x) * comps + c] * load(c)
    return total


def write_edges(mat_ref, wt_ref, psi_ref, face_ref, axs_ref, q2_ref, q3_ref, comps, tile_r):
    rows = psi_ref.shape[1]
    layers = rows // tile_r
    top = pl.ds(rows - tile_r, tile_r)
    bottom = pl.ds(0, tile_r)
    r_top = pl.ds(tile_r - 1, layers, stride=tile_r)
    r_bottom = pl.ds(0, layers, stride=tile_r)
    keep_top = wt_ref[6 * comps * comps + 1]
    keep_bottom = wt_ref[6 * comps * comps + 0]
    for x in range(comps):
        up = face_ref[0, top, :] * applied(mat_ref, 0, x, comps, lambda c: psi_ref[c, top, :])
        down = face_ref[1, bottom, :] * applied(mat_ref, 1, x, comps, lambda c: psi_ref[c, bottom, :])
        axs_ref[x] = up * keep_top + down * keep_bottom
        q2_ref[x] = face_ref[2, r_top, :] * applied(mat_ref, 2, x, comps, lambda c: psi_ref[c, r_top, :])
        q3_ref[x] = face_ref[3, r_bottom, :] * applied(mat_ref, 3, x, comps, lambda c: psi_ref[c, r_bottom, :])


def edges_kernel(mat_ref, wt_ref, psi_ref, face_ref, axs_ref, q2_ref, q3_ref, *, tile_r):
    write_edges(mat_ref, wt_ref, psi_ref, face_ref, axs_ref, q2_ref, q3_ref, psi_ref.shape[0], tile_r)


def interior_kernel(
    mat_ref, wt_ref, psi_ref, src_ref, face_ref, diag_ref, pick_ref, res_ref, inc_ref, *, tile_r,
):
    comps, rows, lanes = psi_ref.shape
    half = comps // 2
    lane = lax.broadcasted_iota(jnp.int32, (rows, lanes), 1)
    row = lax.broadcasted_iota(jnp.int32, (rows, lanes), 0) % tile_r
    omega = wt_ref[6 * comps * comps + 2]
    cosine = wt_ref[6 * comps * comps + 3]
    sine = wt_ref[6 * comps * comps + 4]
    pack4 = jnp.zeros((rows, lanes), jnp.float32)
    pack5 = jnp.zeros((rows, lanes), jnp.float32)
    edge = jnp.zeros((tile_r, lanes), jnp.float32)
    load = lambda c: psi_ref[c]
    for x in range(comps):
        q0 = face_ref[0] * applied(mat_ref, 0, x, comps, load)
        q1 = face_ref[1] * applied(mat_ref, 1, x, comps, load)
        q2 = face_ref[2] * applied(mat_ref, 2, x, comps, load)
        q3 = face_ref[3] * applied(mat_ref, 3, x, comps, load)
        q4 = face_ref[4] * applied(mat_ref, 4, x, comps, load)
        q5 = face_ref[5] * applied(mat_ref, 5, x, comps, load)
        lower_a = jnp.concatenate([edge, q0[: rows - tile_r]], axis=0)
        upper_a = jnp.concatenate([q1[tile_r:], edge], axis=0)
        lower_r = jnp.where(row == 0, 0.0, pltpu.roll(q2, 1, 0))
        upper_r = jnp.where(row == tile_r - 1, 0.0, pltpu.roll(q3, rows - 1, 0))
        lower_t = jnp.where(lane == 0, 0.0, pltpu.roll(q4, 1, 1))
        upper_t = jnp.where(lane == lanes - 1, 0.0, pltpu.roll(q5, lanes - 1, 1))
        inc_ref[x] = lower_a + upper_a + lower_r + upper_r + lower_t + upper_t
        pack4 = pack4 + jnp.where(lane == x, pltpu.roll(q4, (x + 1) % lanes, 1), 0.0)
        pack5 = pack5 + jnp.where(lane == x, pltpu.roll(q5, x, 1), 0.0) if x else jnp.where(lane == 0, q5, 0.0)
    pick = (pick_ref[...] == lax.broadcasted_iota(jnp.int32, (rows, rows), 1)).astype(jnp.bfloat16)
    got4 = exact_pick(pick, pack4)
    got5 = exact_pick(pick, pack5)
    up4 = pltpu.roll(got4, lanes - half, 1)
    down4 = pltpu.roll(got4, half, 1)
    up5 = pltpu.roll(got5, lanes - half, 1)
    down5 = pltpu.roll(got5, half, 1)
    real_half = lane < half
    wrap4 = jnp.where(real_half, cosine * got4 - sine * up4, sine * down4 + cosine * got4)
    wrap5 = jnp.where(real_half, cosine * got5 - (-sine) * up5, (-sine) * down5 + cosine * got5)
    diag = diag_ref[...]
    for x in range(comps):
        at_start = pltpu.roll(wrap4, (lanes - x) % lanes, 1)
        at_end = pltpu.roll(wrap5, lanes - 1 - x, 1)
        incoming = inc_ref[x] + jnp.where(lane == 0, at_start, 0.0) + jnp.where(lane == lanes - 1, at_end, 0.0)
        psi = psi_ref[x]
        swapped = psi_ref[x + half] if x < half else -psi_ref[x - half]
        res_ref[x] = src_ref[x] - (diag * psi + omega * swapped) + incoming


def fixup_kernel(
    mat_ref, wt_ref, psi_ref, res_ref, face_ref, diag_ref, axr_ref, ralo_ref, rahi_ref,
    out_ref, axs_ref, *radial_refs, tile_r, edges, dims,
):
    comps, rows, lanes = psi_ref.shape
    layers = rows // tile_r
    row = lax.broadcasted_iota(jnp.int32, (rows, lanes), 0) % tile_r
    from_below = wt_ref[6 * comps * comps + 5]
    from_above = wt_ref[6 * comps * comps + 6]
    middle = jnp.zeros((rows - 2 * tile_r, lanes), jnp.float32)
    diag = diag_ref[...]
    for x in range(comps):
        got = axr_ref[x]
        low_r = ralo_ref[x]
        high_r = rahi_ref[x]
        low_rows = jnp.concatenate(
            [jnp.broadcast_to(low_r[j : j + 1, :], (tile_r, lanes)) for j in range(layers)], axis=0
        )
        high_rows = jnp.concatenate(
            [jnp.broadcast_to(high_r[j : j + 1, :], (tile_r, lanes)) for j in range(layers)], axis=0
        )
        halo = jnp.concatenate([got * from_below, middle, got * from_above], axis=0)
        halo = halo + jnp.where(row == 0, low_rows, 0.0) + jnp.where(row == tile_r - 1, high_rows, 0.0)
        out_ref[x] = psi_ref[x] + RELAX * (res_ref[x] + halo) / diag
    if edges:
        write_edges(mat_ref, wt_ref, out_ref, face_ref, axs_ref, *radial_refs, comps, tile_r)
    else:
        for d in range(dims):
            height = wt_ref[6 * comps * comps + METRIC + d * comps] * out_ref[0]
            for c in range(1, comps):
                height = height + wt_ref[6 * comps * comps + METRIC + d * comps + c] * out_ref[c]
            axs_ref[d] = wt_ref[6 * comps * comps + METRIC - 1] * height


def modes_kernel(where_ref, mode_ref, out_ref, *, blocks):
    owned = where_ref.shape[1]
    lanes = mode_ref.shape[1]
    lane_of = where_ref[0:1, :]
    row_of = where_ref[1:2, :]
    pick = (lax.broadcasted_iota(jnp.int32, (lanes, owned), 0) == lane_of).astype(jnp.bfloat16)
    hit = lax.broadcasted_iota(jnp.int32, (blocks, owned), 0) == row_of
    for g in range(out_ref.shape[0]):
        part = jnp.dot(mode_ref[pl.ds(g * blocks, blocks), :], pick, preferred_element_type=jnp.float32)
        out_ref[pl.ds(g, 1), :] = jnp.sum(jnp.where(hit, part, 0.0), axis=0, keepdims=True)


def vmem_spec():
    return pl.BlockSpec(memory_space=pltpu.MemorySpace.VMEM)


def smem_spec():
    return pl.BlockSpec(memory_space=SMEM)


def edge_shapes(comps, rows, tile_r):
    layers = rows // tile_r
    return (
        jax.ShapeDtypeStruct((comps, tile_r, LANES), jnp.float32),
        jax.ShapeDtypeStruct((comps, layers, LANES), jnp.float32),
        jax.ShapeDtypeStruct((comps, layers, LANES), jnp.float32),
    )


def run_edges(mat, weights, psi, face, tile_r):
    comps, rows, _ = psi.shape
    return pl.pallas_call(
        functools.partial(edges_kernel, tile_r=tile_r),
        out_shape=edge_shapes(comps, rows, tile_r),
        in_specs=[smem_spec(), smem_spec(), vmem_spec(), vmem_spec()],
        out_specs=tuple(vmem_spec() for _ in range(3)),
    )(mat, weights, psi, face)


def run_interior(mat, weights, psi, src, face, diag, pick, tile_r):
    comps, rows, lanes = psi.shape
    return pl.pallas_call(
        functools.partial(interior_kernel, tile_r=tile_r),
        out_shape=jax.ShapeDtypeStruct(psi.shape, jnp.float32),
        in_specs=[smem_spec(), smem_spec()] + [vmem_spec() for _ in range(5)],
        out_specs=vmem_spec(),
        scratch_shapes=[pltpu.VMEM((comps, rows, lanes), jnp.float32)],
    )(mat, weights, psi, src, face, diag, pick)


def run_fixup(mat, weights, psi, res, face, diag, axr, ralo, rahi, tile_r, edges, dims):
    comps, rows, lanes = psi.shape
    tail = edge_shapes(comps, rows, tile_r) if edges else (jax.ShapeDtypeStruct((dims, rows, lanes), jnp.float32),)
    return pl.pallas_call(
        functools.partial(fixup_kernel, tile_r=tile_r, edges=edges, dims=dims),
        out_shape=(jax.ShapeDtypeStruct(psi.shape, jnp.float32),) + tail,
        in_specs=[smem_spec(), smem_spec()] + [vmem_spec() for _ in range(7)],
        out_specs=tuple(vmem_spec() for _ in range(1 + len(tail))),
    )(mat, weights, psi, res, face, diag, axr, ralo, rahi)


def neighbours(axis):
    count = lax.axis_size(axis)
    up = [(i, (i + 1) % count) for i in range(count - 1)]
    return up, [(j, i) for i, j in up]


def body(
    psi_start,
    source,
    face_coef,
    diag_coef,
    flux_jac,
    omega,
    metric,
    mode_shape,
    phase_weight,
    pairing,
    owner_order,
):
    matrices = build_matrices(flux_jac)
    comps = matrices.shape[1]
    mat = matrices.reshape(-1)
    local_phases, _, tile_a, tile_r, pitch = psi_start.shape
    rows = tile_a * tile_r
    cells = rows * pitch
    angle = lax.axis_index("phase").astype(jnp.float32) * (2.0 * math.pi / BLADES)
    me_axial = lax.axis_index("axial")
    lower_side = (me_axial == 0).astype(jnp.float32)
    upper_side = 1.0 - lower_side
    dims = metric.shape[0]
    scalars = jnp.stack(
        [
            upper_side,
            lower_side,
            omega[0],
            jnp.cos(angle),
            jnp.sin(angle),
            upper_side,
            lower_side,
            phase_weight[0],
        ]
    ).astype(jnp.float32)
    weights = jnp.concatenate([scalars, metric.reshape(-1)])
    mat_weights = jnp.concatenate([mat, weights])
    mat = mat_weights
    weights = mat_weights
    partner = pairing[0, 0]
    faces = face_coef.astype(jnp.float32).reshape(6, rows, pitch)
    diag = diag_coef.reshape(rows, pitch)
    pick = partner.astype(jnp.int32).reshape(rows, 1)
    up_r, down_r = neighbours("radial")
    psi = psi_start.reshape(comps, rows, pitch)
    src = source.reshape(comps, rows, pitch)
    axs, q2, q3 = run_edges(mat, weights, psi, faces, tile_r)
    for section in range(ITERS):
        axr = lax.ppermute(axs, "axial", [(0, 1), (1, 0)])
        ralo = lax.ppermute(q2, "radial", up_r)
        rahi = lax.ppermute(q3, "radial", down_r)
        res = run_interior(mat, weights, psi, src, faces, diag, pick, tile_r)
        if section < ITERS - 1:
            psi, axs, q2, q3 = run_fixup(
                mat, weights, psi, res, faces, diag, axr, ralo, rahi, tile_r, True, dims
            )
        else:
            psi, weighted = run_fixup(
                mat, weights, psi, res, faces, diag, axr, ralo, rahi, tile_r, False, dims
            )
    psi_out = psi.reshape(psi_start.shape)
    order = owner_order[0, 0]
    owners = lax.axis_size("phase")
    owned = cells // owners
    dims = weighted.shape[0]
    lanes = LANES
    blocks = cells // lanes
    lane_of = order % lanes
    row_of = order // lanes
    pick_lane = (lane_of[None, :] == jnp.arange(lanes, dtype=order.dtype)[:, None]).astype(jnp.float32)
    by_lane = jnp.einsum(
        "xl,lj->xj",
        weighted.reshape(dims * blocks, lanes),
        pick_lane,
        precision=lax.Precision.HIGHEST,
    ).reshape(dims, blocks, cells)
    pick_row = row_of[None, None, :] == jnp.arange(blocks, dtype=order.dtype)[None, :, None]
    in_order = jnp.sum(jnp.where(pick_row, by_lane, 0.0), axis=1)
    gathered = sum_at_owner_paired(in_order, "phase", 1) if owners % 2 == 0 else sum_at_owner(in_order, "phase", 1)
    mine = lax.dynamic_slice_in_dim(order, lax.axis_index("phase") * owned, owned)
    count_k = mode_shape.shape[0]
    where = jnp.stack([mine % lanes, mine // lanes]).astype(jnp.int32)
    modes = pl.pallas_call(
        functools.partial(modes_kernel, blocks=blocks),
        out_shape=jax.ShapeDtypeStruct((count_k * 3, owned), jnp.float32),
        in_specs=[vmem_spec(), vmem_spec()],
        out_specs=vmem_spec(),
    )(where, mode_shape.reshape(count_k * 3 * blocks, lanes)).reshape(count_k, 3, owned)
    sens = modes[:, 0] * gathered[0] + modes[:, 1] * gathered[1] + modes[:, 2] * gathered[2]
    return (psi_out, sens.reshape(count_k, 1, 1, owned))


def solution(mesh):
    return jax.shard_map(
        body,
        mesh=mesh,
        in_specs=(
            P("phase", None, "axial", "radial", None),
            P("phase", None, "axial", "radial", None),
            P(None, "axial", "radial", None),
            P("axial", "radial", None),
            P(),
            P(),
            P(),
            P(None, None, "axial", "radial", None),
            P("phase"),
            P("axial", "radial", None),
            P("axial", "radial", None),
        ),
        out_specs=(P("phase", None, "axial", "radial", None), P(None, "axial", "radial", "phase")),
        check_vma=False,
    )
```

```python
import functools
import math

import jax
import jax.numpy as jnp
from jax import lax
from jax.experimental import pallas as pl
from jax.experimental.pallas import tpu as pltpu
from jax.sharding import PartitionSpec as P

BLADES = 16
ITERS = 4


RELAX = 0.8
LANES = 128
SMEM = pltpu.MemorySpace.SMEM
METRIC = 8


def split_up(value, dim, count):
    dims = value.shape
    blocks = value.reshape(*dims[:dim], count, dims[dim] // count, *dims[dim + 1 :])
    return jnp.moveaxis(blocks, dim, 0)


def sum_at_owner(value, axis, dim):
    count = lax.axis_size(axis)
    blocks = lax.all_to_all(split_up(value, dim, count), axis, 0, 0, tiled=True)
    return jnp.sum(blocks, axis=0)


def sum_at_owner_paired(value, axis, dim):
    count = lax.axis_size(axis)
    blocks = split_up(value, dim, count)
    core = lax.axis_index(axis) % 2
    even, odd = blocks[0::2], blocks[1::2]
    send = jnp.where(core == 0, odd, even)
    keep = jnp.where(core == 0, even, odd)
    got = lax.ppermute(send, axis, [(p, p ^ 1) for p in range(count)])
    groups = [list(range(parity, count, 2)) for parity in range(2)]
    mixed = lax.all_to_all(keep + got, axis, 0, 0, tiled=True, axis_index_groups=groups)
    return jnp.sum(mixed, axis=0)


def build_matrices(flux_jac):
    real_part = jnp.swapaxes(flux_jac[:, 0], 1, 2)
    imag_part = jnp.swapaxes(flux_jac[:, 1], 1, 2)
    top_rows = jnp.concatenate([real_part, imag_part], axis=2)
    low_rows = jnp.concatenate([-imag_part, real_part], axis=2)
    return jnp.concatenate([top_rows, low_rows], axis=1)


def exact_pick(pick, values):
    first = values.astype(jnp.bfloat16)
    rest = values - first.astype(jnp.float32)
    second = rest.astype(jnp.bfloat16)
    third = (rest - second.astype(jnp.float32)).astype(jnp.bfloat16)
    out = jnp.dot(pick, first, preferred_element_type=jnp.float32)
    out = out + jnp.dot(pick, second, preferred_element_type=jnp.float32)
    return out + jnp.dot(pick, third, preferred_element_type=jnp.float32)


def applied(mat_ref, d, x, comps, load):
    total = mat_ref[(d * comps + x) * comps] * load(0)
    for c in range(1, comps):
        total = total + mat_ref[(d * comps + x) * comps + c] * load(c)
    return total


def write_edges(mat_ref, wt_ref, psi_ref, face_ref, axs_ref, q2_ref, q3_ref, comps, tile_r):
    rows = psi_ref.shape[1]
    layers = rows // tile_r
    top = pl.ds(rows - tile_r, tile_r)
    bottom = pl.ds(0, tile_r)
    r_top = pl.ds(tile_r - 1, layers, stride=tile_r)
    r_bottom = pl.ds(0, layers, stride=tile_r)
    keep_top = wt_ref[6 * comps * comps + 1]
    keep_bottom = wt_ref[6 * comps * comps + 0]
    for x in range(comps):
        up = face_ref[0, top, :] * applied(mat_ref, 0, x, comps, lambda c: psi_ref[c, top, :])
        down = face_ref[1, bottom, :] * applied(mat_ref, 1, x, comps, lambda c: psi_ref[c, bottom, :])
        axs_ref[x] = up * keep_top + down * keep_bottom
        q2_ref[x] = face_ref[2, r_top, :] * applied(mat_ref, 2, x, comps, lambda c: psi_ref[c, r_top, :])
        q3_ref[x] = face_ref[3, r_bottom, :] * applied(mat_ref, 3, x, comps, lambda c: psi_ref[c, r_bottom, :])


def edges_kernel(mat_ref, wt_ref, psi_ref, face_ref, axs_ref, q2_ref, q3_ref, *, tile_r):
    write_edges(mat_ref, wt_ref, psi_ref, face_ref, axs_ref, q2_ref, q3_ref, psi_ref.shape[0], tile_r)


def gauss_pair(gauss_ref, d, x, half, sum_ref, psi_ref):
    base = (d * 3) * half * half + x * half
    def dot(which, load):
        start = base + which * half * half
        total = gauss_ref[start] * load(0)
        for c in range(1, half):
            total = total + gauss_ref[start + c] * load(c)
        return total
    shared = dot(0, lambda c: sum_ref[c])
    real = shared + dot(1, lambda c: psi_ref[c + half])
    imag = shared - dot(2, lambda c: psi_ref[c])
    return real, imag


def interior_kernel(
    mat_ref, wt_ref, psi_ref, src_ref, face_ref, diag_ref, pick_ref, res_ref, inc_ref, sum_ref, *, tile_r,
):
    comps, rows, lanes = psi_ref.shape
    half = comps // 2
    gauss_ref = mat_ref
    gauss_at = 6 * comps * comps + METRIC + 64
    lane = lax.broadcasted_iota(jnp.int32, (rows, lanes), 1)
    row = lax.broadcasted_iota(jnp.int32, (rows, lanes), 0) % tile_r
    omega = wt_ref[6 * comps * comps + 2]
    cosine = wt_ref[6 * comps * comps + 3]
    sine = wt_ref[6 * comps * comps + 4]
    for c in range(half):
        sum_ref[c] = psi_ref[c] + psi_ref[c + half]
    pack4 = jnp.zeros((rows, lanes), jnp.float32)
    pack5 = jnp.zeros((rows, lanes), jnp.float32)
    edge = jnp.zeros((tile_r, lanes), jnp.float32)
    shifted = gauss_ref.at[pl.ds(gauss_at, 6 * 3 * half * half)]
    for x in range(half):
        pair = [(x, 0), (x + half, 1)]
        q = [[None, None] for _ in range(6)]
        for d in range(6):
            real, imag = gauss_pair(shifted, d, x, half, sum_ref, psi_ref)
            q[d][0] = face_ref[d] * real
            q[d][1] = face_ref[d] * imag
        for comp, k in pair:
            q0, q1, q2, q3, q4, q5 = (q[d][k] for d in range(6))
            lower_a = jnp.concatenate([edge, q0[: rows - tile_r]], axis=0)
            upper_a = jnp.concatenate([q1[tile_r:], edge], axis=0)
            lower_r = jnp.where(row == 0, 0.0, pltpu.roll(q2, 1, 0))
            upper_r = jnp.where(row == tile_r - 1, 0.0, pltpu.roll(q3, rows - 1, 0))
            lower_t = jnp.where(lane == 0, 0.0, pltpu.roll(q4, 1, 1))
            upper_t = jnp.where(lane == lanes - 1, 0.0, pltpu.roll(q5, lanes - 1, 1))
            inc_ref[comp] = lower_a + upper_a + lower_r + upper_r + lower_t + upper_t
            pack4 = pack4 + jnp.where(lane == comp, pltpu.roll(q4, (comp + 1) % lanes, 1), 0.0)
            pack5 = pack5 + jnp.where(lane == comp, pltpu.roll(q5, comp, 1), 0.0) if comp else jnp.where(lane == 0, q5, 0.0)
    pick = (pick_ref[...] == lax.broadcasted_iota(jnp.int32, (rows, rows), 1)).astype(jnp.bfloat16)
    got4 = exact_pick(pick, pack4)
    got5 = exact_pick(pick, pack5)
    up4 = pltpu.roll(got4, lanes - half, 1)
    down4 = pltpu.roll(got4, half, 1)
    up5 = pltpu.roll(got5, lanes - half, 1)
    down5 = pltpu.roll(got5, half, 1)
    real_half = lane < half
    wrap4 = jnp.where(real_half, cosine * got4 - sine * up4, sine * down4 + cosine * got4)
    wrap5 = jnp.where(real_half, cosine * got5 - (-sine) * up5, (-sine) * down5 + cosine * got5)
    diag = diag_ref[...]
    for x in range(comps):
        at_start = pltpu.roll(wrap4, (lanes - x) % lanes, 1)
        at_end = pltpu.roll(wrap5, lanes - 1 - x, 1)
        incoming = inc_ref[x] + jnp.where(lane == 0, at_start, 0.0) + jnp.where(lane == lanes - 1, at_end, 0.0)
        psi = psi_ref[x]
        swapped = psi_ref[x + half] if x < half else -psi_ref[x - half]
        res_ref[x] = src_ref[x] - (diag * psi + omega * swapped) + incoming


def fixup_kernel(
    mat_ref, wt_ref, psi_ref, res_ref, face_ref, diag_ref, axr_ref, ralo_ref, rahi_ref,
    out_ref, axs_ref, *radial_refs, tile_r, edges, dims,
):
    comps, rows, lanes = psi_ref.shape
    layers = rows // tile_r
    row = lax.broadcasted_iota(jnp.int32, (rows, lanes), 0) % tile_r
    from_below = wt_ref[6 * comps * comps + 5]
    from_above = wt_ref[6 * comps * comps + 6]
    middle = jnp.zeros((rows - 2 * tile_r, lanes), jnp.float32)
    diag = diag_ref[...]
    for x in range(comps):
        got = axr_ref[x]
        low_r = ralo_ref[x]
        high_r = rahi_ref[x]
        low_rows = jnp.concatenate(
            [jnp.broadcast_to(low_r[j : j + 1, :], (tile_r, lanes)) for j in range(layers)], axis=0
        )
        high_rows = jnp.concatenate(
            [jnp.broadcast_to(high_r[j : j + 1, :], (tile_r, lanes)) for j in range(layers)], axis=0
        )
        halo = jnp.concatenate([got * from_below, middle, got * from_above], axis=0)
        halo = halo + jnp.where(row == 0, low_rows, 0.0) + jnp.where(row == tile_r - 1, high_rows, 0.0)
        out_ref[x] = psi_ref[x] + RELAX * (res_ref[x] + halo) / diag
    if edges:
        write_edges(mat_ref, wt_ref, out_ref, face_ref, axs_ref, *radial_refs, comps, tile_r)
    else:
        for d in range(dims):
            height = wt_ref[6 * comps * comps + METRIC + d * comps] * out_ref[0]
            for c in range(1, comps):
                height = height + wt_ref[6 * comps * comps + METRIC + d * comps + c] * out_ref[c]
            axs_ref[d] = wt_ref[6 * comps * comps + METRIC - 1] * height


def modes_kernel(where_ref, mode_ref, out_ref, *, blocks):
    owned = where_ref.shape[1]
    lanes = mode_ref.shape[1]
    lane_of = where_ref[0:1, :]
    row_of = where_ref[1:2, :]
    pick = (lax.broadcasted_iota(jnp.int32, (lanes, owned), 0) == lane_of).astype(jnp.bfloat16)
    hit = lax.broadcasted_iota(jnp.int32, (blocks, owned), 0) == row_of
    for g in range(out_ref.shape[0]):
        part = jnp.dot(mode_ref[pl.ds(g * blocks, blocks), :], pick, preferred_element_type=jnp.float32)
        out_ref[pl.ds(g, 1), :] = jnp.sum(jnp.where(hit, part, 0.0), axis=0, keepdims=True)


def vmem_spec():
    return pl.BlockSpec(memory_space=pltpu.MemorySpace.VMEM)


def smem_spec():
    return pl.BlockSpec(memory_space=SMEM)


def edge_shapes(comps, rows, tile_r):
    layers = rows // tile_r
    return (
        jax.ShapeDtypeStruct((comps, tile_r, LANES), jnp.float32),
        jax.ShapeDtypeStruct((comps, layers, LANES), jnp.float32),
        jax.ShapeDtypeStruct((comps, layers, LANES), jnp.float32),
    )


def run_edges(mat, weights, psi, face, tile_r):
    comps, rows, _ = psi.shape
    return pl.pallas_call(
        functools.partial(edges_kernel, tile_r=tile_r),
        out_shape=edge_shapes(comps, rows, tile_r),
        in_specs=[smem_spec(), smem_spec(), vmem_spec(), vmem_spec()],
        out_specs=tuple(vmem_spec() for _ in range(3)),
    )(mat, weights, psi, face)


def run_interior(mat, weights, psi, src, face, diag, pick, tile_r):
    comps, rows, lanes = psi.shape
    return pl.pallas_call(
        functools.partial(interior_kernel, tile_r=tile_r),
        out_shape=jax.ShapeDtypeStruct(psi.shape, jnp.float32),
        in_specs=[smem_spec(), smem_spec()] + [vmem_spec() for _ in range(5)],
        out_specs=vmem_spec(),
        scratch_shapes=[pltpu.VMEM((comps, rows, lanes), jnp.float32), pltpu.VMEM((comps // 2, rows, lanes), jnp.float32)],
    )(mat, weights, psi, src, face, diag, pick)


def run_fixup(mat, weights, psi, res, face, diag, axr, ralo, rahi, tile_r, edges, dims):
    comps, rows, lanes = psi.shape
    tail = edge_shapes(comps, rows, tile_r) if edges else (jax.ShapeDtypeStruct((dims, rows, lanes), jnp.float32),)
    return pl.pallas_call(
        functools.partial(fixup_kernel, tile_r=tile_r, edges=edges, dims=dims),
        out_shape=(jax.ShapeDtypeStruct(psi.shape, jnp.float32),) + tail,
        in_specs=[smem_spec(), smem_spec()] + [vmem_spec() for _ in range(7)],
        out_specs=tuple(vmem_spec() for _ in range(1 + len(tail))),
    )(mat, weights, psi, res, face, diag, axr, ralo, rahi)


def neighbours(axis):
    count = lax.axis_size(axis)
    up = [(i, (i + 1) % count) for i in range(count - 1)]
    return up, [(j, i) for i, j in up]


def body(
    psi_start,
    source,
    face_coef,
    diag_coef,
    flux_jac,
    omega,
    metric,
    mode_shape,
    phase_weight,
    pairing,
    owner_order,
):
    matrices = build_matrices(flux_jac)
    comps = matrices.shape[1]
    mat = matrices.reshape(-1)
    local_phases, _, tile_a, tile_r, pitch = psi_start.shape
    rows = tile_a * tile_r
    cells = rows * pitch
    angle = lax.axis_index("phase").astype(jnp.float32) * (2.0 * math.pi / BLADES)
    me_axial = lax.axis_index("axial")
    lower_side = (me_axial == 0).astype(jnp.float32)
    upper_side = 1.0 - lower_side
    dims = metric.shape[0]
    scalars = jnp.stack(
        [
            upper_side,
            lower_side,
            omega[0],
            jnp.cos(angle),
            jnp.sin(angle),
            upper_side,
            lower_side,
            phase_weight[0],
        ]
    ).astype(jnp.float32)
    weights = jnp.concatenate([scalars, metric.reshape(-1)])
    real_t = jnp.swapaxes(flux_jac[:, 0], 1, 2)
    imag_t = jnp.swapaxes(flux_jac[:, 1], 1, 2)
    gauss = jnp.stack([real_t, imag_t - real_t, real_t + imag_t], axis=1).reshape(-1)
    pad = jnp.zeros((METRIC + 64 - weights.shape[0],), jnp.float32)
    mat_weights = jnp.concatenate([mat, weights, pad, gauss])
    mat = mat_weights
    weights = mat_weights
    partner = pairing[0, 0]
    faces = face_coef.astype(jnp.float32).reshape(6, rows, pitch)
    diag = diag_coef.reshape(rows, pitch)
    pick = partner.astype(jnp.int32).reshape(rows, 1)
    up_r, down_r = neighbours("radial")
    psi = psi_start.reshape(comps, rows, pitch)
    src = source.reshape(comps, rows, pitch)
    axs, q2, q3 = run_edges(mat, weights, psi, faces, tile_r)
    for section in range(ITERS):
        axr = lax.ppermute(axs, "axial", [(0, 1), (1, 0)])
        ralo = lax.ppermute(q2, "radial", up_r)
        rahi = lax.ppermute(q3, "radial", down_r)
        res = run_interior(mat, weights, psi, src, faces, diag, pick, tile_r)
        if section < ITERS - 1:
            psi, axs, q2, q3 = run_fixup(
                mat, weights, psi, res, faces, diag, axr, ralo, rahi, tile_r, True, dims
            )
        else:
            psi, weighted = run_fixup(
                mat, weights, psi, res, faces, diag, axr, ralo, rahi, tile_r, False, dims
            )
    psi_out = psi.reshape(psi_start.shape)
    order = owner_order[0, 0]
    owners = lax.axis_size("phase")
    owned = cells // owners
    dims = weighted.shape[0]
    lanes = LANES
    blocks = cells // lanes
    lane_of = order % lanes
    row_of = order // lanes
    pick_lane = (lane_of[None, :] == jnp.arange(lanes, dtype=order.dtype)[:, None]).astype(jnp.float32)
    by_lane = jnp.einsum(
        "xl,lj->xj",
        weighted.reshape(dims * blocks, lanes),
        pick_lane,
        precision=lax.Precision.HIGHEST,
    ).reshape(dims, blocks, cells)
    pick_row = row_of[None, None, :] == jnp.arange(blocks, dtype=order.dtype)[None, :, None]
    in_order = jnp.sum(jnp.where(pick_row, by_lane, 0.0), axis=1)
    gathered = sum_at_owner_paired(in_order, "phase", 1) if owners % 2 == 0 else sum_at_owner(in_order, "phase", 1)
    mine = lax.dynamic_slice_in_dim(order, lax.axis_index("phase") * owned, owned)
    count_k = mode_shape.shape[0]
    where = jnp.stack([mine % lanes, mine // lanes]).astype(jnp.int32)
    modes = pl.pallas_call(
        functools.partial(modes_kernel, blocks=blocks),
        out_shape=jax.ShapeDtypeStruct((count_k * 3, owned), jnp.float32),
        in_specs=[vmem_spec(), vmem_spec()],
        out_specs=vmem_spec(),
    )(where, mode_shape.reshape(count_k * 3 * blocks, lanes)).reshape(count_k, 3, owned)
    sens = modes[:, 0] * gathered[0] + modes[:, 1] * gathered[1] + modes[:, 2] * gathered[2]
    return (psi_out, sens.reshape(count_k, 1, 1, owned))


def solution(mesh):
    return jax.shard_map(
        body,
        mesh=mesh,
        in_specs=(
            P("phase", None, "axial", "radial", None),
            P("phase", None, "axial", "radial", None),
            P(None, "axial", "radial", None),
            P("axial", "radial", None),
            P(),
            P(),
            P(),
            P(None, None, "axial", "radial", None),
            P("phase"),
            P("axial", "radial", None),
            P("axial", "radial", None),
        ),
        out_specs=(P("phase", None, "axial", "radial", None), P(None, "axial", "radial", "phase")),
        check_vma=False,
    )
```

```python
import functools
import math

import jax
import jax.numpy as jnp
from jax import lax
from jax.experimental import pallas as pl
from jax.experimental.pallas import tpu as pltpu
from jax.sharding import PartitionSpec as P

BLADES = 16
ITERS = 4


RELAX = 0.8
LANES = 128
SMEM = pltpu.MemorySpace.SMEM
METRIC = 8


def split_up(value, dim, count):
    dims = value.shape
    blocks = value.reshape(*dims[:dim], count, dims[dim] // count, *dims[dim + 1 :])
    return jnp.moveaxis(blocks, dim, 0)


def sum_at_owner(value, axis, dim):
    count = lax.axis_size(axis)
    blocks = lax.all_to_all(split_up(value, dim, count), axis, 0, 0, tiled=True)
    return jnp.sum(blocks, axis=0)


def sum_at_owner_paired(value, axis, dim):
    count = lax.axis_size(axis)
    blocks = split_up(value, dim, count)
    core = lax.axis_index(axis) % 2
    even, odd = blocks[0::2], blocks[1::2]
    send = jnp.where(core == 0, odd, even)
    keep = jnp.where(core == 0, even, odd)
    got = lax.ppermute(send, axis, [(p, p ^ 1) for p in range(count)])
    groups = [list(range(parity, count, 2)) for parity in range(2)]
    mixed = lax.all_to_all(keep + got, axis, 0, 0, tiled=True, axis_index_groups=groups)
    return jnp.sum(mixed, axis=0)


def build_matrices(flux_jac):
    real_part = jnp.swapaxes(flux_jac[:, 0], 1, 2)
    imag_part = jnp.swapaxes(flux_jac[:, 1], 1, 2)
    top_rows = jnp.concatenate([real_part, imag_part], axis=2)
    low_rows = jnp.concatenate([-imag_part, real_part], axis=2)
    return jnp.concatenate([top_rows, low_rows], axis=1)


def exact_pick(pick, values):
    first = values.astype(jnp.bfloat16)
    rest = values - first.astype(jnp.float32)
    second = rest.astype(jnp.bfloat16)
    third = (rest - second.astype(jnp.float32)).astype(jnp.bfloat16)
    out = jnp.dot(pick, first, preferred_element_type=jnp.float32)
    out = out + jnp.dot(pick, second, preferred_element_type=jnp.float32)
    return out + jnp.dot(pick, third, preferred_element_type=jnp.float32)


def applied(mat_ref, d, x, comps, load):
    total = mat_ref[(d * comps + x) * comps] * load(0)
    for c in range(1, comps):
        total = total + mat_ref[(d * comps + x) * comps + c] * load(c)
    return total


def write_edges(mat_ref, wt_ref, psi_ref, face_ref, axs_ref, q2_ref, q3_ref, comps, tile_r):
    rows = psi_ref.shape[1]
    layers = rows // tile_r
    top = pl.ds(rows - tile_r, tile_r)
    bottom = pl.ds(0, tile_r)
    r_top = pl.ds(tile_r - 1, layers, stride=tile_r)
    r_bottom = pl.ds(0, layers, stride=tile_r)
    keep_top = wt_ref[6 * comps * comps + 1]
    keep_bottom = wt_ref[6 * comps * comps + 0]
    for x in range(comps):
        up = face_ref[0, top, :] * applied(mat_ref, 0, x, comps, lambda c: psi_ref[c, top, :])
        down = face_ref[1, bottom, :] * applied(mat_ref, 1, x, comps, lambda c: psi_ref[c, bottom, :])
        axs_ref[x] = up * keep_top + down * keep_bottom
        q2_ref[x] = face_ref[2, r_top, :] * applied(mat_ref, 2, x, comps, lambda c: psi_ref[c, r_top, :])
        q3_ref[x] = face_ref[3, r_bottom, :] * applied(mat_ref, 3, x, comps, lambda c: psi_ref[c, r_bottom, :])


def edges_kernel(mat_ref, wt_ref, psi_ref, coef_ref, axs_ref, q2_ref, q3_ref, face_ref, *, tile_r):
    for d in range(face_ref.shape[0]):
        face_ref[d] = coef_ref[d].astype(jnp.float32)
    write_edges(mat_ref, wt_ref, psi_ref, face_ref, axs_ref, q2_ref, q3_ref, psi_ref.shape[0], tile_r)


def gauss_pair(gauss_ref, d, x, half, sum_ref, psi_ref):
    base = (d * 3) * half * half + x * half
    def dot(which, load):
        start = base + which * half * half
        total = gauss_ref[start] * load(0)
        for c in range(1, half):
            total = total + gauss_ref[start + c] * load(c)
        return total
    shared = dot(0, lambda c: sum_ref[c])
    real = shared + dot(1, lambda c: psi_ref[c + half])
    imag = shared - dot(2, lambda c: psi_ref[c])
    return real, imag


def interior_kernel(
    mat_ref, wt_ref, psi_ref, src_ref, face_ref, diag_ref, pick_ref, res_ref, inc_ref, sum_ref, *, tile_r,
):
    comps, rows, lanes = psi_ref.shape
    half = comps // 2
    gauss_ref = mat_ref
    gauss_at = 6 * comps * comps + METRIC + 64
    lane = lax.broadcasted_iota(jnp.int32, (rows, lanes), 1)
    row = lax.broadcasted_iota(jnp.int32, (rows, lanes), 0) % tile_r
    omega = wt_ref[6 * comps * comps + 2]
    cosine = wt_ref[6 * comps * comps + 3]
    sine = wt_ref[6 * comps * comps + 4]
    for c in range(half):
        sum_ref[c] = psi_ref[c] + psi_ref[c + half]
    pack4 = jnp.zeros((rows, lanes), jnp.float32)
    pack5 = jnp.zeros((rows, lanes), jnp.float32)
    edge = jnp.zeros((tile_r, lanes), jnp.float32)
    shifted = gauss_ref.at[pl.ds(gauss_at, 6 * 3 * half * half)]
    for x in range(half):
        pair = [(x, 0), (x + half, 1)]
        q = [[None, None] for _ in range(6)]
        for d in range(6):
            real, imag = gauss_pair(shifted, d, x, half, sum_ref, psi_ref)
            q[d][0] = face_ref[d] * real
            q[d][1] = face_ref[d] * imag
        for comp, k in pair:
            q0, q1, q2, q3, q4, q5 = (q[d][k] for d in range(6))
            lower_a = jnp.concatenate([edge, q0[: rows - tile_r]], axis=0)
            upper_a = jnp.concatenate([q1[tile_r:], edge], axis=0)
            lower_r = jnp.where(row == 0, 0.0, pltpu.roll(q2, 1, 0))
            upper_r = jnp.where(row == tile_r - 1, 0.0, pltpu.roll(q3, rows - 1, 0))
            lower_t = jnp.where(lane == 0, 0.0, pltpu.roll(q4, 1, 1))
            upper_t = jnp.where(lane == lanes - 1, 0.0, pltpu.roll(q5, lanes - 1, 1))
            inc_ref[comp] = lower_a + upper_a + lower_r + upper_r + lower_t + upper_t
            pack4 = pack4 + jnp.where(lane == comp, pltpu.roll(q4, (comp + 1) % lanes, 1), 0.0)
            pack5 = pack5 + jnp.where(lane == comp, pltpu.roll(q5, comp, 1), 0.0) if comp else jnp.where(lane == 0, q5, 0.0)
    pick = (pick_ref[...] == lax.broadcasted_iota(jnp.int32, (rows, rows), 1)).astype(jnp.bfloat16)
    got4 = exact_pick(pick, pack4)
    got5 = exact_pick(pick, pack5)
    up4 = pltpu.roll(got4, lanes - half, 1)
    down4 = pltpu.roll(got4, half, 1)
    up5 = pltpu.roll(got5, lanes - half, 1)
    down5 = pltpu.roll(got5, half, 1)
    real_half = lane < half
    wrap4 = jnp.where(real_half, cosine * got4 - sine * up4, sine * down4 + cosine * got4)
    wrap5 = jnp.where(real_half, cosine * got5 - (-sine) * up5, (-sine) * down5 + cosine * got5)
    diag = diag_ref[...]
    for x in range(comps):
        at_start = pltpu.roll(wrap4, (lanes - x) % lanes, 1)
        at_end = pltpu.roll(wrap5, lanes - 1 - x, 1)
        incoming = inc_ref[x] + jnp.where(lane == 0, at_start, 0.0) + jnp.where(lane == lanes - 1, at_end, 0.0)
        psi = psi_ref[x]
        swapped = psi_ref[x + half] if x < half else -psi_ref[x - half]
        res_ref[x] = src_ref[x] - (diag * psi + omega * swapped) + incoming


def fixup_kernel(
    mat_ref, wt_ref, psi_ref, res_ref, face_ref, diag_ref, axr_ref, ralo_ref, rahi_ref,
    out_ref, axs_ref, *radial_refs, tile_r, edges, dims,
):
    comps, rows, lanes = psi_ref.shape
    layers = rows // tile_r
    row = lax.broadcasted_iota(jnp.int32, (rows, lanes), 0) % tile_r
    from_below = wt_ref[6 * comps * comps + 5]
    from_above = wt_ref[6 * comps * comps + 6]
    middle = jnp.zeros((rows - 2 * tile_r, lanes), jnp.float32)
    diag = diag_ref[...]
    for x in range(comps):
        got = axr_ref[x]
        low_r = ralo_ref[x]
        high_r = rahi_ref[x]
        low_rows = jnp.concatenate(
            [jnp.broadcast_to(low_r[j : j + 1, :], (tile_r, lanes)) for j in range(layers)], axis=0
        )
        high_rows = jnp.concatenate(
            [jnp.broadcast_to(high_r[j : j + 1, :], (tile_r, lanes)) for j in range(layers)], axis=0
        )
        halo = jnp.concatenate([got * from_below, middle, got * from_above], axis=0)
        halo = halo + jnp.where(row == 0, low_rows, 0.0) + jnp.where(row == tile_r - 1, high_rows, 0.0)
        out_ref[x] = psi_ref[x] + RELAX * (res_ref[x] + halo) / diag
    if edges:
        write_edges(mat_ref, wt_ref, out_ref, face_ref, axs_ref, *radial_refs, comps, tile_r)
    else:
        for d in range(dims):
            height = wt_ref[6 * comps * comps + METRIC + d * comps] * out_ref[0]
            for c in range(1, comps):
                height = height + wt_ref[6 * comps * comps + METRIC + d * comps + c] * out_ref[c]
            axs_ref[d] = wt_ref[6 * comps * comps + METRIC - 1] * height


def modes_kernel(where_ref, mode_ref, out_ref, *, blocks):
    owned = where_ref.shape[1]
    lanes = mode_ref.shape[1]
    lane_of = where_ref[0:1, :]
    row_of = where_ref[1:2, :]
    pick = (lax.broadcasted_iota(jnp.int32, (lanes, owned), 0) == lane_of).astype(jnp.bfloat16)
    hit = lax.broadcasted_iota(jnp.int32, (blocks, owned), 0) == row_of
    for g in range(out_ref.shape[0]):
        part = jnp.dot(mode_ref[pl.ds(g * blocks, blocks), :], pick, preferred_element_type=jnp.float32)
        out_ref[pl.ds(g, 1), :] = jnp.sum(jnp.where(hit, part, 0.0), axis=0, keepdims=True)


def vmem_spec():
    return pl.BlockSpec(memory_space=pltpu.MemorySpace.VMEM)


def smem_spec():
    return pl.BlockSpec(memory_space=SMEM)


def edge_shapes(comps, rows, tile_r):
    layers = rows // tile_r
    return (
        jax.ShapeDtypeStruct((comps, tile_r, LANES), jnp.float32),
        jax.ShapeDtypeStruct((comps, layers, LANES), jnp.float32),
        jax.ShapeDtypeStruct((comps, layers, LANES), jnp.float32),
    )


def run_edges(mat, weights, psi, face, tile_r):
    comps, rows, _ = psi.shape
    return pl.pallas_call(
        functools.partial(edges_kernel, tile_r=tile_r),
        out_shape=edge_shapes(comps, rows, tile_r) + (jax.ShapeDtypeStruct(face.shape, jnp.float32),),
        in_specs=[smem_spec(), smem_spec(), vmem_spec(), vmem_spec()],
        out_specs=tuple(vmem_spec() for _ in range(4)),
    )(mat, weights, psi, face)


def run_interior(mat, weights, psi, src, face, diag, pick, tile_r):
    comps, rows, lanes = psi.shape
    return pl.pallas_call(
        functools.partial(interior_kernel, tile_r=tile_r),
        out_shape=jax.ShapeDtypeStruct(psi.shape, jnp.float32),
        in_specs=[smem_spec(), smem_spec()] + [vmem_spec() for _ in range(5)],
        out_specs=vmem_spec(),
        scratch_shapes=[pltpu.VMEM((comps, rows, lanes), jnp.float32), pltpu.VMEM((comps // 2, rows, lanes), jnp.float32)],
    )(mat, weights, psi, src, face, diag, pick)


def run_fixup(mat, weights, psi, res, face, diag, axr, ralo, rahi, tile_r, edges, dims):
    comps, rows, lanes = psi.shape
    tail = edge_shapes(comps, rows, tile_r) if edges else (jax.ShapeDtypeStruct((dims, rows, lanes), jnp.float32),)
    return pl.pallas_call(
        functools.partial(fixup_kernel, tile_r=tile_r, edges=edges, dims=dims),
        out_shape=(jax.ShapeDtypeStruct(psi.shape, jnp.float32),) + tail,
        in_specs=[smem_spec(), smem_spec()] + [vmem_spec() for _ in range(7)],
        out_specs=tuple(vmem_spec() for _ in range(1 + len(tail))),
    )(mat, weights, psi, res, face, diag, axr, ralo, rahi)


def neighbours(axis):
    count = lax.axis_size(axis)
    up = [(i, (i + 1) % count) for i in range(count - 1)]
    return up, [(j, i) for i, j in up]


def body(
    psi_start,
    source,
    face_coef,
    diag_coef,
    flux_jac,
    omega,
    metric,
    mode_shape,
    phase_weight,
    pairing,
    owner_order,
):
    matrices = build_matrices(flux_jac)
    comps = matrices.shape[1]
    mat = matrices.reshape(-1)
    local_phases, _, tile_a, tile_r, pitch = psi_start.shape
    rows = tile_a * tile_r
    cells = rows * pitch
    angle = lax.axis_index("phase").astype(jnp.float32) * (2.0 * math.pi / BLADES)
    me_axial = lax.axis_index("axial")
    lower_side = (me_axial == 0).astype(jnp.float32)
    upper_side = 1.0 - lower_side
    dims = metric.shape[0]
    scalars = jnp.stack(
        [
            upper_side,
            lower_side,
            omega[0],
            jnp.cos(angle),
            jnp.sin(angle),
            upper_side,
            lower_side,
            phase_weight[0],
        ]
    ).astype(jnp.float32)
    weights = jnp.concatenate([scalars, metric.reshape(-1)])
    real_t = jnp.swapaxes(flux_jac[:, 0], 1, 2)
    imag_t = jnp.swapaxes(flux_jac[:, 1], 1, 2)
    gauss = jnp.stack([real_t, imag_t - real_t, real_t + imag_t], axis=1).reshape(-1)
    pad = jnp.zeros((METRIC + 64 - weights.shape[0],), jnp.float32)
    mat_weights = jnp.concatenate([mat, weights, pad, gauss])
    mat = mat_weights
    weights = mat_weights
    partner = pairing[0, 0]
    coefs = face_coef.reshape(face_coef.shape[0], rows, pitch)
    diag = diag_coef.reshape(rows, pitch)
    pick = partner.astype(jnp.int32).reshape(rows, 1)
    up_r, down_r = neighbours("radial")
    psi = psi_start.reshape(comps, rows, pitch)
    src = source.reshape(comps, rows, pitch)
    axs, q2, q3, faces = run_edges(mat, weights, psi, coefs, tile_r)
    for section in range(ITERS):
        axr = lax.ppermute(axs, "axial", [(0, 1), (1, 0)])
        ralo = lax.ppermute(q2, "radial", up_r)
        rahi = lax.ppermute(q3, "radial", down_r)
        res = run_interior(mat, weights, psi, src, faces, diag, pick, tile_r)
        if section < ITERS - 1:
            psi, axs, q2, q3 = run_fixup(
                mat, weights, psi, res, faces, diag, axr, ralo, rahi, tile_r, True, dims
            )
        else:
            psi, weighted = run_fixup(
                mat, weights, psi, res, faces, diag, axr, ralo, rahi, tile_r, False, dims
            )
    psi_out = psi.reshape(psi_start.shape)
    order = owner_order[0, 0]
    owners = lax.axis_size("phase")
    owned = cells // owners
    dims = weighted.shape[0]
    lanes = LANES
    blocks = cells // lanes
    lane_of = order % lanes
    row_of = order // lanes
    pick_lane = (lane_of[None, :] == jnp.arange(lanes, dtype=order.dtype)[:, None]).astype(jnp.float32)
    by_lane = jnp.einsum(
        "xl,lj->xj",
        weighted.reshape(dims * blocks, lanes),
        pick_lane,
        precision=lax.Precision.HIGHEST,
    ).reshape(dims, blocks, cells)
    pick_row = row_of[None, None, :] == jnp.arange(blocks, dtype=order.dtype)[None, :, None]
    in_order = jnp.sum(jnp.where(pick_row, by_lane, 0.0), axis=1)
    gathered = sum_at_owner_paired(in_order, "phase", 1) if owners % 2 == 0 else sum_at_owner(in_order, "phase", 1)
    mine = lax.dynamic_slice_in_dim(order, lax.axis_index("phase") * owned, owned)
    count_k = mode_shape.shape[0]
    where = jnp.stack([mine % lanes, mine // lanes]).astype(jnp.int32)
    modes = pl.pallas_call(
        functools.partial(modes_kernel, blocks=blocks),
        out_shape=jax.ShapeDtypeStruct((count_k * 3, owned), jnp.float32),
        in_specs=[vmem_spec(), vmem_spec()],
        out_specs=vmem_spec(),
    )(where, mode_shape.reshape(count_k * 3 * blocks, lanes)).reshape(count_k, 3, owned)
    sens = modes[:, 0] * gathered[0] + modes[:, 1] * gathered[1] + modes[:, 2] * gathered[2]
    return (psi_out, sens.reshape(count_k, 1, 1, owned))


def solution(mesh):
    return jax.shard_map(
        body,
        mesh=mesh,
        in_specs=(
            P("phase", None, "axial", "radial", None),
            P("phase", None, "axial", "radial", None),
            P(None, "axial", "radial", None),
            P("axial", "radial", None),
            P(),
            P(),
            P(),
            P(None, None, "axial", "radial", None),
            P("phase"),
            P("axial", "radial", None),
            P("axial", "radial", None),
        ),
        out_specs=(P("phase", None, "axial", "radial", None), P(None, "axial", "radial", "phase")),
        check_vma=False,
    )
```

```python
import functools
import math

import jax
import jax.numpy as jnp
from jax import lax
from jax.experimental import pallas as pl
from jax.experimental.pallas import tpu as pltpu
from jax.sharding import PartitionSpec as P

BLADES = 16
ITERS = 4


RELAX = 0.8
LANES = 128
SMEM = pltpu.MemorySpace.SMEM
METRIC = 8


def split_up(value, dim, count):
    dims = value.shape
    blocks = value.reshape(*dims[:dim], count, dims[dim] // count, *dims[dim + 1 :])
    return jnp.moveaxis(blocks, dim, 0)


def sum_at_owner(value, axis, dim):
    count = lax.axis_size(axis)
    blocks = lax.all_to_all(split_up(value, dim, count), axis, 0, 0, tiled=True)
    return jnp.sum(blocks, axis=0)


def sum_at_owner_paired(value, axis, dim):
    count = lax.axis_size(axis)
    blocks = split_up(value, dim, count)
    core = lax.axis_index(axis) % 2
    even, odd = blocks[0::2], blocks[1::2]
    send = jnp.where(core == 0, odd, even)
    keep = jnp.where(core == 0, even, odd)
    got = lax.ppermute(send, axis, [(p, p ^ 1) for p in range(count)])
    groups = [list(range(parity, count, 2)) for parity in range(2)]
    mixed = lax.all_to_all(keep + got, axis, 0, 0, tiled=True, axis_index_groups=groups)
    return jnp.sum(mixed, axis=0)


def build_matrices(flux_jac):
    real_part = jnp.swapaxes(flux_jac[:, 0], 1, 2)
    imag_part = jnp.swapaxes(flux_jac[:, 1], 1, 2)
    top_rows = jnp.concatenate([real_part, imag_part], axis=2)
    low_rows = jnp.concatenate([-imag_part, real_part], axis=2)
    return jnp.concatenate([top_rows, low_rows], axis=1)


def exact_pick(pick_t, values):
    first = values.astype(jnp.bfloat16)
    rest = values - first.astype(jnp.float32)
    second = rest.astype(jnp.bfloat16)
    third = (rest - second.astype(jnp.float32)).astype(jnp.bfloat16)
    dims = (((0,), (0,)), ((), ()))
    out = lax.dot_general(pick_t, first, dims, preferred_element_type=jnp.float32)
    out = out + lax.dot_general(pick_t, second, dims, preferred_element_type=jnp.float32)
    return out + lax.dot_general(pick_t, third, dims, preferred_element_type=jnp.float32)


def applied(mat_ref, d, x, comps, load):
    total = mat_ref[(d * comps + x) * comps] * load(0)
    for c in range(1, comps):
        total = total + mat_ref[(d * comps + x) * comps + c] * load(c)
    return total


def write_edges(mat_ref, wt_ref, psi_ref, face_ref, axs_ref, q2_ref, q3_ref, comps, tile_r):
    rows = psi_ref.shape[1]
    layers = rows // tile_r
    top = pl.ds(rows - tile_r, tile_r)
    bottom = pl.ds(0, tile_r)
    r_top = pl.ds(tile_r - 1, layers, stride=tile_r)
    r_bottom = pl.ds(0, layers, stride=tile_r)
    keep_top = wt_ref[6 * comps * comps + 1]
    keep_bottom = wt_ref[6 * comps * comps + 0]
    for x in range(comps):
        up = face_ref[0, top, :] * applied(mat_ref, 0, x, comps, lambda c: psi_ref[c, top, :])
        down = face_ref[1, bottom, :] * applied(mat_ref, 1, x, comps, lambda c: psi_ref[c, bottom, :])
        axs_ref[x] = up * keep_top + down * keep_bottom
        q2_ref[x] = face_ref[2, r_top, :] * applied(mat_ref, 2, x, comps, lambda c: psi_ref[c, r_top, :])
        q3_ref[x] = face_ref[3, r_bottom, :] * applied(mat_ref, 3, x, comps, lambda c: psi_ref[c, r_bottom, :])


def edges_kernel(mat_ref, wt_ref, psi_ref, coef_ref, axs_ref, q2_ref, q3_ref, face_ref, *, tile_r):
    for d in range(face_ref.shape[0]):
        face_ref[d] = coef_ref[d].astype(jnp.float32)
    write_edges(mat_ref, wt_ref, psi_ref, face_ref, axs_ref, q2_ref, q3_ref, psi_ref.shape[0], tile_r)


def gauss_pair(gauss_ref, d, x, half, sum_ref, psi_ref):
    base = (d * 3) * half * half + x * half
    def dot(which, load):
        start = base + which * half * half
        total = gauss_ref[start] * load(0)
        for c in range(1, half):
            total = total + gauss_ref[start + c] * load(c)
        return total
    shared = dot(0, lambda c: sum_ref[c])
    real = shared + dot(1, lambda c: psi_ref[c + half])
    imag = shared - dot(2, lambda c: psi_ref[c])
    return real, imag


def interior_kernel(
    mat_ref, wt_ref, psi_ref, src_ref, face_ref, diag_ref, pick_ref, res_ref, inc_ref, sum_ref, *, tile_r,
):
    comps, rows, lanes = psi_ref.shape
    half = comps // 2
    gauss_ref = mat_ref
    gauss_at = 6 * comps * comps + METRIC + 64
    lane = lax.broadcasted_iota(jnp.int32, (rows, lanes), 1)
    row = lax.broadcasted_iota(jnp.int32, (rows, lanes), 0) % tile_r
    omega = wt_ref[6 * comps * comps + 2]
    cosine = wt_ref[6 * comps * comps + 3]
    sine = wt_ref[6 * comps * comps + 4]
    for c in range(half):
        sum_ref[c] = psi_ref[c] + psi_ref[c + half]
    pack4 = jnp.zeros((rows, lanes), jnp.float32)
    pack5 = jnp.zeros((rows, lanes), jnp.float32)
    edge = jnp.zeros((tile_r, lanes), jnp.float32)
    shifted = gauss_ref.at[pl.ds(gauss_at, 6 * 3 * half * half)]
    for x in range(half):
        pair = [(x, 0), (x + half, 1)]
        q = [[None, None] for _ in range(6)]
        for d in range(6):
            real, imag = gauss_pair(shifted, d, x, half, sum_ref, psi_ref)
            q[d][0] = face_ref[d] * real
            q[d][1] = face_ref[d] * imag
        for comp, k in pair:
            q0, q1, q2, q3, q4, q5 = (q[d][k] for d in range(6))
            lower_a = jnp.concatenate([edge, q0[: rows - tile_r]], axis=0)
            upper_a = jnp.concatenate([q1[tile_r:], edge], axis=0)
            lower_r = jnp.where(row == 0, 0.0, pltpu.roll(q2, 1, 0))
            upper_r = jnp.where(row == tile_r - 1, 0.0, pltpu.roll(q3, rows - 1, 0))
            lower_t = jnp.where(lane == 0, 0.0, pltpu.roll(q4, 1, 1))
            upper_t = jnp.where(lane == lanes - 1, 0.0, pltpu.roll(q5, lanes - 1, 1))
            inc_ref[comp] = lower_a + upper_a + lower_r + upper_r + lower_t + upper_t
            pack4 = pack4 + jnp.where(lane == comp, pltpu.roll(q4, (comp + 1) % lanes, 1), 0.0)
            pack5 = pack5 + jnp.where(lane == comp, pltpu.roll(q5, comp, 1), 0.0) if comp else jnp.where(lane == 0, q5, 0.0)
    pick = (pick_ref[...] == lax.broadcasted_iota(jnp.int32, (rows, rows), 0)).astype(jnp.bfloat16)
    got4 = exact_pick(pick, pack4)
    got5 = exact_pick(pick, pack5)
    up4 = pltpu.roll(got4, lanes - half, 1)
    down4 = pltpu.roll(got4, half, 1)
    up5 = pltpu.roll(got5, lanes - half, 1)
    down5 = pltpu.roll(got5, half, 1)
    real_half = lane < half
    wrap4 = jnp.where(real_half, cosine * got4 - sine * up4, sine * down4 + cosine * got4)
    wrap5 = jnp.where(real_half, cosine * got5 - (-sine) * up5, (-sine) * down5 + cosine * got5)
    diag = diag_ref[...]
    for x in range(comps):
        at_start = pltpu.roll(wrap4, (lanes - x) % lanes, 1)
        at_end = pltpu.roll(wrap5, lanes - 1 - x, 1)
        incoming = inc_ref[x] + jnp.where(lane == 0, at_start, 0.0) + jnp.where(lane == lanes - 1, at_end, 0.0)
        psi = psi_ref[x]
        swapped = psi_ref[x + half] if x < half else -psi_ref[x - half]
        res_ref[x] = src_ref[x] - (diag * psi + omega * swapped) + incoming


def fixup_kernel(
    mat_ref, wt_ref, psi_ref, res_ref, face_ref, diag_ref, axr_ref, ralo_ref, rahi_ref,
    out_ref, axs_ref, *radial_refs, tile_r, edges, dims,
):
    comps, rows, lanes = psi_ref.shape
    layers = rows // tile_r
    row = lax.broadcasted_iota(jnp.int32, (rows, lanes), 0) % tile_r
    from_below = wt_ref[6 * comps * comps + 5]
    from_above = wt_ref[6 * comps * comps + 6]
    middle = jnp.zeros((rows - 2 * tile_r, lanes), jnp.float32)
    diag = diag_ref[...]
    for x in range(comps):
        got = axr_ref[x]
        low_r = ralo_ref[x]
        high_r = rahi_ref[x]
        low_rows = jnp.concatenate(
            [jnp.broadcast_to(low_r[j : j + 1, :], (tile_r, lanes)) for j in range(layers)], axis=0
        )
        high_rows = jnp.concatenate(
            [jnp.broadcast_to(high_r[j : j + 1, :], (tile_r, lanes)) for j in range(layers)], axis=0
        )
        halo = jnp.concatenate([got * from_below, middle, got * from_above], axis=0)
        halo = halo + jnp.where(row == 0, low_rows, 0.0) + jnp.where(row == tile_r - 1, high_rows, 0.0)
        out_ref[x] = psi_ref[x] + RELAX * (res_ref[x] + halo) / diag
    if edges:
        write_edges(mat_ref, wt_ref, out_ref, face_ref, axs_ref, *radial_refs, comps, tile_r)
    else:
        for d in range(dims):
            height = wt_ref[6 * comps * comps + METRIC + d * comps] * out_ref[0]
            for c in range(1, comps):
                height = height + wt_ref[6 * comps * comps + METRIC + d * comps + c] * out_ref[c]
            axs_ref[d] = wt_ref[6 * comps * comps + METRIC - 1] * height


def modes_kernel(where_ref, mode_ref, out_ref, *, blocks):
    owned = where_ref.shape[1]
    lanes = mode_ref.shape[1]
    lane_of = where_ref[0:1, :]
    row_of = where_ref[1:2, :]
    pick = (lax.broadcasted_iota(jnp.int32, (lanes, owned), 0) == lane_of).astype(jnp.bfloat16)
    hit = lax.broadcasted_iota(jnp.int32, (blocks, owned), 0) == row_of
    for g in range(out_ref.shape[0]):
        part = jnp.dot(mode_ref[pl.ds(g * blocks, blocks), :], pick, preferred_element_type=jnp.float32)
        out_ref[pl.ds(g, 1), :] = jnp.sum(jnp.where(hit, part, 0.0), axis=0, keepdims=True)


def vmem_spec():
    return pl.BlockSpec(memory_space=pltpu.MemorySpace.VMEM)


def smem_spec():
    return pl.BlockSpec(memory_space=SMEM)


def edge_shapes(comps, rows, tile_r):
    layers = rows // tile_r
    return (
        jax.ShapeDtypeStruct((comps, tile_r, LANES), jnp.float32),
        jax.ShapeDtypeStruct((comps, layers, LANES), jnp.float32),
        jax.ShapeDtypeStruct((comps, layers, LANES), jnp.float32),
    )


def run_edges(mat, weights, psi, face, tile_r):
    comps, rows, _ = psi.shape
    return pl.pallas_call(
        functools.partial(edges_kernel, tile_r=tile_r),
        out_shape=edge_shapes(comps, rows, tile_r) + (jax.ShapeDtypeStruct(face.shape, jnp.float32),),
        in_specs=[smem_spec(), smem_spec(), vmem_spec(), vmem_spec()],
        out_specs=tuple(vmem_spec() for _ in range(4)),
    )(mat, weights, psi, face)


def run_interior(mat, weights, psi, src, face, diag, pick, tile_r):
    comps, rows, lanes = psi.shape
    return pl.pallas_call(
        functools.partial(interior_kernel, tile_r=tile_r),
        out_shape=jax.ShapeDtypeStruct(psi.shape, jnp.float32),
        in_specs=[smem_spec(), smem_spec()] + [vmem_spec() for _ in range(5)],
        out_specs=vmem_spec(),
        scratch_shapes=[pltpu.VMEM((comps, rows, lanes), jnp.float32), pltpu.VMEM((comps // 2, rows, lanes), jnp.float32)],
    )(mat, weights, psi, src, face, diag, pick)


def run_fixup(mat, weights, psi, res, face, diag, axr, ralo, rahi, tile_r, edges, dims):
    comps, rows, lanes = psi.shape
    tail = edge_shapes(comps, rows, tile_r) if edges else (jax.ShapeDtypeStruct((dims, rows, lanes), jnp.float32),)
    return pl.pallas_call(
        functools.partial(fixup_kernel, tile_r=tile_r, edges=edges, dims=dims),
        out_shape=(jax.ShapeDtypeStruct(psi.shape, jnp.float32),) + tail,
        in_specs=[smem_spec(), smem_spec()] + [vmem_spec() for _ in range(7)],
        out_specs=tuple(vmem_spec() for _ in range(1 + len(tail))),
    )(mat, weights, psi, res, face, diag, axr, ralo, rahi)


def neighbours(axis):
    count = lax.axis_size(axis)
    up = [(i, (i + 1) % count) for i in range(count - 1)]
    return up, [(j, i) for i, j in up]


def body(
    psi_start,
    source,
    face_coef,
    diag_coef,
    flux_jac,
    omega,
    metric,
    mode_shape,
    phase_weight,
    pairing,
    owner_order,
):
    matrices = build_matrices(flux_jac)
    comps = matrices.shape[1]
    mat = matrices.reshape(-1)
    local_phases, _, tile_a, tile_r, pitch = psi_start.shape
    rows = tile_a * tile_r
    cells = rows * pitch
    angle = lax.axis_index("phase").astype(jnp.float32) * (2.0 * math.pi / BLADES)
    me_axial = lax.axis_index("axial")
    lower_side = (me_axial == 0).astype(jnp.float32)
    upper_side = 1.0 - lower_side
    dims = metric.shape[0]
    scalars = jnp.stack(
        [
            upper_side,
            lower_side,
            omega[0],
            jnp.cos(angle),
            jnp.sin(angle),
            upper_side,
            lower_side,
            phase_weight[0],
        ]
    ).astype(jnp.float32)
    weights = jnp.concatenate([scalars, metric.reshape(-1)])
    real_t = jnp.swapaxes(flux_jac[:, 0], 1, 2)
    imag_t = jnp.swapaxes(flux_jac[:, 1], 1, 2)
    gauss = jnp.stack([real_t, imag_t - real_t, real_t + imag_t], axis=1).reshape(-1)
    pad = jnp.zeros((METRIC + 64 - weights.shape[0],), jnp.float32)
    mat_weights = jnp.concatenate([mat, weights, pad, gauss])
    mat = mat_weights
    weights = mat_weights
    partner = pairing[0, 0]
    coefs = face_coef.reshape(face_coef.shape[0], rows, pitch)
    diag = diag_coef.reshape(rows, pitch)
    pick = partner.astype(jnp.int32).reshape(1, rows)
    up_r, down_r = neighbours("radial")
    psi = psi_start.reshape(comps, rows, pitch)
    src = source.reshape(comps, rows, pitch)
    axs, q2, q3, faces = run_edges(mat, weights, psi, coefs, tile_r)
    for section in range(ITERS):
        axr = lax.ppermute(axs, "axial", [(0, 1), (1, 0)])
        ralo = lax.ppermute(q2, "radial", up_r)
        rahi = lax.ppermute(q3, "radial", down_r)
        res = run_interior(mat, weights, psi, src, faces, diag, pick, tile_r)
        if section < ITERS - 1:
            psi, axs, q2, q3 = run_fixup(
                mat, weights, psi, res, faces, diag, axr, ralo, rahi, tile_r, True, dims
            )
        else:
            psi, weighted = run_fixup(
                mat, weights, psi, res, faces, diag, axr, ralo, rahi, tile_r, False, dims
            )
    psi_out = psi.reshape(psi_start.shape)
    order = owner_order[0, 0]
    owners = lax.axis_size("phase")
    owned = cells // owners
    dims = weighted.shape[0]
    lanes = LANES
    blocks = cells // lanes
    lane_of = order % lanes
    row_of = order // lanes
    pick_lane = (lane_of[None, :] == jnp.arange(lanes, dtype=order.dtype)[:, None]).astype(jnp.float32)
    by_lane = jnp.einsum(
        "xl,lj->xj",
        weighted.reshape(dims * blocks, lanes),
        pick_lane,
        precision=lax.Precision.HIGHEST,
    ).reshape(dims, blocks, cells)
    pick_row = row_of[None, None, :] == jnp.arange(blocks, dtype=order.dtype)[None, :, None]
    in_order = jnp.sum(jnp.where(pick_row, by_lane, 0.0), axis=1)
    gathered = sum_at_owner_paired(in_order, "phase", 1) if owners % 2 == 0 else sum_at_owner(in_order, "phase", 1)
    mine = lax.dynamic_slice_in_dim(order, lax.axis_index("phase") * owned, owned)
    count_k = mode_shape.shape[0]
    where = jnp.stack([mine % lanes, mine // lanes]).astype(jnp.int32)
    modes = pl.pallas_call(
        functools.partial(modes_kernel, blocks=blocks),
        out_shape=jax.ShapeDtypeStruct((count_k * 3, owned), jnp.float32),
        in_specs=[vmem_spec(), vmem_spec()],
        out_specs=vmem_spec(),
    )(where, mode_shape.reshape(count_k * 3 * blocks, lanes)).reshape(count_k, 3, owned)
    sens = modes[:, 0] * gathered[0] + modes[:, 1] * gathered[1] + modes[:, 2] * gathered[2]
    return (psi_out, sens.reshape(count_k, 1, 1, owned))


def solution(mesh):
    return jax.shard_map(
        body,
        mesh=mesh,
        in_specs=(
            P("phase", None, "axial", "radial", None),
            P("phase", None, "axial", "radial", None),
            P(None, "axial", "radial", None),
            P("axial", "radial", None),
            P(),
            P(),
            P(),
            P(None, None, "axial", "radial", None),
            P("phase"),
            P("axial", "radial", None),
            P("axial", "radial", None),
        ),
        out_specs=(P("phase", None, "axial", "radial", None), P(None, "axial", "radial", "phase")),
        check_vma=False,
    )
```

```python
import functools
import math

import jax
import jax.numpy as jnp
from jax import lax
from jax.experimental import pallas as pl
from jax.experimental.pallas import tpu as pltpu
from jax.sharding import PartitionSpec as P

BLADES = 16
ITERS = 4


RELAX = 0.8
LANES = 128
SMEM = pltpu.MemorySpace.SMEM
METRIC = 8


def split_up(value, dim, count):
    dims = value.shape
    blocks = value.reshape(*dims[:dim], count, dims[dim] // count, *dims[dim + 1 :])
    return jnp.moveaxis(blocks, dim, 0)


def sum_at_owner(value, axis, dim):
    count = lax.axis_size(axis)
    blocks = lax.all_to_all(split_up(value, dim, count), axis, 0, 0, tiled=True)
    return jnp.sum(blocks, axis=0)


def sum_at_owner_paired(value, axis, dim):
    count = lax.axis_size(axis)
    blocks = split_up(value, dim, count)
    core = lax.axis_index(axis) % 2
    even, odd = blocks[0::2], blocks[1::2]
    send = jnp.where(core == 0, odd, even)
    keep = jnp.where(core == 0, even, odd)
    got = lax.ppermute(send, axis, [(p, p ^ 1) for p in range(count)])
    groups = [list(range(parity, count, 2)) for parity in range(2)]
    mixed = lax.all_to_all(keep + got, axis, 0, 0, tiled=True, axis_index_groups=groups)
    return jnp.sum(mixed, axis=0)


def build_matrices(flux_jac):
    real_part = jnp.swapaxes(flux_jac[:, 0], 1, 2)
    imag_part = jnp.swapaxes(flux_jac[:, 1], 1, 2)
    top_rows = jnp.concatenate([real_part, imag_part], axis=2)
    low_rows = jnp.concatenate([-imag_part, real_part], axis=2)
    return jnp.concatenate([top_rows, low_rows], axis=1)


def exact_pick(pick_t, values):
    first = values.astype(jnp.bfloat16)
    rest = values - first.astype(jnp.float32)
    second = rest.astype(jnp.bfloat16)
    third = (rest - second.astype(jnp.float32)).astype(jnp.bfloat16)
    dims = (((0,), (0,)), ((), ()))
    out = lax.dot_general(pick_t, first, dims, preferred_element_type=jnp.float32)
    out = out + lax.dot_general(pick_t, second, dims, preferred_element_type=jnp.float32)
    return out + lax.dot_general(pick_t, third, dims, preferred_element_type=jnp.float32)


def applied(mat_ref, d, x, comps, load):
    total = mat_ref[(d * comps + x) * comps] * load(0)
    for c in range(1, comps):
        total = total + mat_ref[(d * comps + x) * comps + c] * load(c)
    return total


def write_edges(mat_ref, wt_ref, psi_ref, face_ref, axs_ref, q2_ref, q3_ref, comps, tile_r):
    rows = psi_ref.shape[1]
    layers = rows // tile_r
    top = pl.ds(rows - tile_r, tile_r)
    bottom = pl.ds(0, tile_r)
    r_top = pl.ds(tile_r - 1, layers, stride=tile_r)
    r_bottom = pl.ds(0, layers, stride=tile_r)
    keep_top = wt_ref[6 * comps * comps + 1]
    keep_bottom = wt_ref[6 * comps * comps + 0]
    for x in range(comps):
        up = face_ref[0, top, :] * applied(mat_ref, 0, x, comps, lambda c: psi_ref[c, top, :])
        down = face_ref[1, bottom, :] * applied(mat_ref, 1, x, comps, lambda c: psi_ref[c, bottom, :])
        axs_ref[x] = up * keep_top + down * keep_bottom
        q2_ref[x] = face_ref[2, r_top, :] * applied(mat_ref, 2, x, comps, lambda c: psi_ref[c, r_top, :])
        q3_ref[x] = face_ref[3, r_bottom, :] * applied(mat_ref, 3, x, comps, lambda c: psi_ref[c, r_bottom, :])


def edges_kernel(mat_ref, wt_ref, psi_ref, coef_ref, axs_ref, q2_ref, q3_ref, face_ref, *, tile_r):
    for d in range(face_ref.shape[0]):
        face_ref[d] = coef_ref[d].astype(jnp.float32)
    write_edges(mat_ref, wt_ref, psi_ref, face_ref, axs_ref, q2_ref, q3_ref, psi_ref.shape[0], tile_r)


def gauss_pair(gauss_ref, d, x, half, sum_ref, psi_ref):
    base = (d * 3) * half * half + x * half
    def dot(which, load):
        start = base + which * half * half
        total = gauss_ref[start] * load(0)
        for c in range(1, half):
            total = total + gauss_ref[start + c] * load(c)
        return total
    shared = dot(0, lambda c: sum_ref[c])
    real = shared + dot(1, lambda c: psi_ref[c + half])
    imag = shared - dot(2, lambda c: psi_ref[c])
    return real, imag


def interior_kernel(
    mat_ref, wt_ref, psi_ref, src_ref, face_ref, diag_ref, pick_ref, res_ref, inc_ref, sum_ref, *, tile_r,
):
    comps, rows, lanes = psi_ref.shape
    half = comps // 2
    gauss_ref = mat_ref
    gauss_at = 6 * comps * comps + METRIC + 64
    lane = lax.broadcasted_iota(jnp.int32, (rows, lanes), 1)
    row = lax.broadcasted_iota(jnp.int32, (rows, lanes), 0) % tile_r
    omega = wt_ref[6 * comps * comps + 2]
    cosine = wt_ref[6 * comps * comps + 3]
    sine = wt_ref[6 * comps * comps + 4]
    for c in range(half):
        sum_ref[c] = psi_ref[c] + psi_ref[c + half]
    pack4 = jnp.zeros((rows, lanes), jnp.float32)
    pack5 = jnp.zeros((rows, lanes), jnp.float32)
    edge = jnp.zeros((tile_r, lanes), jnp.float32)
    shifted = gauss_ref.at[pl.ds(gauss_at, 6 * 3 * half * half)]
    for x in range(half):
        pair = [(x, 0), (x + half, 1)]
        q = [[None, None] for _ in range(6)]
        for d in range(6):
            real, imag = gauss_pair(shifted, d, x, half, sum_ref, psi_ref)
            q[d][0] = face_ref[d] * real
            q[d][1] = face_ref[d] * imag
        for comp, k in pair:
            q0, q1, q2, q3, q4, q5 = (q[d][k] for d in range(6))
            lower_a = jnp.concatenate([edge, q0[: rows - tile_r]], axis=0)
            upper_a = jnp.concatenate([q1[tile_r:], edge], axis=0)
            lower_r = jnp.where(row == 0, 0.0, pltpu.roll(q2, 1, 0))
            upper_r = jnp.where(row == tile_r - 1, 0.0, pltpu.roll(q3, rows - 1, 0))
            lower_t = jnp.where(lane == 0, 0.0, pltpu.roll(q4, 1, 1))
            upper_t = jnp.where(lane == lanes - 1, 0.0, pltpu.roll(q5, lanes - 1, 1))
            inc_ref[comp] = lower_a + upper_a + lower_r + upper_r + lower_t + upper_t
            pack4 = pack4 + jnp.where(lane == comp, pltpu.roll(q4, (comp + 1) % lanes, 1), 0.0)
            pack5 = pack5 + jnp.where(lane == comp, pltpu.roll(q5, comp, 1), 0.0) if comp else jnp.where(lane == 0, q5, 0.0)
    pick = (pick_ref[...] == lax.broadcasted_iota(jnp.int32, (rows, rows), 0)).astype(jnp.bfloat16)
    got4 = exact_pick(pick, pack4)
    got5 = exact_pick(pick, pack5)
    up4 = pltpu.roll(got4, lanes - half, 1)
    down4 = pltpu.roll(got4, half, 1)
    up5 = pltpu.roll(got5, lanes - half, 1)
    down5 = pltpu.roll(got5, half, 1)
    real_half = lane < half
    wrap4 = jnp.where(real_half, cosine * got4 - sine * up4, sine * down4 + cosine * got4)
    wrap5 = jnp.where(real_half, cosine * got5 - (-sine) * up5, (-sine) * down5 + cosine * got5)
    diag = diag_ref[...]
    for x in range(comps):
        at_start = pltpu.roll(wrap4, (lanes - x) % lanes, 1)
        at_end = pltpu.roll(wrap5, lanes - 1 - x, 1)
        incoming = inc_ref[x] + jnp.where(lane == 0, at_start, 0.0) + jnp.where(lane == lanes - 1, at_end, 0.0)
        psi = psi_ref[x]
        swapped = psi_ref[x + half] if x < half else -psi_ref[x - half]
        res_ref[x] = src_ref[x] - (diag * psi + omega * swapped) + incoming


def fixup_kernel(
    mat_ref, wt_ref, metric_ref, psi_ref, res_ref, face_ref, diag_ref, axr_ref, ralo_ref, rahi_ref,
    out_ref, axs_ref, *radial_refs, tile_r, edges, dims,
):
    comps, rows, lanes = psi_ref.shape
    layers = rows // tile_r
    row = lax.broadcasted_iota(jnp.int32, (rows, lanes), 0) % tile_r
    from_below = wt_ref[6 * comps * comps + 5]
    from_above = wt_ref[6 * comps * comps + 6]
    middle = jnp.zeros((rows - 2 * tile_r, lanes), jnp.float32)
    diag = diag_ref[...]
    for x in range(comps):
        got = axr_ref[x]
        low_r = ralo_ref[x]
        high_r = rahi_ref[x]
        low_rows = jnp.concatenate(
            [jnp.broadcast_to(low_r[j : j + 1, :], (tile_r, lanes)) for j in range(layers)], axis=0
        )
        high_rows = jnp.concatenate(
            [jnp.broadcast_to(high_r[j : j + 1, :], (tile_r, lanes)) for j in range(layers)], axis=0
        )
        halo = jnp.concatenate([got * from_below, middle, got * from_above], axis=0)
        halo = halo + jnp.where(row == 0, low_rows, 0.0) + jnp.where(row == tile_r - 1, high_rows, 0.0)
        out_ref[x] = psi_ref[x] + RELAX * (res_ref[x] + halo) / diag
    if edges:
        write_edges(mat_ref, wt_ref, out_ref, face_ref, axs_ref, *radial_refs, comps, tile_r)
    else:
        for d in range(dims):
            height = metric_ref[d * comps] * out_ref[0]
            for c in range(1, comps):
                height = height + metric_ref[d * comps + c] * out_ref[c]
            axs_ref[d] = wt_ref[6 * comps * comps + METRIC - 1] * height


def modes_kernel(where_ref, mode_ref, out_ref, *, blocks):
    owned = where_ref.shape[1]
    lanes = mode_ref.shape[1]
    lane_of = where_ref[0:1, :]
    row_of = where_ref[1:2, :]
    pick = (lax.broadcasted_iota(jnp.int32, (lanes, owned), 0) == lane_of).astype(jnp.bfloat16)
    hit = lax.broadcasted_iota(jnp.int32, (blocks, owned), 0) == row_of
    for g in range(out_ref.shape[0]):
        part = jnp.dot(mode_ref[pl.ds(g * blocks, blocks), :], pick, preferred_element_type=jnp.float32)
        out_ref[pl.ds(g, 1), :] = jnp.sum(jnp.where(hit, part, 0.0), axis=0, keepdims=True)


def vmem_spec():
    return pl.BlockSpec(memory_space=pltpu.MemorySpace.VMEM)


def smem_spec():
    return pl.BlockSpec(memory_space=SMEM)


def edge_shapes(comps, rows, tile_r):
    layers = rows // tile_r
    return (
        jax.ShapeDtypeStruct((comps, tile_r, LANES), jnp.float32),
        jax.ShapeDtypeStruct((comps, layers, LANES), jnp.float32),
        jax.ShapeDtypeStruct((comps, layers, LANES), jnp.float32),
    )


def run_edges(mat, weights, psi, face, tile_r):
    comps, rows, _ = psi.shape
    return pl.pallas_call(
        functools.partial(edges_kernel, tile_r=tile_r),
        out_shape=edge_shapes(comps, rows, tile_r) + (jax.ShapeDtypeStruct(face.shape, jnp.float32),),
        in_specs=[smem_spec(), smem_spec(), vmem_spec(), vmem_spec()],
        out_specs=tuple(vmem_spec() for _ in range(4)),
    )(mat, weights, psi, face)


def run_interior(mat, weights, psi, src, face, diag, pick, tile_r):
    comps, rows, lanes = psi.shape
    return pl.pallas_call(
        functools.partial(interior_kernel, tile_r=tile_r),
        out_shape=jax.ShapeDtypeStruct(psi.shape, jnp.float32),
        in_specs=[smem_spec(), smem_spec()] + [vmem_spec() for _ in range(5)],
        out_specs=vmem_spec(),
        scratch_shapes=[pltpu.VMEM((comps, rows, lanes), jnp.float32), pltpu.VMEM((comps // 2, rows, lanes), jnp.float32)],
    )(mat, weights, psi, src, face, diag, pick)


def run_fixup(mat, weights, metric_flat, psi, res, face, diag, axr, ralo, rahi, tile_r, edges, dims):
    comps, rows, lanes = psi.shape
    tail = edge_shapes(comps, rows, tile_r) if edges else (jax.ShapeDtypeStruct((dims, rows, lanes), jnp.float32),)
    return pl.pallas_call(
        functools.partial(fixup_kernel, tile_r=tile_r, edges=edges, dims=dims),
        out_shape=(jax.ShapeDtypeStruct(psi.shape, jnp.float32),) + tail,
        in_specs=[smem_spec(), smem_spec(), smem_spec()] + [vmem_spec() for _ in range(7)],
        out_specs=tuple(vmem_spec() for _ in range(1 + len(tail))),
    )(mat, weights, metric_flat, psi, res, face, diag, axr, ralo, rahi)


def neighbours(axis):
    count = lax.axis_size(axis)
    up = [(i, (i + 1) % count) for i in range(count - 1)]
    return up, [(j, i) for i, j in up]


def body(
    psi_start,
    source,
    face_coef,
    diag_coef,
    flux_jac,
    omega,
    metric,
    mode_shape,
    phase_weight,
    pairing,
    owner_order,
):
    matrices = build_matrices(flux_jac)
    comps = matrices.shape[1]
    mat = matrices.reshape(-1)
    local_phases, _, tile_a, tile_r, pitch = psi_start.shape
    rows = tile_a * tile_r
    cells = rows * pitch
    angle = lax.axis_index("phase").astype(jnp.float32) * (2.0 * math.pi / BLADES)
    me_axial = lax.axis_index("axial")
    lower_side = (me_axial == 0).astype(jnp.float32)
    upper_side = 1.0 - lower_side
    dims = metric.shape[0]
    scalars = jnp.stack(
        [
            upper_side,
            lower_side,
            omega[0],
            jnp.cos(angle),
            jnp.sin(angle),
            upper_side,
            lower_side,
            phase_weight[0],
        ]
    ).astype(jnp.float32)
    weights = scalars
    metric_flat = metric.reshape(-1)
    real_t = jnp.swapaxes(flux_jac[:, 0], 1, 2)
    imag_t = jnp.swapaxes(flux_jac[:, 1], 1, 2)
    gauss = jnp.stack([real_t, imag_t - real_t, real_t + imag_t], axis=1).reshape(-1)
    pad = jnp.zeros((METRIC + 64 - weights.shape[0],), jnp.float32)
    mat_weights = jnp.concatenate([mat, weights, pad, gauss])
    mat = mat_weights
    weights = mat_weights
    partner = pairing[0, 0]
    coefs = face_coef.reshape(face_coef.shape[0], rows, pitch)
    diag = diag_coef.reshape(rows, pitch)
    pick = partner.astype(jnp.int32).reshape(1, rows)
    up_r, down_r = neighbours("radial")
    psi = psi_start.reshape(comps, rows, pitch)
    src = source.reshape(comps, rows, pitch)
    axs, q2, q3, faces = run_edges(mat, weights, psi, coefs, tile_r)
    for section in range(ITERS):
        axr = lax.ppermute(axs, "axial", [(0, 1), (1, 0)])
        ralo = lax.ppermute(q2, "radial", up_r)
        rahi = lax.ppermute(q3, "radial", down_r)
        res = run_interior(mat, weights, psi, src, faces, diag, pick, tile_r)
        if section < ITERS - 1:
            psi, axs, q2, q3 = run_fixup(
                mat, weights, metric_flat, psi, res, faces, diag, axr, ralo, rahi, tile_r, True, dims
            )
        else:
            psi, weighted = run_fixup(
                mat, weights, metric_flat, psi, res, faces, diag, axr, ralo, rahi, tile_r, False, dims
            )
    psi_out = psi.reshape(psi_start.shape)
    order = owner_order[0, 0]
    owners = lax.axis_size("phase")
    owned = cells // owners
    dims = weighted.shape[0]
    lanes = LANES
    blocks = cells // lanes
    lane_of = order % lanes
    row_of = order // lanes
    pick_lane = (lane_of[None, :] == jnp.arange(lanes, dtype=order.dtype)[:, None]).astype(jnp.float32)
    by_lane = jnp.einsum(
        "xl,lj->xj",
        weighted.reshape(dims * blocks, lanes),
        pick_lane,
        precision=lax.Precision.HIGHEST,
    ).reshape(dims, blocks, cells)
    pick_row = row_of[None, None, :] == jnp.arange(blocks, dtype=order.dtype)[None, :, None]
    in_order = jnp.sum(jnp.where(pick_row, by_lane, 0.0), axis=1)
    gathered = sum_at_owner_paired(in_order, "phase", 1) if owners % 2 == 0 else sum_at_owner(in_order, "phase", 1)
    mine = lax.dynamic_slice_in_dim(order, lax.axis_index("phase") * owned, owned)
    count_k = mode_shape.shape[0]
    where = jnp.stack([mine % lanes, mine // lanes]).astype(jnp.int32)
    modes = pl.pallas_call(
        functools.partial(modes_kernel, blocks=blocks),
        out_shape=jax.ShapeDtypeStruct((count_k * 3, owned), jnp.float32),
        in_specs=[vmem_spec(), vmem_spec()],
        out_specs=vmem_spec(),
    )(where, mode_shape.reshape(count_k * 3 * blocks, lanes)).reshape(count_k, 3, owned)
    sens = modes[:, 0] * gathered[0] + modes[:, 1] * gathered[1] + modes[:, 2] * gathered[2]
    return (psi_out, sens.reshape(count_k, 1, 1, owned))


def solution(mesh):
    return jax.shard_map(
        body,
        mesh=mesh,
        in_specs=(
            P("phase", None, "axial", "radial", None),
            P("phase", None, "axial", "radial", None),
            P(None, "axial", "radial", None),
            P("axial", "radial", None),
            P(),
            P(),
            P(),
            P(None, None, "axial", "radial", None),
            P("phase"),
            P("axial", "radial", None),
            P("axial", "radial", None),
        ),
        out_specs=(P("phase", None, "axial", "radial", None), P(None, "axial", "radial", "phase")),
        check_vma=False,
    )
```

```python
import functools
import math

import jax
import jax.numpy as jnp
from jax import lax
from jax.experimental import pallas as pl
from jax.experimental.pallas import tpu as pltpu
from jax.sharding import PartitionSpec as P

BLADES = 16
ITERS = 4


RELAX = 0.8
LANES = 128
SMEM = pltpu.MemorySpace.SMEM
METRIC = 8


def split_up(value, dim, count):
    dims = value.shape
    blocks = value.reshape(*dims[:dim], count, dims[dim] // count, *dims[dim + 1 :])
    return jnp.moveaxis(blocks, dim, 0)


def sum_at_owner(value, axis, dim):
    count = lax.axis_size(axis)
    blocks = lax.all_to_all(split_up(value, dim, count), axis, 0, 0, tiled=True)
    return jnp.sum(blocks, axis=0)


def sum_at_owner_paired(value, axis, dim):
    count = lax.axis_size(axis)
    blocks = split_up(value, dim, count)
    core = lax.axis_index(axis) % 2
    even, odd = blocks[0::2], blocks[1::2]
    send = jnp.where(core == 0, odd, even)
    keep = jnp.where(core == 0, even, odd)
    got = lax.ppermute(send, axis, [(p, p ^ 1) for p in range(count)])
    groups = [list(range(parity, count, 2)) for parity in range(2)]
    mixed = lax.all_to_all(keep + got, axis, 0, 0, tiled=True, axis_index_groups=groups)
    return jnp.sum(mixed, axis=0)


def build_matrices(flux_jac):
    real_part = jnp.swapaxes(flux_jac[:, 0], 1, 2)
    imag_part = jnp.swapaxes(flux_jac[:, 1], 1, 2)
    top_rows = jnp.concatenate([real_part, imag_part], axis=2)
    low_rows = jnp.concatenate([-imag_part, real_part], axis=2)
    return jnp.concatenate([top_rows, low_rows], axis=1)


def exact_pick(pick_t, values):
    first = values.astype(jnp.bfloat16)
    rest = values - first.astype(jnp.float32)
    second = rest.astype(jnp.bfloat16)
    third = (rest - second.astype(jnp.float32)).astype(jnp.bfloat16)
    dims = (((0,), (0,)), ((), ()))
    out = lax.dot_general(pick_t, first, dims, preferred_element_type=jnp.float32)
    out = out + lax.dot_general(pick_t, second, dims, preferred_element_type=jnp.float32)
    return out + lax.dot_general(pick_t, third, dims, preferred_element_type=jnp.float32)


def applied(mat_ref, d, x, comps, load):
    total = mat_ref[(d * comps + x) * comps] * load(0)
    for c in range(1, comps):
        total = total + mat_ref[(d * comps + x) * comps + c] * load(c)
    return total


def gauss_rows(gauss_ref, d, x, half, sums, reals, imags):
    base = (d * 3) * half * half + x * half
    def dot(which, parts):
        start = base + which * half * half
        total = gauss_ref[start] * parts[0]
        for c in range(1, half):
            total = total + gauss_ref[start + c] * parts[c]
        return total
    shared = dot(0, sums)
    return shared + dot(1, imags), shared - dot(2, reals)


def write_edges(mat_ref, wt_ref, psi_ref, face_ref, axs_ref, q2_ref, q3_ref, comps, tile_r):
    rows = psi_ref.shape[1]
    half = comps // 2
    layers = rows // tile_r
    gauss = mat_ref.at[pl.ds(6 * comps * comps + METRIC + 64, 6 * 3 * half * half)]
    top = pl.ds(rows - tile_r, tile_r)
    bottom = pl.ds(0, tile_r)
    r_top = pl.ds(tile_r - 1, layers, stride=tile_r)
    r_bottom = pl.ds(0, layers, stride=tile_r)
    keep_top = wt_ref[6 * comps * comps + 1]
    keep_bottom = wt_ref[6 * comps * comps + 0]
    outs = {}
    for d, where in ((0, top), (1, bottom), (2, r_top), (3, r_bottom)):
        reals = [psi_ref[c, where, :] for c in range(half)]
        imags = [psi_ref[c + half, where, :] for c in range(half)]
        sums = [reals[c] + imags[c] for c in range(half)]
        face = face_ref[d, where, :]
        for x in range(half):
            real, imag = gauss_rows(gauss, d, x, half, sums, reals, imags)
            outs[d, x] = face * real
            outs[d, x + half] = face * imag
    for x in range(comps):
        axs_ref[x] = outs[0, x] * keep_top + outs[1, x] * keep_bottom
        q2_ref[x] = outs[2, x]
        q3_ref[x] = outs[3, x]


def edges_kernel(mat_ref, wt_ref, psi_ref, coef_ref, axs_ref, q2_ref, q3_ref, face_ref, *, tile_r):
    for d in range(face_ref.shape[0]):
        face_ref[d] = coef_ref[d].astype(jnp.float32)
    write_edges(mat_ref, wt_ref, psi_ref, face_ref, axs_ref, q2_ref, q3_ref, psi_ref.shape[0], tile_r)


def gauss_pair(gauss_ref, d, x, half, sum_ref, psi_ref):
    base = (d * 3) * half * half + x * half
    def dot(which, load):
        start = base + which * half * half
        total = gauss_ref[start] * load(0)
        for c in range(1, half):
            total = total + gauss_ref[start + c] * load(c)
        return total
    shared = dot(0, lambda c: sum_ref[c])
    real = shared + dot(1, lambda c: psi_ref[c + half])
    imag = shared - dot(2, lambda c: psi_ref[c])
    return real, imag


def interior_kernel(
    mat_ref, wt_ref, psi_ref, src_ref, face_ref, diag_ref, pick_ref, res_ref, inc_ref, sum_ref, *, tile_r,
):
    comps, rows, lanes = psi_ref.shape
    half = comps // 2
    gauss_ref = mat_ref
    gauss_at = 6 * comps * comps + METRIC + 64
    lane = lax.broadcasted_iota(jnp.int32, (rows, lanes), 1)
    row = lax.broadcasted_iota(jnp.int32, (rows, lanes), 0) % tile_r
    omega = wt_ref[6 * comps * comps + 2]
    cosine = wt_ref[6 * comps * comps + 3]
    sine = wt_ref[6 * comps * comps + 4]
    for c in range(half):
        sum_ref[c] = psi_ref[c] + psi_ref[c + half]
    pack4 = jnp.zeros((rows, lanes), jnp.float32)
    pack5 = jnp.zeros((rows, lanes), jnp.float32)
    edge = jnp.zeros((tile_r, lanes), jnp.float32)
    shifted = gauss_ref.at[pl.ds(gauss_at, 6 * 3 * half * half)]
    for x in range(half):
        pair = [(x, 0), (x + half, 1)]
        q = [[None, None] for _ in range(6)]
        for d in range(6):
            real, imag = gauss_pair(shifted, d, x, half, sum_ref, psi_ref)
            q[d][0] = face_ref[d] * real
            q[d][1] = face_ref[d] * imag
        for comp, k in pair:
            q0, q1, q2, q3, q4, q5 = (q[d][k] for d in range(6))
            lower_a = jnp.concatenate([edge, q0[: rows - tile_r]], axis=0)
            upper_a = jnp.concatenate([q1[tile_r:], edge], axis=0)
            lower_r = jnp.where(row == 0, 0.0, pltpu.roll(q2, 1, 0))
            upper_r = jnp.where(row == tile_r - 1, 0.0, pltpu.roll(q3, rows - 1, 0))
            lower_t = jnp.where(lane == 0, 0.0, pltpu.roll(q4, 1, 1))
            upper_t = jnp.where(lane == lanes - 1, 0.0, pltpu.roll(q5, lanes - 1, 1))
            inc_ref[comp] = lower_a + upper_a + lower_r + upper_r + lower_t + upper_t
            pack4 = pack4 + jnp.where(lane == comp, pltpu.roll(q4, (comp + 1) % lanes, 1), 0.0)
            pack5 = pack5 + jnp.where(lane == comp, pltpu.roll(q5, comp, 1), 0.0) if comp else jnp.where(lane == 0, q5, 0.0)
    pick = (pick_ref[...] == lax.broadcasted_iota(jnp.int32, (rows, rows), 0)).astype(jnp.bfloat16)
    got4 = exact_pick(pick, pack4)
    got5 = exact_pick(pick, pack5)
    up4 = pltpu.roll(got4, lanes - half, 1)
    down4 = pltpu.roll(got4, half, 1)
    up5 = pltpu.roll(got5, lanes - half, 1)
    down5 = pltpu.roll(got5, half, 1)
    real_half = lane < half
    wrap4 = jnp.where(real_half, cosine * got4 - sine * up4, sine * down4 + cosine * got4)
    wrap5 = jnp.where(real_half, cosine * got5 - (-sine) * up5, (-sine) * down5 + cosine * got5)
    diag = diag_ref[...]
    for x in range(comps):
        at_start = pltpu.roll(wrap4, (lanes - x) % lanes, 1)
        at_end = pltpu.roll(wrap5, lanes - 1 - x, 1)
        incoming = inc_ref[x] + jnp.where(lane == 0, at_start, 0.0) + jnp.where(lane == lanes - 1, at_end, 0.0)
        psi = psi_ref[x]
        swapped = psi_ref[x + half] if x < half else -psi_ref[x - half]
        res_ref[x] = src_ref[x] - (diag * psi + omega * swapped) + incoming


def fixup_kernel(
    mat_ref, wt_ref, psi_ref, res_ref, face_ref, diag_ref, axr_ref, ralo_ref, rahi_ref,
    out_ref, axs_ref, *radial_refs, tile_r, edges, dims,
):
    comps, rows, lanes = psi_ref.shape
    layers = rows // tile_r
    row = lax.broadcasted_iota(jnp.int32, (rows, lanes), 0) % tile_r
    from_below = wt_ref[6 * comps * comps + 5]
    from_above = wt_ref[6 * comps * comps + 6]
    middle = jnp.zeros((rows - 2 * tile_r, lanes), jnp.float32)
    diag = diag_ref[...]
    for x in range(comps):
        got = axr_ref[x]
        low_r = ralo_ref[x]
        high_r = rahi_ref[x]
        low_rows = jnp.concatenate(
            [jnp.broadcast_to(low_r[j : j + 1, :], (tile_r, lanes)) for j in range(layers)], axis=0
        )
        high_rows = jnp.concatenate(
            [jnp.broadcast_to(high_r[j : j + 1, :], (tile_r, lanes)) for j in range(layers)], axis=0
        )
        halo = jnp.concatenate([got * from_below, middle, got * from_above], axis=0)
        halo = halo + jnp.where(row == 0, low_rows, 0.0) + jnp.where(row == tile_r - 1, high_rows, 0.0)
        out_ref[x] = psi_ref[x] + RELAX * (res_ref[x] + halo) / diag
    if edges:
        write_edges(mat_ref, wt_ref, out_ref, face_ref, axs_ref, *radial_refs, comps, tile_r)
    else:
        for d in range(dims):
            height = wt_ref[6 * comps * comps + METRIC + d * comps] * out_ref[0]
            for c in range(1, comps):
                height = height + wt_ref[6 * comps * comps + METRIC + d * comps + c] * out_ref[c]
            axs_ref[d] = wt_ref[6 * comps * comps + METRIC - 1] * height


def modes_kernel(where_ref, mode_ref, out_ref, *, blocks):
    owned = where_ref.shape[1]
    lanes = mode_ref.shape[1]
    lane_of = where_ref[0:1, :]
    row_of = where_ref[1:2, :]
    pick = (lax.broadcasted_iota(jnp.int32, (lanes, owned), 0) == lane_of).astype(jnp.bfloat16)
    hit = lax.broadcasted_iota(jnp.int32, (blocks, owned), 0) == row_of
    for g in range(out_ref.shape[0]):
        part = jnp.dot(mode_ref[pl.ds(g * blocks, blocks), :], pick, preferred_element_type=jnp.float32)
        out_ref[pl.ds(g, 1), :] = jnp.sum(jnp.where(hit, part, 0.0), axis=0, keepdims=True)


def vmem_spec():
    return pl.BlockSpec(memory_space=pltpu.MemorySpace.VMEM)


def smem_spec():
    return pl.BlockSpec(memory_space=SMEM)


def edge_shapes(comps, rows, tile_r):
    layers = rows // tile_r
    return (
        jax.ShapeDtypeStruct((comps, tile_r, LANES), jnp.float32),
        jax.ShapeDtypeStruct((comps, layers, LANES), jnp.float32),
        jax.ShapeDtypeStruct((comps, layers, LANES), jnp.float32),
    )


def run_edges(mat, weights, psi, face, tile_r):
    comps, rows, _ = psi.shape
    return pl.pallas_call(
        functools.partial(edges_kernel, tile_r=tile_r),
        out_shape=edge_shapes(comps, rows, tile_r) + (jax.ShapeDtypeStruct(face.shape, jnp.float32),),
        in_specs=[smem_spec(), smem_spec(), vmem_spec(), vmem_spec()],
        out_specs=tuple(vmem_spec() for _ in range(4)),
    )(mat, weights, psi, face)


def run_interior(mat, weights, psi, src, face, diag, pick, tile_r):
    comps, rows, lanes = psi.shape
    return pl.pallas_call(
        functools.partial(interior_kernel, tile_r=tile_r),
        out_shape=jax.ShapeDtypeStruct(psi.shape, jnp.float32),
        in_specs=[smem_spec(), smem_spec()] + [vmem_spec() for _ in range(5)],
        out_specs=vmem_spec(),
        scratch_shapes=[pltpu.VMEM((comps, rows, lanes), jnp.float32), pltpu.VMEM((comps // 2, rows, lanes), jnp.float32)],
    )(mat, weights, psi, src, face, diag, pick)


def run_fixup(mat, weights, psi, res, face, diag, axr, ralo, rahi, tile_r, edges, dims):
    comps, rows, lanes = psi.shape
    tail = edge_shapes(comps, rows, tile_r) if edges else (jax.ShapeDtypeStruct((dims, rows, lanes), jnp.float32),)
    return pl.pallas_call(
        functools.partial(fixup_kernel, tile_r=tile_r, edges=edges, dims=dims),
        out_shape=(jax.ShapeDtypeStruct(psi.shape, jnp.float32),) + tail,
        in_specs=[smem_spec(), smem_spec()] + [vmem_spec() for _ in range(7)],
        out_specs=tuple(vmem_spec() for _ in range(1 + len(tail))),
    )(mat, weights, psi, res, face, diag, axr, ralo, rahi)


def neighbours(axis):
    count = lax.axis_size(axis)
    up = [(i, (i + 1) % count) for i in range(count - 1)]
    return up, [(j, i) for i, j in up]


def body(
    psi_start,
    source,
    face_coef,
    diag_coef,
    flux_jac,
    omega,
    metric,
    mode_shape,
    phase_weight,
    pairing,
    owner_order,
):
    matrices = build_matrices(flux_jac)
    comps = matrices.shape[1]
    mat = matrices.reshape(-1)
    local_phases, _, tile_a, tile_r, pitch = psi_start.shape
    rows = tile_a * tile_r
    cells = rows * pitch
    angle = lax.axis_index("phase").astype(jnp.float32) * (2.0 * math.pi / BLADES)
    me_axial = lax.axis_index("axial")
    lower_side = (me_axial == 0).astype(jnp.float32)
    upper_side = 1.0 - lower_side
    dims = metric.shape[0]
    scalars = jnp.stack(
        [
            upper_side,
            lower_side,
            omega[0],
            jnp.cos(angle),
            jnp.sin(angle),
            upper_side,
            lower_side,
            phase_weight[0],
        ]
    ).astype(jnp.float32)
    weights = jnp.concatenate([scalars, metric.reshape(-1)])
    real_t = jnp.swapaxes(flux_jac[:, 0], 1, 2)
    imag_t = jnp.swapaxes(flux_jac[:, 1], 1, 2)
    gauss = jnp.stack([real_t, imag_t - real_t, real_t + imag_t], axis=1).reshape(-1)
    pad = jnp.zeros((METRIC + 64 - weights.shape[0],), jnp.float32)
    mat_weights = jnp.concatenate([jnp.zeros_like(mat), weights, pad, gauss])
    mat = mat_weights
    weights = mat_weights
    partner = pairing[0, 0]
    coefs = face_coef.reshape(face_coef.shape[0], rows, pitch)
    diag = diag_coef.reshape(rows, pitch)
    pick = partner.astype(jnp.int32).reshape(1, rows)
    up_r, down_r = neighbours("radial")
    psi = psi_start.reshape(comps, rows, pitch)
    src = source.reshape(comps, rows, pitch)
    axs, q2, q3, faces = run_edges(mat, weights, psi, coefs, tile_r)
    for section in range(ITERS):
        axr = lax.ppermute(axs, "axial", [(0, 1), (1, 0)])
        ralo = lax.ppermute(q2, "radial", up_r)
        rahi = lax.ppermute(q3, "radial", down_r)
        res = run_interior(mat, weights, psi, src, faces, diag, pick, tile_r)
        if section < ITERS - 1:
            psi, axs, q2, q3 = run_fixup(
                mat, weights, psi, res, faces, diag, axr, ralo, rahi, tile_r, True, dims
            )
        else:
            psi, weighted = run_fixup(
                mat, weights, psi, res, faces, diag, axr, ralo, rahi, tile_r, False, dims
            )
    psi_out = psi.reshape(psi_start.shape)
    order = owner_order[0, 0]
    owners = lax.axis_size("phase")
    owned = cells // owners
    dims = weighted.shape[0]
    lanes = LANES
    blocks = cells // lanes
    lane_of = order % lanes
    row_of = order // lanes
    pick_lane = (lane_of[None, :] == jnp.arange(lanes, dtype=order.dtype)[:, None]).astype(jnp.float32)
    by_lane = jnp.einsum(
        "xl,lj->xj",
        weighted.reshape(dims * blocks, lanes),
        pick_lane,
        precision=lax.Precision.HIGHEST,
    ).reshape(dims, blocks, cells)
    pick_row = row_of[None, None, :] == jnp.arange(blocks, dtype=order.dtype)[None, :, None]
    in_order = jnp.sum(jnp.where(pick_row, by_lane, 0.0), axis=1)
    gathered = sum_at_owner_paired(in_order, "phase", 1) if owners % 2 == 0 else sum_at_owner(in_order, "phase", 1)
    mine = lax.dynamic_slice_in_dim(order, lax.axis_index("phase") * owned, owned)
    count_k = mode_shape.shape[0]
    where = jnp.stack([mine % lanes, mine // lanes]).astype(jnp.int32)
    modes = pl.pallas_call(
        functools.partial(modes_kernel, blocks=blocks),
        out_shape=jax.ShapeDtypeStruct((count_k * 3, owned), jnp.float32),
        in_specs=[vmem_spec(), vmem_spec()],
        out_specs=vmem_spec(),
    )(where, mode_shape.reshape(count_k * 3 * blocks, lanes)).reshape(count_k, 3, owned)
    sens = modes[:, 0] * gathered[0] + modes[:, 1] * gathered[1] + modes[:, 2] * gathered[2]
    return (psi_out, sens.reshape(count_k, 1, 1, owned))


def solution(mesh):
    return jax.shard_map(
        body,
        mesh=mesh,
        in_specs=(
            P("phase", None, "axial", "radial", None),
            P("phase", None, "axial", "radial", None),
            P(None, "axial", "radial", None),
            P("axial", "radial", None),
            P(),
            P(),
            P(),
            P(None, None, "axial", "radial", None),
            P("phase"),
            P("axial", "radial", None),
            P("axial", "radial", None),
        ),
        out_specs=(P("phase", None, "axial", "radial", None), P(None, "axial", "radial", "phase")),
        check_vma=False,
    )
```

```python
import functools
import math

import jax
import jax.numpy as jnp
from jax import lax
from jax.experimental import pallas as pl
from jax.experimental.pallas import tpu as pltpu
from jax.sharding import PartitionSpec as P

BLADES = 16
ITERS = 4


RELAX = 0.8
LANES = 128
SMEM = pltpu.MemorySpace.SMEM
METRIC = 8


def split_up(value, dim, count):
    dims = value.shape
    blocks = value.reshape(*dims[:dim], count, dims[dim] // count, *dims[dim + 1 :])
    return jnp.moveaxis(blocks, dim, 0)


def sum_at_owner(value, axis, dim):
    count = lax.axis_size(axis)
    blocks = lax.all_to_all(split_up(value, dim, count), axis, 0, 0, tiled=True)
    return jnp.sum(blocks, axis=0)


def sum_at_owner_paired(value, axis, dim):
    count = lax.axis_size(axis)
    blocks = split_up(value, dim, count)
    core = lax.axis_index(axis) % 2
    even, odd = blocks[0::2], blocks[1::2]
    send = jnp.where(core == 0, odd, even)
    keep = jnp.where(core == 0, even, odd)
    got = lax.ppermute(send, axis, [(p, p ^ 1) for p in range(count)])
    groups = [list(range(parity, count, 2)) for parity in range(2)]
    mixed = lax.all_to_all(keep + got, axis, 0, 0, tiled=True, axis_index_groups=groups)
    return jnp.sum(mixed, axis=0)


def build_matrices(flux_jac):
    real_part = jnp.swapaxes(flux_jac[:, 0], 1, 2)
    imag_part = jnp.swapaxes(flux_jac[:, 1], 1, 2)
    top_rows = jnp.concatenate([real_part, imag_part], axis=2)
    low_rows = jnp.concatenate([-imag_part, real_part], axis=2)
    return jnp.concatenate([top_rows, low_rows], axis=1)


def exact_pick(pick_t, values):
    first = values.astype(jnp.bfloat16)
    rest = values - first.astype(jnp.float32)
    second = rest.astype(jnp.bfloat16)
    third = (rest - second.astype(jnp.float32)).astype(jnp.bfloat16)
    dims = (((0,), (0,)), ((), ()))
    out = lax.dot_general(pick_t, first, dims, preferred_element_type=jnp.float32)
    out = out + lax.dot_general(pick_t, second, dims, preferred_element_type=jnp.float32)
    return out + lax.dot_general(pick_t, third, dims, preferred_element_type=jnp.float32)


def applied(mat_ref, d, x, comps, load):
    total = mat_ref[(d * comps + x) * comps] * load(0)
    for c in range(1, comps):
        total = total + mat_ref[(d * comps + x) * comps + c] * load(c)
    return total


def gauss_rows(gauss_ref, d, x, half, sums, reals, imags):
    base = (d * 3) * half * half + x * half
    def dot(which, parts):
        start = base + which * half * half
        total = gauss_ref[start] * parts[0]
        for c in range(1, half):
            total = total + gauss_ref[start + c] * parts[c]
        return total
    shared = dot(0, sums)
    return shared + dot(1, imags), shared - dot(2, reals)


def write_edges(mat_ref, wt_ref, psi_ref, face_ref, axs_ref, q2_ref, q3_ref, comps, tile_r):
    rows = psi_ref.shape[1]
    half = comps // 2
    layers = rows // tile_r
    gauss = mat_ref.at[pl.ds(6 * comps * comps + METRIC + 64, 6 * 3 * half * half)]
    top = pl.ds(rows - tile_r, tile_r)
    bottom = pl.ds(0, tile_r)
    r_top = pl.ds(tile_r - 1, layers, stride=tile_r)
    r_bottom = pl.ds(0, layers, stride=tile_r)
    keep_top = wt_ref[6 * comps * comps + 1]
    keep_bottom = wt_ref[6 * comps * comps + 0]
    outs = {}
    for d, where in ((0, top), (1, bottom), (2, r_top), (3, r_bottom)):
        reals = [psi_ref[c, where, :] for c in range(half)]
        imags = [psi_ref[c + half, where, :] for c in range(half)]
        sums = [reals[c] + imags[c] for c in range(half)]
        face = face_ref[d, where, :]
        for x in range(half):
            real, imag = gauss_rows(gauss, d, x, half, sums, reals, imags)
            outs[d, x] = face * real
            outs[d, x + half] = face * imag
    for x in range(comps):
        axs_ref[x] = outs[0, x] * keep_top + outs[1, x] * keep_bottom
        q2_ref[x] = outs[2, x]
        q3_ref[x] = outs[3, x]


def edges_kernel(mat_ref, wt_ref, psi_ref, coef_ref, axs_ref, q2_ref, q3_ref, face_ref, *, tile_r):
    for d in range(face_ref.shape[0]):
        face_ref[d] = coef_ref[d].astype(jnp.float32)
    write_edges(mat_ref, wt_ref, psi_ref, face_ref, axs_ref, q2_ref, q3_ref, psi_ref.shape[0], tile_r)


def gauss_pair(gauss_ref, d, x, half, sum_ref, psi_ref):
    base = (d * 3) * half * half + x * half
    def dot(which, load):
        start = base + which * half * half
        total = gauss_ref[start] * load(0)
        for c in range(1, half):
            total = total + gauss_ref[start + c] * load(c)
        return total
    shared = dot(0, lambda c: sum_ref[c])
    real = shared + dot(1, lambda c: psi_ref[c + half])
    imag = shared - dot(2, lambda c: psi_ref[c])
    return real, imag


def interior_kernel(
    mat_ref, wt_ref, psi_ref, src_ref, face_ref, diag_ref, pick_ref, res_ref, inc_ref, sum_ref, *, tile_r,
):
    comps, rows, lanes = psi_ref.shape
    half = comps // 2
    gauss_ref = mat_ref
    gauss_at = 6 * comps * comps + METRIC + 64
    lane = lax.broadcasted_iota(jnp.int32, (rows, lanes), 1)
    row = lax.broadcasted_iota(jnp.int32, (rows, lanes), 0) % tile_r
    omega = wt_ref[6 * comps * comps + 2]
    cosine = wt_ref[6 * comps * comps + 3]
    sine = wt_ref[6 * comps * comps + 4]
    for c in range(half):
        sum_ref[c] = psi_ref[c] + psi_ref[c + half]
    pack4 = jnp.zeros((rows, lanes), jnp.float32)
    pack5 = jnp.zeros((rows, lanes), jnp.float32)
    edge = jnp.zeros((tile_r, lanes), jnp.float32)
    shifted = gauss_ref.at[pl.ds(gauss_at, 6 * 3 * half * half)]
    for x in range(half):
        pair = [(x, 0), (x + half, 1)]
        q = [[None, None] for _ in range(6)]
        for d in range(6):
            real, imag = gauss_pair(shifted, d, x, half, sum_ref, psi_ref)
            q[d][0] = face_ref[d] * real
            q[d][1] = face_ref[d] * imag
        for comp, k in pair:
            q0, q1, q2, q3, q4, q5 = (q[d][k] for d in range(6))
            lower_a = jnp.concatenate([edge, q0[: rows - tile_r]], axis=0)
            upper_a = jnp.concatenate([q1[tile_r:], edge], axis=0)
            lower_r = jnp.where(row == 0, 0.0, pltpu.roll(q2, 1, 0))
            upper_r = jnp.where(row == tile_r - 1, 0.0, pltpu.roll(q3, rows - 1, 0))
            lower_t = jnp.where(lane == 0, 0.0, pltpu.roll(q4, 1, 1))
            upper_t = jnp.where(lane == lanes - 1, 0.0, pltpu.roll(q5, lanes - 1, 1))
            inc_ref[comp] = lower_a + upper_a + lower_r + upper_r + lower_t + upper_t
            pack4 = pack4 + jnp.where(lane == comp, pltpu.roll(q4, (comp + 1) % lanes, 1), 0.0)
            pack5 = pack5 + jnp.where(lane == comp, pltpu.roll(q5, comp, 1), 0.0) if comp else jnp.where(lane == 0, q5, 0.0)
    pick = (pick_ref[...] == lax.broadcasted_iota(jnp.int32, (rows, rows), 0)).astype(jnp.bfloat16)
    got4 = exact_pick(pick, pack4)
    got5 = exact_pick(pick, pack5)
    up4 = pltpu.roll(got4, lanes - half, 1)
    down4 = pltpu.roll(got4, half, 1)
    up5 = pltpu.roll(got5, lanes - half, 1)
    down5 = pltpu.roll(got5, half, 1)
    real_half = lane < half
    wrap4 = jnp.where(real_half, cosine * got4 - sine * up4, sine * down4 + cosine * got4)
    wrap5 = jnp.where(real_half, cosine * got5 - (-sine) * up5, (-sine) * down5 + cosine * got5)
    diag = diag_ref[...]
    for x in range(comps):
        at_start = pltpu.roll(wrap4, (lanes - x) % lanes, 1)
        at_end = pltpu.roll(wrap5, lanes - 1 - x, 1)
        incoming = inc_ref[x] + jnp.where(lane == 0, at_start, 0.0) + jnp.where(lane == lanes - 1, at_end, 0.0)
        psi = psi_ref[x]
        swapped = psi_ref[x + half] if x < half else -psi_ref[x - half]
        res_ref[x] = src_ref[x] - (diag * psi + omega * swapped) + incoming


def fixup_kernel(
    mat_ref, wt_ref, psi_ref, res_ref, face_ref, diag_ref, axr_ref, ralo_ref, rahi_ref,
    out_ref, axs_ref, *radial_refs, tile_r, edges, dims,
):
    comps, rows, lanes = psi_ref.shape
    layers = rows // tile_r
    row = lax.broadcasted_iota(jnp.int32, (rows, lanes), 0) % tile_r
    from_below = wt_ref[6 * comps * comps + 5]
    from_above = wt_ref[6 * comps * comps + 6]
    middle = jnp.zeros((rows - 2 * tile_r, lanes), jnp.float32)
    diag = diag_ref[...]
    for x in range(comps):
        got = axr_ref[x]
        low_r = ralo_ref[x]
        high_r = rahi_ref[x]
        low_rows = jnp.concatenate(
            [jnp.broadcast_to(low_r[j : j + 1, :], (tile_r, lanes)) for j in range(layers)], axis=0
        )
        high_rows = jnp.concatenate(
            [jnp.broadcast_to(high_r[j : j + 1, :], (tile_r, lanes)) for j in range(layers)], axis=0
        )
        halo = jnp.concatenate([got * from_below, middle, got * from_above], axis=0)
        halo = halo + jnp.where(row == 0, low_rows, 0.0) + jnp.where(row == tile_r - 1, high_rows, 0.0)
        out_ref[x] = psi_ref[x] + RELAX * (res_ref[x] + halo) / diag
    if edges:
        write_edges(mat_ref, wt_ref, out_ref, face_ref, axs_ref, *radial_refs, comps, tile_r)
    else:
        for d in range(dims):
            height = wt_ref[6 * comps * comps + METRIC + d * comps] * out_ref[0]
            for c in range(1, comps):
                height = height + wt_ref[6 * comps * comps + METRIC + d * comps + c] * out_ref[c]
            axs_ref[d] = wt_ref[6 * comps * comps + METRIC - 1] * height


def modes_kernel(where_ref, mode_ref, out_ref, *, blocks):
    owned = where_ref.shape[1]
    lanes = mode_ref.shape[1]
    lane_of = where_ref[0:1, :]
    row_of = where_ref[1:2, :]
    pick = (lax.broadcasted_iota(jnp.int32, (lanes, owned), 0) == lane_of).astype(jnp.bfloat16)
    hit = lax.broadcasted_iota(jnp.int32, (blocks, owned), 0) == row_of
    for g in range(out_ref.shape[0]):
        part = jnp.dot(mode_ref[pl.ds(g * blocks, blocks), :], pick, preferred_element_type=jnp.float32)
        out_ref[pl.ds(g, 1), :] = jnp.sum(jnp.where(hit, part, 0.0), axis=0, keepdims=True)


def vmem_spec():
    return pl.BlockSpec(memory_space=pltpu.MemorySpace.VMEM)


def smem_spec():
    return pl.BlockSpec(memory_space=SMEM)


def edge_shapes(comps, rows, tile_r):
    layers = rows // tile_r
    return (
        jax.ShapeDtypeStruct((comps, tile_r, LANES), jnp.float32),
        jax.ShapeDtypeStruct((comps, layers, LANES), jnp.float32),
        jax.ShapeDtypeStruct((comps, layers, LANES), jnp.float32),
    )


def run_edges(mat, weights, psi, face, tile_r):
    comps, rows, _ = psi.shape
    return pl.pallas_call(
        functools.partial(edges_kernel, tile_r=tile_r),
        out_shape=edge_shapes(comps, rows, tile_r) + (jax.ShapeDtypeStruct(face.shape, jnp.float32),),
        in_specs=[smem_spec(), smem_spec(), vmem_spec(), vmem_spec()],
        out_specs=tuple(vmem_spec() for _ in range(4)),
    )(mat, weights, psi, face)


def run_interior(mat, weights, psi, src, face, diag, pick, tile_r):
    comps, rows, lanes = psi.shape
    return pl.pallas_call(
        functools.partial(interior_kernel, tile_r=tile_r),
        out_shape=jax.ShapeDtypeStruct(psi.shape, jnp.float32),
        in_specs=[smem_spec(), smem_spec()] + [vmem_spec() for _ in range(5)],
        out_specs=vmem_spec(),
        scratch_shapes=[pltpu.VMEM((comps, rows, lanes), jnp.float32), pltpu.VMEM((comps // 2, rows, lanes), jnp.float32)],
    )(mat, weights, psi, src, face, diag, pick)


def run_fixup(mat, weights, psi, res, face, diag, axr, ralo, rahi, tile_r, edges, dims):
    comps, rows, lanes = psi.shape
    tail = edge_shapes(comps, rows, tile_r) if edges else (jax.ShapeDtypeStruct((dims, rows, lanes), jnp.float32),)
    return pl.pallas_call(
        functools.partial(fixup_kernel, tile_r=tile_r, edges=edges, dims=dims),
        out_shape=(jax.ShapeDtypeStruct(psi.shape, jnp.float32),) + tail,
        in_specs=[smem_spec(), smem_spec()] + [vmem_spec() for _ in range(7)],
        out_specs=tuple(vmem_spec() for _ in range(1 + len(tail))),
    )(mat, weights, psi, res, face, diag, axr, ralo, rahi)


def neighbours(axis):
    count = lax.axis_size(axis)
    up = [(i, (i + 1) % count) for i in range(count - 1)]
    return up, [(j, i) for i, j in up]


def body(
    psi_start,
    source,
    face_coef,
    diag_coef,
    flux_jac,
    omega,
    metric,
    mode_shape,
    phase_weight,
    pairing,
    owner_order,
):
    matrices = build_matrices(flux_jac)
    comps = matrices.shape[1]
    mat = matrices.reshape(-1)
    local_phases, _, tile_a, tile_r, pitch = psi_start.shape
    rows = tile_a * tile_r
    cells = rows * pitch
    angle = lax.axis_index("phase").astype(jnp.float32) * (2.0 * math.pi / BLADES)
    me_axial = lax.axis_index("axial")
    lower_side = (me_axial == 0).astype(jnp.float32)
    upper_side = 1.0 - lower_side
    dims = metric.shape[0]
    scalars = jnp.stack(
        [
            upper_side,
            lower_side,
            omega[0],
            jnp.cos(angle),
            jnp.sin(angle),
            upper_side,
            lower_side,
            phase_weight[0],
        ]
    ).astype(jnp.float32)
    weights = jnp.concatenate([scalars, metric.reshape(-1)])
    real_t = jnp.swapaxes(flux_jac[:, 0], 1, 2)
    imag_t = jnp.swapaxes(flux_jac[:, 1], 1, 2)
    gauss = jnp.stack([real_t, imag_t - real_t, real_t + imag_t], axis=1).reshape(-1)
    pad = jnp.zeros((METRIC + 64 - weights.shape[0],), jnp.float32)
    mat_weights = jnp.concatenate([jnp.zeros_like(mat), weights, pad, gauss])
    mat = mat_weights
    weights = mat_weights
    partner = pairing[0, 0]
    coefs = face_coef.reshape(face_coef.shape[0], rows, pitch)
    diag = diag_coef.reshape(rows, pitch)
    pick = partner.astype(jnp.int32).reshape(1, rows)
    up_r, down_r = neighbours("radial")
    psi = psi_start.reshape(comps, rows, pitch)
    src = source.reshape(comps, rows, pitch)
    axs, q2, q3, faces = run_edges(mat, weights, psi, coefs, tile_r)
    for section in range(ITERS):
        axr = lax.ppermute(axs, "axial", [(0, 1), (1, 0)])
        ralo = lax.ppermute(q2, "radial", up_r)
        rahi = lax.ppermute(q3, "radial", down_r)
        res = run_interior(mat, weights, psi, src, faces, diag, pick, tile_r)
        if section < ITERS - 1:
            psi, axs, q2, q3 = run_fixup(
                mat, weights, psi, res, faces, diag, axr, ralo, rahi, tile_r, True, dims
            )
        else:
            psi, weighted = run_fixup(
                mat, weights, psi, res, faces, diag, axr, ralo, rahi, tile_r, False, dims
            )
    psi_out = psi.reshape(psi_start.shape)
    order = owner_order[0, 0]
    owners = lax.axis_size("phase")
    owned = cells // owners
    dims = weighted.shape[0]
    lanes = LANES
    blocks = cells // lanes
    lane_of = order % lanes
    row_of = order // lanes
    pick_lane = (lane_of[None, :] == jnp.arange(lanes, dtype=order.dtype)[:, None]).astype(jnp.bfloat16)
    flat_w = weighted.reshape(dims * blocks, lanes)
    first = lax.reduce_precision(flat_w, exponent_bits=8, mantissa_bits=7)
    rest = flat_w - first
    second = lax.reduce_precision(rest, exponent_bits=8, mantissa_bits=7)
    parts = jnp.concatenate([first, second, rest - second]).astype(jnp.bfloat16)
    by_lane = jnp.einsum(
        "xl,lj->xj", parts, pick_lane, preferred_element_type=jnp.float32
    ).reshape(3, dims, blocks, cells)
    by_lane = by_lane[0] + by_lane[1] + by_lane[2]
    pick_row = row_of[None, None, :] == jnp.arange(blocks, dtype=order.dtype)[None, :, None]
    in_order = jnp.sum(jnp.where(pick_row, by_lane, 0.0), axis=1)
    gathered = sum_at_owner_paired(in_order, "phase", 1) if owners % 2 == 0 else sum_at_owner(in_order, "phase", 1)
    mine = lax.dynamic_slice_in_dim(order, lax.axis_index("phase") * owned, owned)
    count_k = mode_shape.shape[0]
    where = jnp.stack([mine % lanes, mine // lanes]).astype(jnp.int32)
    modes = pl.pallas_call(
        functools.partial(modes_kernel, blocks=blocks),
        out_shape=jax.ShapeDtypeStruct((count_k * 3, owned), jnp.float32),
        in_specs=[vmem_spec(), vmem_spec()],
        out_specs=vmem_spec(),
    )(where, mode_shape.reshape(count_k * 3 * blocks, lanes)).reshape(count_k, 3, owned)
    sens = modes[:, 0] * gathered[0] + modes[:, 1] * gathered[1] + modes[:, 2] * gathered[2]
    return (psi_out, sens.reshape(count_k, 1, 1, owned))


def solution(mesh):
    return jax.shard_map(
        body,
        mesh=mesh,
        in_specs=(
            P("phase", None, "axial", "radial", None),
            P("phase", None, "axial", "radial", None),
            P(None, "axial", "radial", None),
            P("axial", "radial", None),
            P(),
            P(),
            P(),
            P(None, None, "axial", "radial", None),
            P("phase"),
            P("axial", "radial", None),
            P("axial", "radial", None),
        ),
        out_specs=(P("phase", None, "axial", "radial", None), P(None, "axial", "radial", "phase")),
        check_vma=False,
    )
```
